32 devices in a mesh: dp: 8 (over y, x, core), fsdp: 4 (over z).
Axes of the slice: x: 2, y: 2, z: 4, core: 2. Of those that a mesh axis runs over, the one named last changes fastest.
Arguments:
- tokens: bfloat16 [64, 256, 768], P(('dp', 'fsdp')), may hold values from -6 to 6
- band_waves: int32 [64, 13], P(('dp', 'fsdp')), may hold values from 0 to 128, as said below
- visible_slot: int32 [64, 256], P(('dp', 'fsdp')), may hold values from 0 to 1023, as said below
- wave_table: bfloat16 [128, 768], P(('dp', 'fsdp')), may hold values from -1.75 to 1.75
- norm1_gain: bfloat16 [768], P(('dp', 'fsdp')), may hold values from 0.5 to 1.5
- norm1_bias: bfloat16 [768], P(('dp', 'fsdp')), may hold values from -1.75 to 1.75
- qkv_weight: bfloat16 [768, 2304], P(('dp', 'fsdp')), may hold values from -0.3125 to 0.3125
- out_weight: bfloat16 [768, 768], P(('dp', 'fsdp')), may hold values from -0.875 to 0.875
- norm2_gain: bfloat16 [768], P(('dp', 'fsdp')), may hold values from 0.5 to 1.5
- norm2_bias: bfloat16 [768], P(('dp', 'fsdp')), may hold values from -1.75 to 1.75
- mlp_in: bfloat16 [768, 3072], P(('dp', 'fsdp')), may hold values from -0.21875 to 0.21875
- mlp_in_bias: bfloat16 [3072], P(('dp', 'fsdp')), may hold values from -3 to 3
- mlp_out: bfloat16 [3072, 768], P(('dp', 'fsdp')), may hold values from -0.15625 to 0.15625
- mlp_out_bias: bfloat16 [768], P(('dp', 'fsdp')), may hold values from -1.75 to 1.75
- dec_weight: bfloat16 [768, 512], P(('dp', 'fsdp')), may hold values from -0.21875 to 0.21875
- dec_bias: bfloat16 [512], P(('dp', 'fsdp')), may hold values from -1.75 to 1.75
- mask_token: bfloat16 [512], P(('dp', 'fsdp')), may hold values from -6 to 6
- cot_decoded: bfloat16 [64, 1024, 512], P(None, ('dp', 'fsdp')), may hold values from -6 to 6
Outputs:
- decoded: bfloat16 [64, 1024, 512], P(None, ('dp', 'fsdp'))
- grad_tokens: float32 [64, 256, 768], P(('dp', 'fsdp'))
- grad_wave_table: float32 [128, 768], P(('dp', 'fsdp'))
- grad_norm1_gain: float32 [768], P(('dp', 'fsdp'))
- grad_norm1_bias: float32 [768], P(('dp', 'fsdp'))
- grad_qkv_weight: float32 [768, 2304], P(('dp', 'fsdp'))
- grad_out_weight: float32 [768, 768], P(('dp', 'fsdp'))
- grad_norm2_gain: float32 [768], P(('dp', 'fsdp'))
- grad_norm2_bias: float32 [768], P(('dp', 'fsdp'))
- grad_mlp_in: float32 [768, 3072], P(('dp', 'fsdp'))
- grad_mlp_in_bias: float32 [3072], P(('dp', 'fsdp'))
- grad_mlp_out: float32 [3072, 768], P(('dp', 'fsdp'))
- grad_mlp_out_bias: float32 [768], P(('dp', 'fsdp'))
- grad_dec_weight: float32 [768, 512], P(('dp', 'fsdp'))
- grad_dec_bias: float32 [512], P(('dp', 'fsdp'))
- grad_mask_token: float32 [512], P(('dp', 'fsdp'))
The draws below stay inside these ranges and needn't reach their ends.
Inputs may be any that keep to these rules, and one draw needn't show every extreme that they name: `band_waves`: the first 4 entries of a row are ids below 128; an entry equal to 128 marks an unused band slot, so a chip has 4 to 13 bands; ids may repeat. `visible_slot`: the 256 entries of a row are distinct; the other slots of that chip hold the mask token.
All inputs are finite; a program needn't handle non-finite values.
Results may differ from the reference program's by a relative error of at most 0.012.
The reference program's roundings to bfloat16 on the way count: a program that leaves them out, or rounds other values in their place, can miss the bound.
Values may be sent and summed in bfloat16 or wider, within the bound.
No kernel may reach another device: no remote copies, remote signals or barrier semaphores. Data moves between devices by JAX's collectives and lax.ppermute only.
A program may use at most 128 MiB of HBM per device.

```python
import math
from functools import partial
import jax
import jax.numpy as jnp
from jax import lax

D = 768
H = 12
HD = 64
FF = 3072
DEC = 512
VIS = 256
WAVES = 128
BANDS = 13
L = 1024
CHIPS = 64


def draw_band_waves(key, part):
    first_key, second_key = jax.random.split(jax.random.fold_in(key, 11))
    wave_ids = jax.random.randint(first_key, (CHIPS, BANDS), 0, WAVES, dtype=jnp.int32)
    keep_flags = jax.random.randint(second_key, (CHIPS, BANDS), 0, 2, dtype=jnp.int32)
    slot_index = jnp.arange(BANDS, dtype=jnp.int32)[None, :]
    chip_index = jnp.arange(CHIPS, dtype=jnp.int32)[:, None]
    keep_flags = jnp.where(slot_index < 4, 1, keep_flags)
    keep_flags = jnp.where((slot_index == BANDS - 1) & (chip_index == 0), 0, keep_flags)
    return jnp.where(keep_flags == 1, wave_ids, WAVES).astype(jnp.int32)


def draw_visible_slot(key, part):
    chip_keys = jax.random.split(jax.random.fold_in(key, 23), CHIPS)
    orders = jax.vmap(lambda one_key: jax.random.permutation(one_key, L))(chip_keys)
    return orders[:, :VIS].astype(jnp.int32)


def block_scale(own_key, shape, cuts, smallest, high):
    def one(dim, shards_of):
        steps = jax.random.uniform(jax.random.fold_in(jax.random.fold_in(own_key, 6), dim), (shards_of,), jnp.float32, smallest / len(cuts), high / len(cuts))
        return jnp.repeat(jnp.exp(steps), shape[dim] // shards_of).reshape((-1,) + (1,) * (len(shape) - dim - 1))

    level = one(*cuts[0])
    for cut in cuts[1:]:
        level = level * one(*cut)
    return level


def centred(stream_key, shape, width, bound, cuts=(), held_as=jnp.bfloat16):
    array = jax.random.normal(stream_key, shape, jnp.float32) * width
    if len(cuts) > 0:
        array = block_scale(stream_key, shape, cuts, -0.22, 0.18) * array
    return jnp.clip(array, min=-bound, max=bound).astype(held_as)


def setup_inputs(seed: int = 0) -> dict:
    key_list = jax.random.split(jax.random.key(seed), 19)
    tokens = centred(key_list[0], (CHIPS, VIS, D), 1.0, 6.0, ((0, 32),))
    band_waves = draw_band_waves(jax.random.fold_in(key_list[18], 71), 0)
    visible_slot = draw_visible_slot(jax.random.fold_in(key_list[18], 71), 0)
    wave_table = centred(key_list[3], (WAVES, D), 0.3, 1.75, ((0, 32),))
    norm1_gain = jnp.clip(1.0 + 0.1 * jax.random.normal(key_list[4], (D,), jnp.float32), 0.5, 1.5).astype(jnp.bfloat16)
    norm1_bias = centred(key_list[5], (D,), 0.3, 1.75, ((0, 32),))
    qkv_weight = centred(key_list[6], (D, 3 * D), (D // 2) ** -0.5, 0.3125, ((0, 32),))
    out_weight = centred(key_list[7], (D, D), (D // 16) ** -0.5, 0.875, ((0, 32),))
    norm2_gain = jnp.clip(1.0 + 0.1 * jax.random.normal(key_list[8], (D,), jnp.float32), 0.5, 1.5).astype(jnp.bfloat16)
    norm2_bias = centred(key_list[9], (D,), 0.3, 1.75, ((0, 32),))
    mlp_in = centred(key_list[10], (D, FF), D ** -0.5, 0.21875, ((0, 32),))
    mlp_in_bias = centred(key_list[11], (FF,), 0.5, 3.0, ((0, 32),))
    mlp_out = centred(key_list[12], (FF, D), (FF // 2) ** -0.5, 0.15625, ((0, 32),))
    mlp_out_bias = centred(key_list[13], (D,), 0.3, 1.75, ((0, 32),))
    dec_weight = centred(key_list[14], (D, DEC), D ** -0.5, 0.21875, ((0, 32),))
    dec_bias = centred(key_list[15], (DEC,), 0.3, 1.75, ((0, 32),))
    mask_token = centred(key_list[16], (DEC,), 1.0, 6.0, ((0, 32),))
    cot_decoded = centred(key_list[17], (CHIPS, L, DEC), 1.0, 6.0, ((1, 32),))
    return dict(tokens=tokens, band_waves=band_waves, visible_slot=visible_slot, wave_table=wave_table, norm1_gain=norm1_gain, norm1_bias=norm1_bias, qkv_weight=qkv_weight, out_weight=out_weight, norm2_gain=norm2_gain, norm2_bias=norm2_bias, mlp_in=mlp_in, mlp_in_bias=mlp_in_bias, mlp_out=mlp_out, mlp_out_bias=mlp_out_bias, dec_weight=dec_weight, dec_bias=dec_bias, mask_token=mask_token, cot_decoded=cot_decoded)


@jax.custom_vjp
def low(v):
    return lax.optimization_barrier(v.astype(jnp.bfloat16)).astype(jnp.float32)

@jax.custom_vjp
def low_back(v):
    return v

def low_keep(v):
    return (low(v), None)

def low_pass(kept, grad):
    return (grad,)

def back_keep(v):
    return (v, None)

def back_low(kept, grad):
    return (low(grad),)
low.defvjp(low_keep, low_pass)
low_back.defvjp(back_keep, back_low)
NORM_EPSILON = 1e-05
ROOT_HALF = 0.7071067811865476
HIGH_PRECISION = lax.Precision.HIGHEST

def layer_norm(residual, gain, shift):
    mean_val = lax.optimization_barrier(jnp.mean(residual, axis=-1, keepdims=True))
    centered = residual - mean_val
    variance = lax.optimization_barrier(jnp.mean(centered * centered, axis=-1, keepdims=True))
    return centered * lax.rsqrt(variance + NORM_EPSILON) * gain + shift

def gelu_exact(hidden):
    return 0.5 * hidden * (1.0 + lax.erf(hidden * ROOT_HALF))

def product(left_op, right_op):
    return jnp.dot(left_op, right_op, precision=HIGH_PRECISION)

def one_chip(params, chip_tokens, chip_counts, chip_slots):
    wave_rows, gain_one, shift_one, qkv_mat, out_mat, gain_two, shift_two, inner_mat, inner_bias, outer_mat, outer_bias, dec_mat, dec_shift, mask_row = params
    spectral = jnp.dot(chip_counts, wave_rows, precision=HIGH_PRECISION)
    residual = chip_tokens + spectral
    act_one = low(layer_norm(residual, gain_one, shift_one))
    qkv_vals = low(low_back(product(act_one, qkv_mat)))
    queries = qkv_vals[:, :D].reshape(VIS, H, HD)
    key_rows = qkv_vals[:, D:2 * D].reshape(VIS, H, HD)
    value_rows = qkv_vals[:, 2 * D:].reshape(VIS, H, HD)
    scores = low_back(jnp.einsum('qhd,khd->hqk', queries, key_rows, precision=HIGH_PRECISION) * HD ** (-0.5))
    row_peak = lax.optimization_barrier(jnp.max(scores, axis=-1, keepdims=True))
    exponents = jnp.exp(scores - row_peak)
    soft_weights = low(exponents / lax.optimization_barrier(jnp.sum(exponents, axis=-1, keepdims=True)))
    mixture = jnp.einsum('hqk,khd->qhd', soft_weights, value_rows, precision=HIGH_PRECISION).reshape(VIS, D)
    mixture = low(low_back(mixture))
    residual = residual + low_back(product(mixture, out_mat))
    act_two = low(layer_norm(residual, gain_two, shift_two))
    hidden = low_back(product(act_two, inner_mat) + inner_bias)
    active = low(gelu_exact(hidden))
    residual = residual + low_back(product(active, outer_mat) + outer_bias)
    projected = low(product(low(residual), dec_mat) + dec_shift)
    filled = jnp.broadcast_to(mask_row, (L, DEC)).at[chip_slots].set(projected)
    return filled

def reference(tokens, band_waves, visible_slot, wave_table, norm1_gain, norm1_bias, qkv_weight, out_weight, norm2_gain, norm2_bias, mlp_in, mlp_in_bias, mlp_out, mlp_out_bias, dec_weight, dec_bias, mask_token, cot_decoded):
    counts = lax.optimization_barrier(jnp.sum((band_waves[:, :, None] == jnp.arange(WAVES, dtype=jnp.int32)[None, None, :]).astype(jnp.float32), axis=1))
    group_size = math.gcd(CHIPS, max(1, 4096 // VIS))
    batches = CHIPS // group_size

    def forward(chip_tokens, *params):

        def one_group(pieces):
            group_tokens, group_counts, group_slots = pieces
            return jax.vmap(partial(one_chip, params))(group_tokens, group_counts, group_slots)
        pieces = (chip_tokens.reshape(batches, group_size, VIS, D), counts.reshape(batches, group_size, WAVES), visible_slot.reshape(batches, group_size, VIS))
        filled = lax.map(jax.checkpoint(one_group), pieces)
        return filled.reshape(CHIPS, L, DEC)
    weights = (wave_table, norm1_gain, norm1_bias, qkv_weight, out_weight, norm2_gain, norm2_bias, mlp_in, mlp_in_bias, mlp_out, mlp_out_bias, dec_weight, dec_bias, mask_token)
    floats = [tokens.astype(jnp.float32)] + [weight_arr.astype(jnp.float32) for weight_arr in weights]
    decoded, pullback = jax.vjp(forward, *floats)
    gradients = pullback(cot_decoded.astype(jnp.float32))
    return (decoded.astype(jnp.bfloat16), gradients[0], gradients[1], gradients[2], gradients[3], gradients[4], gradients[5], gradients[6], gradients[7], gradients[8], gradients[9], gradients[10], gradients[11], gradients[12], gradients[13], gradients[14])
```

```python
import numpy as np
import jax
import jax.numpy as jnp
from jax import lax
from jax.sharding import PartitionSpec as P

D = 768
HD = 64
DEC = 512
WAVES = 128
L = 1024

NORM_EPSILON = 1e-05
ROOT_HALF = 0.7071067811865476
INVERSE_ROOT_TAU = 0.3989422804014327
HIGH_PRECISION = lax.Precision.HIGHEST
AX = ("dp", "fsdp")


def product(left_op, right_op):
    return jnp.dot(left_op, right_op, preferred_element_type=jnp.float32)


def inner_rows(left_op, right_op):
    return lax.dot_general(
        left_op, right_op, (((0,), (0,)), ((), ())), preferred_element_type=jnp.float32
    )


def outer_cols(left_op, right_op):
    return lax.dot_general(
        left_op, right_op, (((1,), (1,)), ((), ())), preferred_element_type=jnp.float32
    )


def norm_forward(residual, gain, shift):
    mean_val = jnp.mean(residual, axis=-1, keepdims=True)
    centered = residual - mean_val
    variance = jnp.mean(centered * centered, axis=-1, keepdims=True)
    inverse = lax.rsqrt(variance + NORM_EPSILON)
    normed = centered * inverse
    return (normed * gain + shift, normed, inverse)


def norm_backward(incoming, normed, inverse, gain):
    scaled = incoming * gain
    first_mean = jnp.mean(scaled, axis=-1, keepdims=True)
    second_mean = jnp.mean(scaled * normed, axis=-1, keepdims=True)
    grad_input = inverse * (scaled - first_mean - normed * second_mean)
    return (grad_input, jnp.sum(incoming * normed, axis=0), jnp.sum(incoming, axis=0))


def gelu_value(hidden):
    return 0.5 * hidden * (1.0 + lax.erf(hidden * ROOT_HALF))


def gelu_slope(hidden):
    return (
        0.5 * (1.0 + lax.erf(hidden * ROOT_HALF))
        + hidden * jnp.exp(-0.5 * hidden * hidden) * INVERSE_ROOT_TAU
    )


def core_bit_of(mesh):
    flat = list(mesh.devices.reshape(-1))
    cores = [d.core_on_chip for d in flat]
    stride = 1
    while stride < len(flat) and cores[stride] == cores[0]:
        stride *= 2
    return stride.bit_length() - 1


def halving_order(n_bits, core_bit):
    rest = [b for b in reversed(range(n_bits)) if b != core_bit]
    return [core_bit] + rest


def to_order(block_rows, n_bits, order):
    k = block_rows.shape[1]
    split = block_rows.reshape([2] * n_bits + [k])
    axes = [n_bits - 1 - b for b in order] + [n_bits]
    return split.transpose(axes).reshape(2 ** n_bits, k)


def reduce_scatter_rows(packed, n_bits, order):
    me = lax.axis_index(AX)
    n_dev = 2 ** n_bits
    current = packed
    for bit in order:
        rows, width = current.shape
        halves = current.reshape(2, rows // 2, width)
        mine = (me >> bit) & 1
        keep = lax.dynamic_index_in_dim(halves, mine, 0, keepdims=False)
        send = lax.dynamic_index_in_dim(halves, 1 - mine, 0, keepdims=False)
        moved = lax.ppermute(
            send.astype(jnp.bfloat16), AX, [(i, i ^ (1 << bit)) for i in range(n_dev)]
        )
        current = keep + moved.astype(jnp.float32)
    return current.reshape(-1)


def attend(queries, key_rows, value_rows):
    score_scale = HD ** (-0.5)
    scores = (
        jnp.einsum("cqhd,ckhd->chqk", queries, key_rows, preferred_element_type=jnp.float32)
        * score_scale
    )
    row_peak = jnp.max(scores, axis=-1, keepdims=True)
    exponents = jnp.exp(scores - row_peak)
    row_total = jnp.sum(exponents, axis=-1, keepdims=True)
    soft_full = exponents / row_total
    soft_low = soft_full.astype(jnp.bfloat16)
    mixture = jnp.einsum(
        "chqk,ckhd->cqhd", soft_low, value_rows, preferred_element_type=jnp.float32
    )
    return mixture.astype(jnp.bfloat16), soft_full, soft_low


def attend_back(queries, key_rows, value_rows, soft_full, soft_low, grad_mixture):
    score_scale = HD ** (-0.5)
    grad_values = jnp.einsum(
        "chqk,cqhd->ckhd", soft_low, grad_mixture, preferred_element_type=jnp.float32
    )
    grad_soft = jnp.einsum(
        "cqhd,ckhd->chqk", grad_mixture, value_rows, preferred_element_type=jnp.float32
    )
    row_delta = jnp.sum(grad_soft * soft_full, axis=-1, keepdims=True)
    grad_scores = (soft_full * (grad_soft - row_delta)).astype(jnp.bfloat16)
    grad_queries = (
        jnp.einsum("chqk,ckhd->cqhd", grad_scores, key_rows, preferred_element_type=jnp.float32)
        * score_scale
    )
    grad_keys = (
        jnp.einsum("chqk,cqhd->ckhd", grad_scores, queries, preferred_element_type=jnp.float32)
        * score_scale
    )
    return grad_queries, grad_keys, grad_values


def make_local(n_bits, order):
    n_dev = 2 ** n_bits

    def local(
        tokens,
        band_waves,
        visible_slot,
        wave_table,
        norm1_gain,
        norm1_bias,
        qkv_weight,
        out_weight,
        norm2_gain,
        norm2_bias,
        mlp_in,
        mlp_in_bias,
        mlp_out,
        mlp_out_bias,
        dec_weight,
        dec_bias,
        mask_token,
        cot_decoded,
    ):
        shards = (
            wave_table,
            norm1_gain,
            norm1_bias,
            qkv_weight,
            out_weight,
            norm2_gain,
            norm2_bias,
            mlp_in,
            mlp_in_bias,
            mlp_out,
            mlp_out_bias,
            dec_weight,
            dec_bias,
            mask_token,
        )
        sizes = [int(np.prod(s.shape)) for s in shards]
        padded = -sum(sizes) % 1024
        packed_w = jnp.concatenate(
            [s.reshape(-1) for s in shards] + [jnp.zeros((padded,), jnp.bfloat16)]
        )
        gathered_w = lax.all_gather(packed_w, AX, axis=0, tiled=True).reshape(n_dev, -1)
        full = []
        offset = 0
        for s, size in zip(shards, sizes):
            piece = gathered_w[:, offset : offset + size]
            full.append(piece.reshape((n_dev * s.shape[0],) + s.shape[1:]))
            offset += size
        (
            wave_full,
            gain_one,
            shift_one,
            qkv_full,
            out_full,
            gain_two,
            shift_two,
            inner_full,
            inner_bias,
            outer_full,
            outer_bias,
            dec_full,
            dec_shift,
            mask_full,
        ) = full

        chip_count, vis_len, feature_width = tokens.shape
        row_count = chip_count * vis_len
        heads = feature_width // HD
        counts = jnp.sum(
            (band_waves[:, :, None] == jnp.arange(WAVES, dtype=jnp.int32)[None, None, :]).astype(
                jnp.float32
            ),
            axis=1,
        )
        spectral = jnp.dot(
            counts.astype(jnp.bfloat16), wave_full, preferred_element_type=jnp.float32
        )
        residual = (tokens.astype(jnp.float32) + spectral[:, None, :]).reshape(row_count, D)
        norm_out_one, normed_one, inverse_one = norm_forward(
            residual, gain_one.astype(jnp.float32), shift_one.astype(jnp.float32)
        )
        act_one = norm_out_one.astype(jnp.bfloat16)
        qkv_vals = product(act_one, qkv_full).astype(jnp.bfloat16)
        head_shape = (chip_count, vis_len, heads, HD)
        queries = qkv_vals[:, :D].reshape(head_shape)
        key_rows = qkv_vals[:, D : 2 * D].reshape(head_shape)
        value_rows = qkv_vals[:, 2 * D :].reshape(head_shape)
        mixture4, soft_full, soft_low = attend(queries, key_rows, value_rows)
        mixture = mixture4.reshape(row_count, D)
        res_one = residual + product(mixture, out_full)
        norm_out_two, normed_two, inverse_two = norm_forward(
            res_one, gain_two.astype(jnp.float32), shift_two.astype(jnp.float32)
        )
        act_two = norm_out_two.astype(jnp.bfloat16)
        hidden = product(act_two, inner_full) + inner_bias.astype(jnp.float32)
        active = gelu_value(hidden).astype(jnp.bfloat16)
        res_two = res_one + (product(active, outer_full) + outer_bias.astype(jnp.float32))
        enc_low = res_two.astype(jnp.bfloat16)
        projected = (product(enc_low, dec_full) + dec_shift.astype(jnp.float32)).astype(
            jnp.bfloat16
        )
        slot_ids = jnp.arange(L, dtype=jnp.int32)
        one_hot = (visible_slot[:, None, :] == slot_ids[None, :, None]).astype(jnp.bfloat16)
        filled_vis = jnp.einsum(
            "csi,cie->cse",
            one_hot,
            projected.reshape(chip_count, vis_len, DEC),
            preferred_element_type=jnp.float32,
        )
        has_row = jnp.sum(one_hot.astype(jnp.float32), axis=2, keepdims=True) > 0.5
        filled = jnp.where(has_row, filled_vis, mask_full.astype(jnp.float32)[None, None, :])
        filled = filled.astype(jnp.bfloat16)
        decoded = lax.all_to_all(filled, AX, split_axis=1, concat_axis=0, tiled=True)
        grad_full = lax.all_to_all(cot_decoded, AX, split_axis=0, concat_axis=1, tiled=True)

        grad_vis_low = (
            jnp.einsum("csi,cse->cie", one_hot, grad_full, preferred_element_type=jnp.float32)
            .astype(jnp.bfloat16)
            .reshape(row_count, DEC)
        )
        grad_vis = grad_vis_low.astype(jnp.float32)
        grad_mask_token = jnp.sum(
            jnp.where(has_row, 0.0, grad_full.astype(jnp.float32)), axis=(0, 1)
        )
        grad_dec_bias = jnp.sum(grad_vis, axis=0)
        grad_dec_weight = inner_rows(enc_low, grad_vis_low)
        grad_res_two = outer_cols(grad_vis_low, dec_full)
        grad_ffo = grad_res_two.astype(jnp.bfloat16)
        grad_mlp_out_bias = jnp.sum(grad_ffo.astype(jnp.float32), axis=0)
        grad_mlp_out = inner_rows(active, grad_ffo)
        grad_hidden = (outer_cols(grad_ffo, outer_full) * gelu_slope(hidden)).astype(jnp.bfloat16)
        grad_mlp_in_bias = jnp.sum(grad_hidden.astype(jnp.float32), axis=0)
        grad_mlp_in = inner_rows(act_two, grad_hidden)
        grad_act_two = outer_cols(grad_hidden, inner_full)
        grad_norm_two, grad_norm2_gain, grad_norm2_bias = norm_backward(
            grad_act_two, normed_two, inverse_two, gain_two.astype(jnp.float32)
        )
        grad_res_one = grad_res_two + grad_norm_two
        grad_att = grad_res_one.astype(jnp.bfloat16)
        grad_out_weight = inner_rows(mixture, grad_att)
        grad_mixed = outer_cols(grad_att, out_full).astype(jnp.bfloat16).reshape(head_shape)
        grad_queries, grad_keys, grad_values = attend_back(
            queries, key_rows, value_rows, soft_full, soft_low, grad_mixed
        )
        grad_qkv = jnp.concatenate(
            [
                grad_queries.reshape(row_count, D),
                grad_keys.reshape(row_count, D),
                grad_values.reshape(row_count, D),
            ],
            axis=1,
        ).astype(jnp.bfloat16)
        grad_qkv_weight = inner_rows(act_one, grad_qkv)
        grad_act_one = outer_cols(grad_qkv, qkv_full)
        grad_norm_one, grad_norm1_gain, grad_norm1_bias = norm_backward(
            grad_act_one, normed_one, inverse_one, gain_one.astype(jnp.float32)
        )
        grad_tokens = (grad_res_one + grad_norm_one).reshape(chip_count, vis_len, D)
        chip_sums = jnp.sum(grad_tokens, axis=1)
        grad_wave_table = lax.dot_general(
            counts, chip_sums, (((0,), (0,)), ((), ())), precision=HIGH_PRECISION
        )
        local_grads = (
            grad_wave_table,
            grad_norm1_gain,
            grad_norm1_bias,
            grad_qkv_weight,
            grad_out_weight,
            grad_norm2_gain,
            grad_norm2_bias,
            grad_mlp_in,
            grad_mlp_in_bias,
            grad_mlp_out,
            grad_mlp_out_bias,
            grad_dec_weight,
            grad_dec_bias,
            grad_mask_token,
        )
        widths = [int(np.prod(g.shape)) // n_dev for g in local_grads]
        packed_g = jnp.concatenate(
            [to_order(g.reshape(n_dev, -1), n_bits, order) for g in local_grads], axis=1
        )
        reduced = reduce_scatter_rows(packed_g, n_bits, order)
        summed = []
        offset = 0
        for g, width in zip(local_grads, widths):
            piece = reduced[offset : offset + width]
            summed.append(piece.reshape((g.shape[0] // n_dev,) + g.shape[1:]))
            offset += width
        return (decoded, grad_tokens, *summed)

    return local


def solution(mesh):
    n_dev = mesh.devices.size
    n_bits = n_dev.bit_length() - 1
    order = halving_order(n_bits, core_bit_of(mesh))
    placed = (
        P(AX, None, None),
        P(AX, None),
        P(AX, None),
        P(AX, None),
        P(AX),
        P(AX),
        P(AX, None),
        P(AX, None),
        P(AX),
        P(AX),
        P(AX, None),
        P(AX),
        P(AX, None),
        P(AX),
        P(AX, None),
        P(AX),
        P(AX),
        P(None, AX, None),
    )
    return jax.shard_map(
        make_local(n_bits, order),
        mesh=mesh,
        in_specs=placed,
        out_specs=(
            P(None, AX, None),
            P(AX, None, None),
            P(AX, None),
            P(AX),
            P(AX),
            P(AX, None),
            P(AX, None),
            P(AX),
            P(AX),
            P(AX, None),
            P(AX),
            P(AX, None),
            P(AX),
            P(AX, None),
            P(AX),
            P(AX),
        ),
        check_vma=False,
    )
```

```python
import numpy as np
import jax
import jax.numpy as jnp
from jax import lax
from jax.sharding import PartitionSpec as P

D = 768
HD = 64
DEC = 512
WAVES = 128
L = 1024

NORM_EPSILON = 1e-05
ROOT_HALF = 0.7071067811865476
INVERSE_ROOT_TAU = 0.3989422804014327
HIGH_PRECISION = lax.Precision.HIGHEST
AX = ("dp", "fsdp")


def product(left_op, right_op):
    return jnp.dot(left_op, right_op, preferred_element_type=jnp.float32)


def inner_rows(left_op, right_op):
    return lax.dot_general(
        left_op, right_op, (((0,), (0,)), ((), ())), preferred_element_type=jnp.float32
    )


def outer_cols(left_op, right_op):
    return lax.dot_general(
        left_op, right_op, (((1,), (1,)), ((), ())), preferred_element_type=jnp.float32
    )


def norm_forward(residual, gain, shift):
    mean_val = jnp.mean(residual, axis=-1, keepdims=True)
    centered = residual - mean_val
    variance = jnp.mean(centered * centered, axis=-1, keepdims=True)
    inverse = lax.rsqrt(variance + NORM_EPSILON)
    normed = centered * inverse
    return (normed * gain + shift, normed, inverse)


def norm_backward(incoming, normed, inverse, gain):
    scaled = incoming * gain
    first_mean = jnp.mean(scaled, axis=-1, keepdims=True)
    second_mean = jnp.mean(scaled * normed, axis=-1, keepdims=True)
    grad_input = inverse * (scaled - first_mean - normed * second_mean)
    return (grad_input, jnp.sum(incoming * normed, axis=0), jnp.sum(incoming, axis=0))


def gelu_value(hidden):
    return 0.5 * hidden * (1.0 + lax.erf(hidden * ROOT_HALF))


def gelu_slope(hidden):
    return (
        0.5 * (1.0 + lax.erf(hidden * ROOT_HALF))
        + hidden * jnp.exp(-0.5 * hidden * hidden) * INVERSE_ROOT_TAU
    )


def core_bit_of(mesh):
    flat = list(mesh.devices.reshape(-1))
    cores = [d.core_on_chip for d in flat]
    stride = 1
    while stride < len(flat) and cores[stride] == cores[0]:
        stride *= 2
    return stride.bit_length() - 1


def halving_order(n_bits, core_bit):
    rest = [b for b in reversed(range(n_bits)) if b != core_bit]
    if len(rest) >= 2:
        rest[-2:] = rest[-2:][::-1]
    return [core_bit] + rest


def rs_chain(grad, n_bits, order):
    n_dev = 2 ** n_bits
    me = lax.axis_index(AX)
    rows = grad.shape[0] // n_dev
    current = grad.reshape((2,) * n_bits + (rows,) + grad.shape[1:])
    for bit in order:
        axis = n_bits - 1 - bit
        mine = (me >> bit) & 1
        keep = lax.dynamic_slice_in_dim(current, mine, 1, axis=axis)
        send = lax.dynamic_slice_in_dim(current, 1 - mine, 1, axis=axis)
        moved = lax.ppermute(
            send.astype(jnp.bfloat16), AX, [(i, i ^ (1 << bit)) for i in range(n_dev)]
        )
        current = keep + moved.astype(jnp.float32)
    return current.reshape((rows,) + grad.shape[1:])


def pack_rows(arrays, n_dev, dtype):
    flat = [a.reshape(n_dev, -1).astype(dtype) for a in arrays]
    widths = [f.shape[1] for f in flat]
    padded = -sum(widths) % 1024
    flat.append(jnp.zeros((n_dev, padded), dtype))
    packed = jnp.concatenate(flat, axis=1)
    return packed.reshape(n_dev, 8, -1), widths


def unpack_rows(packed, arrays, widths, n_dev, leading):
    flat = packed.reshape(packed.shape[0], -1)
    out = []
    offset = 0
    for a, width in zip(arrays, widths):
        piece = flat[:, offset : offset + width]
        out.append(piece.reshape((leading * a.shape[0] // n_dev,) + a.shape[1:]))
        offset += width
    return out


def attend(queries, key_rows, value_rows):
    score_scale = HD ** (-0.5)
    scores = (
        jnp.einsum("cqhd,ckhd->chqk", queries, key_rows, preferred_element_type=jnp.float32)
        * score_scale
    )
    row_peak = jnp.max(scores, axis=-1, keepdims=True)
    exponents = jnp.exp(scores - row_peak)
    row_total = jnp.sum(exponents, axis=-1, keepdims=True)
    soft_full = exponents / row_total
    soft_low = soft_full.astype(jnp.bfloat16)
    mixture = jnp.einsum(
        "chqk,ckhd->cqhd", soft_low, value_rows, preferred_element_type=jnp.float32
    )
    return mixture.astype(jnp.bfloat16), soft_full, soft_low


def attend_back(queries, key_rows, value_rows, soft_full, soft_low, grad_mixture):
    score_scale = HD ** (-0.5)
    grad_values = jnp.einsum(
        "chqk,cqhd->ckhd", soft_low, grad_mixture, preferred_element_type=jnp.float32
    )
    grad_soft = jnp.einsum(
        "cqhd,ckhd->chqk", grad_mixture, value_rows, preferred_element_type=jnp.float32
    )
    row_delta = jnp.sum(grad_soft * soft_full, axis=-1, keepdims=True)
    grad_scores = (soft_full * (grad_soft - row_delta)).astype(jnp.bfloat16)
    grad_queries = (
        jnp.einsum("chqk,ckhd->cqhd", grad_scores, key_rows, preferred_element_type=jnp.float32)
        * score_scale
    )
    grad_keys = (
        jnp.einsum("chqk,cqhd->ckhd", grad_scores, queries, preferred_element_type=jnp.float32)
        * score_scale
    )
    return grad_queries, grad_keys, grad_values


def make_local(n_bits, order):
    n_dev = 2 ** n_bits

    def local(
        tokens,
        band_waves,
        visible_slot,
        wave_table,
        norm1_gain,
        norm1_bias,
        qkv_weight,
        out_weight,
        norm2_gain,
        norm2_bias,
        mlp_in,
        mlp_in_bias,
        mlp_out,
        mlp_out_bias,
        dec_weight,
        dec_bias,
        mask_token,
        cot_decoded,
    ):
        shards = (
            wave_table,
            norm1_gain,
            norm1_bias,
            qkv_weight,
            out_weight,
            norm2_gain,
            norm2_bias,
            mlp_in,
            mlp_in_bias,
            mlp_out,
            mlp_out_bias,
            dec_weight,
            dec_bias,
            mask_token,
        )
        small = (wave_table, norm1_gain, norm1_bias, norm2_gain, norm2_bias, mlp_in_bias,
                 mlp_out_bias, dec_bias, mask_token)
        packed_small, small_widths = pack_rows(
            [a.reshape(1, -1) for a in small], 1, jnp.bfloat16
        )
        gathered_small = lax.all_gather(packed_small, AX, axis=0, tiled=True)
        (wave_full, gain_one, shift_one, gain_two, shift_two, inner_bias, outer_bias,
         dec_shift, mask_full) = unpack_rows(gathered_small, small, small_widths, 1, n_dev)
        wide = (qkv_weight, out_weight, mlp_in, dec_weight)
        wide_cols = [a.shape[1] for a in wide]
        gathered_wide = lax.all_gather(jnp.concatenate(wide, axis=1), AX, axis=0, tiled=True)
        wide_full = []
        offset = 0
        for cols in wide_cols:
            wide_full.append(gathered_wide[:, offset : offset + cols])
            offset += cols
        qkv_full, out_full, inner_full, dec_full = wide_full
        outer_full = lax.all_gather(mlp_out, AX, axis=0, tiled=True)

        chip_count, vis_len, feature_width = tokens.shape
        row_count = chip_count * vis_len
        heads = feature_width // HD
        counts = jnp.sum(
            (band_waves[:, :, None] == jnp.arange(WAVES, dtype=jnp.int32)[None, None, :]).astype(
                jnp.float32
            ),
            axis=1,
        )
        spectral = jnp.dot(
            counts.astype(jnp.bfloat16), wave_full, preferred_element_type=jnp.float32
        )
        residual = (tokens.astype(jnp.float32) + spectral[:, None, :]).reshape(row_count, D)
        norm_out_one, normed_one, inverse_one = norm_forward(
            residual, gain_one.astype(jnp.float32), shift_one.astype(jnp.float32)
        )
        act_one = norm_out_one.astype(jnp.bfloat16)
        qkv_vals = product(act_one, qkv_full).astype(jnp.bfloat16)
        head_shape = (chip_count, vis_len, heads, HD)
        queries = qkv_vals[:, :D].reshape(head_shape)
        key_rows = qkv_vals[:, D : 2 * D].reshape(head_shape)
        value_rows = qkv_vals[:, 2 * D :].reshape(head_shape)
        mixture4, soft_full, soft_low = attend(queries, key_rows, value_rows)
        mixture = mixture4.reshape(row_count, D)
        res_one = residual + product(mixture, out_full)
        norm_out_two, normed_two, inverse_two = norm_forward(
            res_one, gain_two.astype(jnp.float32), shift_two.astype(jnp.float32)
        )
        act_two = norm_out_two.astype(jnp.bfloat16)
        hidden = product(act_two, inner_full) + inner_bias.astype(jnp.float32)
        active = gelu_value(hidden).astype(jnp.bfloat16)
        res_two = res_one + (product(active, outer_full) + outer_bias.astype(jnp.float32))
        enc_low = res_two.astype(jnp.bfloat16)
        projected = (product(enc_low, dec_full) + dec_shift.astype(jnp.float32)).astype(
            jnp.bfloat16
        )
        slot_ids = jnp.arange(L, dtype=jnp.int32)
        one_hot = (visible_slot[:, None, :] == slot_ids[None, :, None]).astype(jnp.bfloat16)
        filled_vis = jnp.einsum(
            "csi,cie->cse",
            one_hot,
            projected.reshape(chip_count, vis_len, DEC),
            preferred_element_type=jnp.float32,
        )
        has_row = jnp.sum(one_hot.astype(jnp.float32), axis=2, keepdims=True) > 0.5
        filled = jnp.where(has_row, filled_vis, mask_full.astype(jnp.float32)[None, None, :])
        filled = filled.astype(jnp.bfloat16)
        decoded = lax.all_to_all(filled, AX, split_axis=1, concat_axis=0, tiled=True)
        grad_full = lax.all_to_all(cot_decoded, AX, split_axis=0, concat_axis=1, tiled=True)

        grad_vis_low = (
            jnp.einsum("csi,cse->cie", one_hot, grad_full, preferred_element_type=jnp.float32)
            .astype(jnp.bfloat16)
            .reshape(row_count, DEC)
        )
        grad_vis = grad_vis_low.astype(jnp.float32)
        grad_mask_token = jnp.sum(
            jnp.where(has_row, 0.0, grad_full.astype(jnp.float32)), axis=(0, 1)
        )
        grad_dec_bias = jnp.sum(grad_vis, axis=0)
        grad_dec_weight = inner_rows(enc_low, grad_vis_low)
        grad_res_two = outer_cols(grad_vis_low, dec_full)
        grad_ffo = grad_res_two.astype(jnp.bfloat16)
        grad_mlp_out_bias = jnp.sum(grad_ffo.astype(jnp.float32), axis=0)
        grad_mlp_out = inner_rows(active, grad_ffo)
        grad_hidden = (outer_cols(grad_ffo, outer_full) * gelu_slope(hidden)).astype(jnp.bfloat16)
        grad_mlp_in_bias = jnp.sum(grad_hidden.astype(jnp.float32), axis=0)
        grad_mlp_in = inner_rows(act_two, grad_hidden)
        grad_act_two = outer_cols(grad_hidden, inner_full)
        grad_norm_two, grad_norm2_gain, grad_norm2_bias = norm_backward(
            grad_act_two, normed_two, inverse_two, gain_two.astype(jnp.float32)
        )
        grad_res_one = grad_res_two + grad_norm_two
        grad_att = grad_res_one.astype(jnp.bfloat16)
        grad_out_weight = inner_rows(mixture, grad_att)
        grad_mixed = outer_cols(grad_att, out_full).astype(jnp.bfloat16).reshape(head_shape)
        grad_queries, grad_keys, grad_values = attend_back(
            queries, key_rows, value_rows, soft_full, soft_low, grad_mixed
        )
        grad_qkv = jnp.concatenate(
            [
                grad_queries.reshape(row_count, D),
                grad_keys.reshape(row_count, D),
                grad_values.reshape(row_count, D),
            ],
            axis=1,
        ).astype(jnp.bfloat16)
        grad_qkv_weight = inner_rows(act_one, grad_qkv)
        grad_act_one = outer_cols(grad_qkv, qkv_full)
        grad_norm_one, grad_norm1_gain, grad_norm1_bias = norm_backward(
            grad_act_one, normed_one, inverse_one, gain_one.astype(jnp.float32)
        )
        grad_tokens = (grad_res_one + grad_norm_one).reshape(chip_count, vis_len, D)
        chip_sums = jnp.sum(grad_tokens, axis=1)
        grad_wave_table = lax.dot_general(
            counts, chip_sums, (((0,), (0,)), ((), ())), precision=HIGH_PRECISION
        )
        small_grads = (grad_wave_table, grad_norm1_gain, grad_norm1_bias, grad_norm2_gain,
                       grad_norm2_bias, grad_mlp_in_bias, grad_mlp_out_bias, grad_dec_bias,
                       grad_mask_token)
        packed_sg, sg_widths = pack_rows(small_grads, n_dev, jnp.float32)
        reduced_sg = rs_chain(packed_sg, n_bits, order)
        (sum_wave, sum_g1, sum_b1, sum_g2, sum_b2, sum_ib, sum_ob, sum_db,
         sum_mask) = unpack_rows(reduced_sg, small_grads, sg_widths, n_dev, 1)
        sum_dec = rs_chain(grad_dec_weight, n_bits, order)
        sum_mlp_out = rs_chain(grad_mlp_out, n_bits, order)
        sum_mlp_in = rs_chain(grad_mlp_in, n_bits, order)
        sum_out = rs_chain(grad_out_weight, n_bits, order)
        sum_qkv = rs_chain(grad_qkv_weight, n_bits, order)
        summed = (sum_wave, sum_g1, sum_b1, sum_qkv, sum_out, sum_g2, sum_b2, sum_mlp_in,
                  sum_ib, sum_mlp_out, sum_ob, sum_dec, sum_db, sum_mask)
        return (decoded, grad_tokens, *summed)

    return local


def solution(mesh):
    n_dev = mesh.devices.size
    n_bits = n_dev.bit_length() - 1
    order = halving_order(n_bits, core_bit_of(mesh))
    placed = (
        P(AX, None, None),
        P(AX, None),
        P(AX, None),
        P(AX, None),
        P(AX),
        P(AX),
        P(AX, None),
        P(AX, None),
        P(AX),
        P(AX),
        P(AX, None),
        P(AX),
        P(AX, None),
        P(AX),
        P(AX, None),
        P(AX),
        P(AX),
        P(None, AX, None),
    )
    return jax.shard_map(
        make_local(n_bits, order),
        mesh=mesh,
        in_specs=placed,
        out_specs=(
            P(None, AX, None),
            P(AX, None, None),
            P(AX, None),
            P(AX),
            P(AX),
            P(AX, None),
            P(AX, None),
            P(AX),
            P(AX),
            P(AX, None),
            P(AX),
            P(AX, None),
            P(AX),
            P(AX, None),
            P(AX),
            P(AX),
        ),
        check_vma=False,
    )
```

```python
import numpy as np
import jax
import jax.numpy as jnp
from jax import lax
from jax.sharding import PartitionSpec as P

D = 768
HD = 64
DEC = 512
WAVES = 128
L = 1024

NORM_EPSILON = 1e-05
ROOT_HALF = 0.7071067811865476
INVERSE_ROOT_TAU = 0.3989422804014327
HIGH_PRECISION = lax.Precision.HIGHEST
AX = ("dp", "fsdp")


def product(left_op, right_op):
    return jnp.dot(left_op, right_op, preferred_element_type=jnp.float32)


def inner_rows(left_op, right_op):
    return lax.dot_general(
        left_op, right_op, (((0,), (0,)), ((), ())), preferred_element_type=jnp.float32
    )


def outer_cols(left_op, right_op):
    return lax.dot_general(
        left_op, right_op, (((1,), (1,)), ((), ())), preferred_element_type=jnp.float32
    )


def norm_forward(residual, gain, shift):
    mean_val = jnp.mean(residual, axis=-1, keepdims=True)
    centered = residual - mean_val
    variance = jnp.mean(centered * centered, axis=-1, keepdims=True)
    inverse = lax.rsqrt(variance + NORM_EPSILON)
    normed = centered * inverse
    return (normed * gain + shift, normed, inverse)


def norm_backward(incoming, normed, inverse, gain):
    scaled = incoming * gain
    first_mean = jnp.mean(scaled, axis=-1, keepdims=True)
    second_mean = jnp.mean(scaled * normed, axis=-1, keepdims=True)
    grad_input = inverse * (scaled - first_mean - normed * second_mean)
    return (grad_input, jnp.sum(incoming * normed, axis=0), jnp.sum(incoming, axis=0))


def gelu_value(hidden):
    return 0.5 * hidden * (1.0 + lax.erf(hidden * ROOT_HALF))


def gelu_slope(hidden):
    return (
        0.5 * (1.0 + lax.erf(hidden * ROOT_HALF))
        + hidden * jnp.exp(-0.5 * hidden * hidden) * INVERSE_ROOT_TAU
    )


def bit_groups(mesh):
    flat = list(mesh.devices.reshape(-1))
    n_bits = len(flat).bit_length() - 1
    first = flat[0]
    core_bit = None
    groups = {}
    for bit in range(n_bits):
        other = flat[1 << bit]
        if other.core_on_chip != first.core_on_chip:
            core_bit = bit
            continue
        axis = [a for a in range(len(first.coords)) if first.coords[a] != other.coords[a]]
        groups.setdefault(axis[0] if axis else -1, []).append(bit)
    return core_bit, [sorted(bits) for _, bits in sorted(groups.items())]


def halving_orders(core_bit, groups):
    head = [] if core_bit is None else [core_bit]
    orders = []
    for turn in range(max(1, len(groups))):
        rest = []
        for i in range(len(groups)):
            rest.extend(groups[(i + turn) % len(groups)])
        orders.append(head + rest)
    return orders


def rs_chain(grad, n_bits, order):
    n_dev = 2 ** n_bits
    me = lax.axis_index(AX)
    rows = grad.shape[0] // n_dev
    current = grad.reshape((2,) * n_bits + (rows,) + grad.shape[1:])
    for bit in order:
        axis = n_bits - 1 - bit
        mine = (me >> bit) & 1
        keep = lax.dynamic_slice_in_dim(current, mine, 1, axis=axis)
        send = lax.dynamic_slice_in_dim(current, 1 - mine, 1, axis=axis)
        moved = lax.ppermute(
            send.astype(jnp.bfloat16), AX, [(i, i ^ (1 << bit)) for i in range(n_dev)]
        )
        current = keep + moved.astype(jnp.float32)
    return current.reshape((rows,) + grad.shape[1:])


def pack_rows(arrays, n_dev, dtype):
    flat = [a.reshape(n_dev, -1).astype(dtype) for a in arrays]
    widths = [f.shape[1] for f in flat]
    padded = -sum(widths) % 1024
    flat.append(jnp.zeros((n_dev, padded), dtype))
    packed = jnp.concatenate(flat, axis=1)
    return packed.reshape(n_dev, 8, -1), widths


def unpack_rows(packed, arrays, widths, n_dev, leading):
    flat = packed.reshape(packed.shape[0], -1)
    out = []
    offset = 0
    for a, width in zip(arrays, widths):
        piece = flat[:, offset : offset + width]
        out.append(piece.reshape((leading * a.shape[0] // n_dev,) + a.shape[1:]))
        offset += width
    return out


def attend(queries, key_rows, value_rows):
    score_scale = HD ** (-0.5)
    scores = (
        jnp.einsum("cqhd,ckhd->chqk", queries, key_rows, preferred_element_type=jnp.float32)
        * score_scale
    )
    row_peak = jnp.max(scores, axis=-1, keepdims=True)
    exponents = jnp.exp(scores - row_peak)
    row_total = jnp.sum(exponents, axis=-1, keepdims=True)
    soft_full = exponents / row_total
    soft_low = soft_full.astype(jnp.bfloat16)
    mixture = jnp.einsum(
        "chqk,ckhd->cqhd", soft_low, value_rows, preferred_element_type=jnp.float32
    )
    return mixture.astype(jnp.bfloat16), soft_full, soft_low


def attend_back(queries, key_rows, value_rows, soft_full, soft_low, grad_mixture):
    score_scale = HD ** (-0.5)
    grad_values = jnp.einsum(
        "chqk,cqhd->ckhd", soft_low, grad_mixture, preferred_element_type=jnp.float32
    )
    grad_soft = jnp.einsum(
        "cqhd,ckhd->chqk", grad_mixture, value_rows, preferred_element_type=jnp.float32
    )
    row_delta = jnp.sum(grad_soft * soft_full, axis=-1, keepdims=True)
    grad_scores = (soft_full * (grad_soft - row_delta)).astype(jnp.bfloat16)
    grad_queries = (
        jnp.einsum("chqk,ckhd->cqhd", grad_scores, key_rows, preferred_element_type=jnp.float32)
        * score_scale
    )
    grad_keys = (
        jnp.einsum("chqk,cqhd->ckhd", grad_scores, queries, preferred_element_type=jnp.float32)
        * score_scale
    )
    return grad_queries, grad_keys, grad_values


def make_local(n_bits, orders):
    n_dev = 2 ** n_bits

    def local(
        tokens,
        band_waves,
        visible_slot,
        wave_table,
        norm1_gain,
        norm1_bias,
        qkv_weight,
        out_weight,
        norm2_gain,
        norm2_bias,
        mlp_in,
        mlp_in_bias,
        mlp_out,
        mlp_out_bias,
        dec_weight,
        dec_bias,
        mask_token,
        cot_decoded,
    ):
        shards = (
            wave_table,
            norm1_gain,
            norm1_bias,
            qkv_weight,
            out_weight,
            norm2_gain,
            norm2_bias,
            mlp_in,
            mlp_in_bias,
            mlp_out,
            mlp_out_bias,
            dec_weight,
            dec_bias,
            mask_token,
        )
        small = (wave_table, norm1_gain, norm1_bias, norm2_gain, norm2_bias, mlp_in_bias,
                 mlp_out_bias, dec_bias, mask_token)
        small_flat = [a.reshape(-1) for a in small]
        small_widths = [f.shape[0] for f in small_flat]
        rows_here = qkv_weight.shape[0]
        small_cols = -(-sum(small_widths) // (rows_here * 128)) * 128
        small_pad = rows_here * small_cols - sum(small_widths)
        small_block = jnp.concatenate(
            small_flat + [jnp.zeros((small_pad,), jnp.bfloat16)]
        ).reshape(rows_here, small_cols)
        wide = (qkv_weight, out_weight, mlp_in, dec_weight, small_block)
        wide_cols = [a.shape[1] for a in wide]
        gathered_wide = lax.all_gather(jnp.concatenate(wide, axis=1), AX, axis=0, tiled=True)
        wide_full = []
        offset = 0
        for cols in wide_cols:
            wide_full.append(gathered_wide[:, offset : offset + cols])
            offset += cols
        qkv_full, out_full, inner_full, dec_full, small_full = wide_full
        small_rows = small_full.reshape(n_dev, rows_here * small_cols)
        small_parts = []
        offset = 0
        for a, width in zip(small, small_widths):
            piece = small_rows[:, offset : offset + width]
            small_parts.append(piece.reshape((n_dev * a.shape[0],) + a.shape[1:]))
            offset += width
        (wave_full, gain_one, shift_one, gain_two, shift_two, inner_bias, outer_bias,
         dec_shift, mask_full) = small_parts
        outer_full = lax.all_gather(mlp_out, AX, axis=0, tiled=True)

        chip_count, vis_len, feature_width = tokens.shape
        row_count = chip_count * vis_len
        heads = feature_width // HD
        counts = jnp.sum(
            (band_waves[:, :, None] == jnp.arange(WAVES, dtype=jnp.int32)[None, None, :]).astype(
                jnp.float32
            ),
            axis=1,
        )
        spectral = jnp.dot(
            counts.astype(jnp.bfloat16), wave_full, preferred_element_type=jnp.float32
        )
        residual = (tokens.astype(jnp.float32) + spectral[:, None, :]).reshape(row_count, D)
        norm_out_one, normed_one, inverse_one = norm_forward(
            residual, gain_one.astype(jnp.float32), shift_one.astype(jnp.float32)
        )
        act_one = norm_out_one.astype(jnp.bfloat16)
        qkv_vals = product(act_one, qkv_full).astype(jnp.bfloat16)
        head_shape = (chip_count, vis_len, heads, HD)
        queries = qkv_vals[:, :D].reshape(head_shape)
        key_rows = qkv_vals[:, D : 2 * D].reshape(head_shape)
        value_rows = qkv_vals[:, 2 * D :].reshape(head_shape)
        mixture4, soft_full, soft_low = attend(queries, key_rows, value_rows)
        mixture = mixture4.reshape(row_count, D)
        res_one = residual + product(mixture, out_full)
        norm_out_two, normed_two, inverse_two = norm_forward(
            res_one, gain_two.astype(jnp.float32), shift_two.astype(jnp.float32)
        )
        act_two = norm_out_two.astype(jnp.bfloat16)
        hidden = product(act_two, inner_full) + inner_bias.astype(jnp.float32)
        active = gelu_value(hidden).astype(jnp.bfloat16)
        res_two = res_one + (product(active, outer_full) + outer_bias.astype(jnp.float32))
        enc_low = res_two.astype(jnp.bfloat16)
        projected = (product(enc_low, dec_full) + dec_shift.astype(jnp.float32)).astype(
            jnp.bfloat16
        )
        slot_ids = jnp.arange(L, dtype=jnp.int32)
        one_hot = (visible_slot[:, None, :] == slot_ids[None, :, None]).astype(jnp.bfloat16)
        filled_vis = jnp.einsum(
            "csi,cie->cse",
            one_hot,
            projected.reshape(chip_count, vis_len, DEC),
            preferred_element_type=jnp.float32,
        )
        has_row = jnp.sum(one_hot.astype(jnp.float32), axis=2, keepdims=True) > 0.5
        filled = jnp.where(has_row, filled_vis, mask_full.astype(jnp.float32)[None, None, :])
        filled = filled.astype(jnp.bfloat16)
        decoded = lax.all_to_all(filled, AX, split_axis=1, concat_axis=0, tiled=True)
        grad_full = lax.all_to_all(cot_decoded, AX, split_axis=0, concat_axis=1, tiled=True)

        grad_vis_low = (
            jnp.einsum("csi,cse->cie", one_hot, grad_full, preferred_element_type=jnp.float32)
            .astype(jnp.bfloat16)
            .reshape(row_count, DEC)
        )
        grad_vis = grad_vis_low.astype(jnp.float32)
        grad_mask_token = jnp.sum(
            jnp.where(has_row, 0.0, grad_full.astype(jnp.float32)), axis=(0, 1)
        )
        grad_dec_bias = jnp.sum(grad_vis, axis=0)
        grad_dec_weight = inner_rows(enc_low, grad_vis_low)
        grad_res_two = outer_cols(grad_vis_low, dec_full)
        grad_ffo = grad_res_two.astype(jnp.bfloat16)
        grad_mlp_out_bias = jnp.sum(grad_ffo.astype(jnp.float32), axis=0)
        grad_mlp_out = inner_rows(active, grad_ffo)
        grad_hidden = (outer_cols(grad_ffo, outer_full) * gelu_slope(hidden)).astype(jnp.bfloat16)
        grad_mlp_in_bias = jnp.sum(grad_hidden.astype(jnp.float32), axis=0)
        grad_mlp_in = inner_rows(act_two, grad_hidden)
        grad_act_two = outer_cols(grad_hidden, inner_full)
        grad_norm_two, grad_norm2_gain, grad_norm2_bias = norm_backward(
            grad_act_two, normed_two, inverse_two, gain_two.astype(jnp.float32)
        )
        grad_res_one = grad_res_two + grad_norm_two
        grad_att = grad_res_one.astype(jnp.bfloat16)
        grad_out_weight = inner_rows(mixture, grad_att)
        grad_mixed = outer_cols(grad_att, out_full).astype(jnp.bfloat16).reshape(head_shape)
        grad_queries, grad_keys, grad_values = attend_back(
            queries, key_rows, value_rows, soft_full, soft_low, grad_mixed
        )
        grad_qkv = jnp.concatenate(
            [
                grad_queries.reshape(row_count, D),
                grad_keys.reshape(row_count, D),
                grad_values.reshape(row_count, D),
            ],
            axis=1,
        ).astype(jnp.bfloat16)
        grad_qkv_weight = inner_rows(act_one, grad_qkv)
        grad_act_one = outer_cols(grad_qkv, qkv_full)
        grad_norm_one, grad_norm1_gain, grad_norm1_bias = norm_backward(
            grad_act_one, normed_one, inverse_one, gain_one.astype(jnp.float32)
        )
        grad_tokens = (grad_res_one + grad_norm_one).reshape(chip_count, vis_len, D)
        chip_sums = jnp.sum(grad_tokens, axis=1)
        grad_wave_table = lax.dot_general(
            counts, chip_sums, (((0,), (0,)), ((), ())), precision=HIGH_PRECISION
        )
        small_grads = (grad_wave_table, grad_norm1_gain, grad_norm1_bias, grad_norm2_gain,
                       grad_norm2_bias, grad_mlp_in_bias, grad_mlp_out_bias, grad_dec_bias,
                       grad_mask_token)
        packed_sg, sg_widths = pack_rows(small_grads, n_dev, jnp.float32)
        turn = lambda k: orders[k % len(orders)]
        reduced_sg = rs_chain(packed_sg, n_bits, turn(2))
        (sum_wave, sum_g1, sum_b1, sum_g2, sum_b2, sum_ib, sum_ob, sum_db,
         sum_mask) = unpack_rows(reduced_sg, small_grads, sg_widths, n_dev, 1)
        sum_dec = rs_chain(grad_dec_weight, n_bits, turn(1))
        sum_mlp_out = rs_chain(grad_mlp_out, n_bits, turn(1))
        sum_mlp_in = rs_chain(grad_mlp_in, n_bits, turn(0))
        sum_out = rs_chain(grad_out_weight, n_bits, turn(0))
        sum_qkv = rs_chain(grad_qkv_weight, n_bits, turn(2))
        summed = (sum_wave, sum_g1, sum_b1, sum_qkv, sum_out, sum_g2, sum_b2, sum_mlp_in,
                  sum_ib, sum_mlp_out, sum_ob, sum_dec, sum_db, sum_mask)
        return (decoded, grad_tokens, *summed)

    return local


def solution(mesh):
    n_dev = mesh.devices.size
    n_bits = n_dev.bit_length() - 1
    orders = halving_orders(*bit_groups(mesh))
    placed = (
        P(AX, None, None),
        P(AX, None),
        P(AX, None),
        P(AX, None),
        P(AX),
        P(AX),
        P(AX, None),
        P(AX, None),
        P(AX),
        P(AX),
        P(AX, None),
        P(AX),
        P(AX, None),
        P(AX),
        P(AX, None),
        P(AX),
        P(AX),
        P(None, AX, None),
    )
    return jax.shard_map(
        make_local(n_bits, orders),
        mesh=mesh,
        in_specs=placed,
        out_specs=(
            P(None, AX, None),
            P(AX, None, None),
            P(AX, None),
            P(AX),
            P(AX),
            P(AX, None),
            P(AX, None),
            P(AX),
            P(AX),
            P(AX, None),
            P(AX),
            P(AX, None),
            P(AX),
            P(AX, None),
            P(AX),
            P(AX),
        ),
        check_vma=False,
    )
```

```python
import numpy as np
import jax
import jax.numpy as jnp
from jax import lax
from jax.sharding import PartitionSpec as P

D = 768
HD = 64
DEC = 512
WAVES = 128
L = 1024

NORM_EPSILON = 1e-05
ROOT_HALF = 0.7071067811865476
INVERSE_ROOT_TAU = 0.3989422804014327
HIGH_PRECISION = lax.Precision.HIGHEST
AX = ("dp", "fsdp")


def product(left_op, right_op):
    return jnp.dot(left_op, right_op, preferred_element_type=jnp.float32)


def inner_rows(left_op, right_op):
    return lax.dot_general(
        left_op, right_op, (((0,), (0,)), ((), ())), preferred_element_type=jnp.float32
    )


def outer_cols(left_op, right_op):
    return lax.dot_general(
        left_op, right_op, (((1,), (1,)), ((), ())), preferred_element_type=jnp.float32
    )


def norm_forward(residual, gain, shift):
    mean_val = jnp.mean(residual, axis=-1, keepdims=True)
    centered = residual - mean_val
    variance = jnp.mean(centered * centered, axis=-1, keepdims=True)
    inverse = lax.rsqrt(variance + NORM_EPSILON)
    normed = centered * inverse
    return (normed * gain + shift, normed, inverse)


def norm_backward(incoming, normed, inverse, gain):
    scaled = incoming * gain
    first_mean = jnp.mean(scaled, axis=-1, keepdims=True)
    second_mean = jnp.mean(scaled * normed, axis=-1, keepdims=True)
    grad_input = inverse * (scaled - first_mean - normed * second_mean)
    return (grad_input, jnp.sum(incoming * normed, axis=0), jnp.sum(incoming, axis=0))


def gelu_value(hidden):
    return 0.5 * hidden * (1.0 + lax.erf(hidden * ROOT_HALF))


def gelu_slope(hidden):
    return (
        0.5 * (1.0 + lax.erf(hidden * ROOT_HALF))
        + hidden * jnp.exp(-0.5 * hidden * hidden) * INVERSE_ROOT_TAU
    )


def bit_groups(mesh):
    flat = list(mesh.devices.reshape(-1))
    n_bits = len(flat).bit_length() - 1
    first = flat[0]
    core_bit = None
    groups = {}
    for bit in range(n_bits):
        other = flat[1 << bit]
        if other.core_on_chip != first.core_on_chip:
            core_bit = bit
            continue
        axis = [a for a in range(len(first.coords)) if first.coords[a] != other.coords[a]]
        groups.setdefault(axis[0] if axis else -1, []).append(bit)
    return core_bit, [sorted(bits) for _, bits in sorted(groups.items())]


def halving_orders(core_bit, groups):
    head = [] if core_bit is None else [core_bit]
    orders = []
    for turn in range(max(1, len(groups))):
        rest = []
        for i in range(len(groups)):
            rest.extend(groups[(i + turn) % len(groups)])
        orders.append(head + rest)
    return orders


def rs_chain(grad, n_bits, order):
    n_dev = 2 ** n_bits
    me = lax.axis_index(AX)
    rows = grad.shape[0] // n_dev
    current = grad.reshape((2,) * n_bits + (rows,) + grad.shape[1:])
    for bit in order:
        axis = n_bits - 1 - bit
        mine = (me >> bit) & 1
        keep = lax.dynamic_slice_in_dim(current, mine, 1, axis=axis)
        send = lax.dynamic_slice_in_dim(current, 1 - mine, 1, axis=axis)
        moved = lax.ppermute(
            send.astype(jnp.bfloat16), AX, [(i, i ^ (1 << bit)) for i in range(n_dev)]
        )
        current = keep + moved.astype(jnp.float32)
    return current.reshape((rows,) + grad.shape[1:])


def rs_split(grad, n_bits, orders, first):
    cols = grad.shape[-1]
    parts = 3 if cols % 384 == 0 else (2 if cols % 256 == 0 else 1)
    width = cols // parts
    pieces = [
        rs_chain(grad[..., k * width : (k + 1) * width], n_bits, orders[(first + k) % len(orders)])
        for k in range(parts)
    ]
    return pieces[0] if parts == 1 else jnp.concatenate(pieces, axis=-1)


def pack_rows(arrays, n_dev, dtype):
    flat = [a.reshape(n_dev, -1).astype(dtype) for a in arrays]
    widths = [f.shape[1] for f in flat]
    padded = -sum(widths) % 1024
    flat.append(jnp.zeros((n_dev, padded), dtype))
    packed = jnp.concatenate(flat, axis=1)
    return packed.reshape(n_dev, 8, -1), widths


def unpack_rows(packed, arrays, widths, n_dev, leading):
    flat = packed.reshape(packed.shape[0], -1)
    out = []
    offset = 0
    for a, width in zip(arrays, widths):
        piece = flat[:, offset : offset + width]
        out.append(piece.reshape((leading * a.shape[0] // n_dev,) + a.shape[1:]))
        offset += width
    return out


def attend(queries, key_rows, value_rows):
    score_scale = HD ** (-0.5)
    scores = (
        jnp.einsum("cqhd,ckhd->chqk", queries, key_rows, preferred_element_type=jnp.float32)
        * score_scale
    )
    row_peak = jnp.max(scores, axis=-1, keepdims=True)
    exponents = jnp.exp(scores - row_peak)
    row_total = jnp.sum(exponents, axis=-1, keepdims=True)
    soft_full = exponents / row_total
    soft_low = soft_full.astype(jnp.bfloat16)
    mixture = jnp.einsum(
        "chqk,ckhd->cqhd", soft_low, value_rows, preferred_element_type=jnp.float32
    )
    return mixture.astype(jnp.bfloat16), soft_full, soft_low


def attend_back(queries, key_rows, value_rows, soft_full, soft_low, grad_mixture):
    score_scale = HD ** (-0.5)
    grad_values = jnp.einsum(
        "chqk,cqhd->ckhd", soft_low, grad_mixture, preferred_element_type=jnp.float32
    )
    grad_soft = jnp.einsum(
        "cqhd,ckhd->chqk", grad_mixture, value_rows, preferred_element_type=jnp.float32
    )
    row_delta = jnp.sum(grad_soft * soft_full, axis=-1, keepdims=True)
    grad_scores = (soft_full * (grad_soft - row_delta)).astype(jnp.bfloat16)
    grad_queries = (
        jnp.einsum("chqk,ckhd->cqhd", grad_scores, key_rows, preferred_element_type=jnp.float32)
        * score_scale
    )
    grad_keys = (
        jnp.einsum("chqk,cqhd->ckhd", grad_scores, queries, preferred_element_type=jnp.float32)
        * score_scale
    )
    return grad_queries, grad_keys, grad_values


def make_local(n_bits, orders):
    n_dev = 2 ** n_bits

    def local(
        tokens,
        band_waves,
        visible_slot,
        wave_table,
        norm1_gain,
        norm1_bias,
        qkv_weight,
        out_weight,
        norm2_gain,
        norm2_bias,
        mlp_in,
        mlp_in_bias,
        mlp_out,
        mlp_out_bias,
        dec_weight,
        dec_bias,
        mask_token,
        cot_decoded,
    ):
        shards = (
            wave_table,
            norm1_gain,
            norm1_bias,
            qkv_weight,
            out_weight,
            norm2_gain,
            norm2_bias,
            mlp_in,
            mlp_in_bias,
            mlp_out,
            mlp_out_bias,
            dec_weight,
            dec_bias,
            mask_token,
        )
        small = (wave_table, norm1_gain, norm1_bias, norm2_gain, norm2_bias, mlp_in_bias,
                 mlp_out_bias, dec_bias, mask_token)
        small_flat = [a.reshape(-1) for a in small]
        small_widths = [f.shape[0] for f in small_flat]
        rows_here = qkv_weight.shape[0]
        small_cols = -(-sum(small_widths) // (rows_here * 128)) * 128
        small_pad = rows_here * small_cols - sum(small_widths)
        small_block = jnp.concatenate(
            small_flat + [jnp.zeros((small_pad,), jnp.bfloat16)]
        ).reshape(rows_here, small_cols)
        wide = (qkv_weight, out_weight, mlp_in, dec_weight, small_block)
        wide_cols = [a.shape[1] for a in wide]
        gathered_wide = lax.all_gather(jnp.concatenate(wide, axis=1), AX, axis=0, tiled=True)
        wide_full = []
        offset = 0
        for cols in wide_cols:
            wide_full.append(gathered_wide[:, offset : offset + cols])
            offset += cols
        qkv_full, out_full, inner_full, dec_full, small_full = wide_full
        small_rows = small_full.reshape(n_dev, rows_here * small_cols)
        small_parts = []
        offset = 0
        for a, width in zip(small, small_widths):
            piece = small_rows[:, offset : offset + width]
            small_parts.append(piece.reshape((n_dev * a.shape[0],) + a.shape[1:]))
            offset += width
        (wave_full, gain_one, shift_one, gain_two, shift_two, inner_bias, outer_bias,
         dec_shift, mask_full) = small_parts
        outer_full = lax.all_gather(mlp_out, AX, axis=0, tiled=True)

        chip_count, vis_len, feature_width = tokens.shape
        row_count = chip_count * vis_len
        heads = feature_width // HD
        counts = jnp.sum(
            (band_waves[:, :, None] == jnp.arange(WAVES, dtype=jnp.int32)[None, None, :]).astype(
                jnp.float32
            ),
            axis=1,
        )
        spectral = jnp.dot(
            counts.astype(jnp.bfloat16), wave_full, preferred_element_type=jnp.float32
        )
        residual = (tokens.astype(jnp.float32) + spectral[:, None, :]).reshape(row_count, D)
        norm_out_one, normed_one, inverse_one = norm_forward(
            residual, gain_one.astype(jnp.float32), shift_one.astype(jnp.float32)
        )
        act_one = norm_out_one.astype(jnp.bfloat16)
        qkv_vals = product(act_one, qkv_full).astype(jnp.bfloat16)
        head_shape = (chip_count, vis_len, heads, HD)
        queries = qkv_vals[:, :D].reshape(head_shape)
        key_rows = qkv_vals[:, D : 2 * D].reshape(head_shape)
        value_rows = qkv_vals[:, 2 * D :].reshape(head_shape)
        mixture4, soft_full, soft_low = attend(queries, key_rows, value_rows)
        mixture = mixture4.reshape(row_count, D)
        res_one = residual + product(mixture, out_full)
        norm_out_two, normed_two, inverse_two = norm_forward(
            res_one, gain_two.astype(jnp.float32), shift_two.astype(jnp.float32)
        )
        act_two = norm_out_two.astype(jnp.bfloat16)
        hidden = product(act_two, inner_full) + inner_bias.astype(jnp.float32)
        active = gelu_value(hidden).astype(jnp.bfloat16)
        res_two = res_one + (product(active, outer_full) + outer_bias.astype(jnp.float32))
        enc_low = res_two.astype(jnp.bfloat16)
        projected = (product(enc_low, dec_full) + dec_shift.astype(jnp.float32)).astype(
            jnp.bfloat16
        )
        slot_ids = jnp.arange(L, dtype=jnp.int32)
        one_hot = (visible_slot[:, None, :] == slot_ids[None, :, None]).astype(jnp.bfloat16)
        filled_vis = jnp.einsum(
            "csi,cie->cse",
            one_hot,
            projected.reshape(chip_count, vis_len, DEC),
            preferred_element_type=jnp.float32,
        )
        has_row = jnp.sum(one_hot.astype(jnp.float32), axis=2, keepdims=True) > 0.5
        filled = jnp.where(has_row, filled_vis, mask_full.astype(jnp.float32)[None, None, :])
        filled = filled.astype(jnp.bfloat16)
        decoded = lax.all_to_all(filled, AX, split_axis=1, concat_axis=0, tiled=True)
        grad_full = lax.all_to_all(cot_decoded, AX, split_axis=0, concat_axis=1, tiled=True)

        grad_vis_low = (
            jnp.einsum("csi,cse->cie", one_hot, grad_full, preferred_element_type=jnp.float32)
            .astype(jnp.bfloat16)
            .reshape(row_count, DEC)
        )
        grad_vis = grad_vis_low.astype(jnp.float32)
        grad_mask_token = jnp.sum(
            jnp.where(has_row, 0.0, grad_full.astype(jnp.float32)), axis=(0, 1)
        )
        grad_dec_bias = jnp.sum(grad_vis, axis=0)
        grad_dec_weight = inner_rows(enc_low, grad_vis_low)
        grad_res_two = outer_cols(grad_vis_low, dec_full)
        grad_dec_weight, grad_res_two = lax.optimization_barrier((grad_dec_weight, grad_res_two))
        grad_ffo = grad_res_two.astype(jnp.bfloat16)
        grad_mlp_out_bias = jnp.sum(grad_ffo.astype(jnp.float32), axis=0)
        grad_mlp_out = inner_rows(active, grad_ffo)
        grad_hidden = (outer_cols(grad_ffo, outer_full) * gelu_slope(hidden)).astype(jnp.bfloat16)
        grad_mlp_out, grad_hidden = lax.optimization_barrier((grad_mlp_out, grad_hidden))
        grad_mlp_in_bias = jnp.sum(grad_hidden.astype(jnp.float32), axis=0)
        grad_mlp_in = inner_rows(act_two, grad_hidden)
        grad_act_two = outer_cols(grad_hidden, inner_full)
        grad_mlp_in, grad_act_two = lax.optimization_barrier((grad_mlp_in, grad_act_two))
        grad_norm_two, grad_norm2_gain, grad_norm2_bias = norm_backward(
            grad_act_two, normed_two, inverse_two, gain_two.astype(jnp.float32)
        )
        grad_res_one = grad_res_two + grad_norm_two
        grad_att = grad_res_one.astype(jnp.bfloat16)
        grad_out_weight = inner_rows(mixture, grad_att)
        grad_out_weight, grad_att = lax.optimization_barrier((grad_out_weight, grad_att))
        grad_mixed = outer_cols(grad_att, out_full).astype(jnp.bfloat16).reshape(head_shape)
        grad_queries, grad_keys, grad_values = attend_back(
            queries, key_rows, value_rows, soft_full, soft_low, grad_mixed
        )
        grad_qkv = jnp.concatenate(
            [
                grad_queries.reshape(row_count, D),
                grad_keys.reshape(row_count, D),
                grad_values.reshape(row_count, D),
            ],
            axis=1,
        ).astype(jnp.bfloat16)
        grad_qkv_weight = inner_rows(act_one, grad_qkv)
        grad_act_one = outer_cols(grad_qkv, qkv_full)
        grad_norm_one, grad_norm1_gain, grad_norm1_bias = norm_backward(
            grad_act_one, normed_one, inverse_one, gain_one.astype(jnp.float32)
        )
        grad_tokens = (grad_res_one + grad_norm_one).reshape(chip_count, vis_len, D)
        chip_sums = jnp.sum(grad_tokens, axis=1)
        grad_wave_table = lax.dot_general(
            counts, chip_sums, (((0,), (0,)), ((), ())), precision=HIGH_PRECISION
        )
        small_grads = (grad_wave_table, grad_norm1_gain, grad_norm1_bias, grad_norm2_gain,
                       grad_norm2_bias, grad_mlp_in_bias, grad_mlp_out_bias, grad_dec_bias,
                       grad_mask_token)
        packed_sg, sg_widths = pack_rows(small_grads, n_dev, jnp.float32)
        turn = lambda k: orders[k % len(orders)]
        reduced_sg = rs_chain(packed_sg, n_bits, turn(2))
        (sum_wave, sum_g1, sum_b1, sum_g2, sum_b2, sum_ib, sum_ob, sum_db,
         sum_mask) = unpack_rows(reduced_sg, small_grads, sg_widths, n_dev, 1)
        sum_dec = rs_split(grad_dec_weight, n_bits, orders, 1)
        sum_mlp_out = rs_split(grad_mlp_out, n_bits, orders, 1)
        sum_mlp_in = rs_split(grad_mlp_in, n_bits, orders, 0)
        sum_out = rs_split(grad_out_weight, n_bits, orders, 0)
        sum_qkv = rs_split(grad_qkv_weight, n_bits, orders, 2)
        summed = (sum_wave, sum_g1, sum_b1, sum_qkv, sum_out, sum_g2, sum_b2, sum_mlp_in,
                  sum_ib, sum_mlp_out, sum_ob, sum_dec, sum_db, sum_mask)
        return (decoded, grad_tokens, *summed)

    return local


def solution(mesh):
    n_dev = mesh.devices.size
    n_bits = n_dev.bit_length() - 1
    orders = halving_orders(*bit_groups(mesh))
    placed = (
        P(AX, None, None),
        P(AX, None),
        P(AX, None),
        P(AX, None),
        P(AX),
        P(AX),
        P(AX, None),
        P(AX, None),
        P(AX),
        P(AX),
        P(AX, None),
        P(AX),
        P(AX, None),
        P(AX),
        P(AX, None),
        P(AX),
        P(AX),
        P(None, AX, None),
    )
    return jax.shard_map(
        make_local(n_bits, orders),
        mesh=mesh,
        in_specs=placed,
        out_specs=(
            P(None, AX, None),
            P(AX, None, None),
            P(AX, None),
            P(AX),
            P(AX),
            P(AX, None),
            P(AX, None),
            P(AX),
            P(AX),
            P(AX, None),
            P(AX),
            P(AX, None),
            P(AX),
            P(AX, None),
            P(AX),
            P(AX),
        ),
        check_vma=False,
    )
```

```python
import numpy as np
import jax
import jax.numpy as jnp
from jax import lax
from jax.sharding import PartitionSpec as P

D = 768
HD = 64
DEC = 512
WAVES = 128
L = 1024

NORM_EPSILON = 1e-05
ROOT_HALF = 0.7071067811865476
INVERSE_ROOT_TAU = 0.3989422804014327
HIGH_PRECISION = lax.Precision.HIGHEST
AX = ("dp", "fsdp")


def product(left_op, right_op):
    return jnp.dot(left_op, right_op, preferred_element_type=jnp.float32)


def inner_rows(left_op, right_op):
    return lax.dot_general(
        left_op, right_op, (((0,), (0,)), ((), ())), preferred_element_type=jnp.float32
    )


def outer_cols(left_op, right_op):
    return lax.dot_general(
        left_op, right_op, (((1,), (1,)), ((), ())), preferred_element_type=jnp.float32
    )


def norm_forward(residual, gain, shift):
    mean_val = jnp.mean(residual, axis=-1, keepdims=True)
    centered = residual - mean_val
    variance = jnp.mean(centered * centered, axis=-1, keepdims=True)
    inverse = lax.rsqrt(variance + NORM_EPSILON)
    normed = centered * inverse
    return (normed * gain + shift, normed, inverse)


def norm_backward(incoming, normed, inverse, gain):
    scaled = incoming * gain
    first_mean = jnp.mean(scaled, axis=-1, keepdims=True)
    second_mean = jnp.mean(scaled * normed, axis=-1, keepdims=True)
    grad_input = inverse * (scaled - first_mean - normed * second_mean)
    return (grad_input, jnp.sum(incoming * normed, axis=0), jnp.sum(incoming, axis=0))


def gelu_value(hidden):
    return 0.5 * hidden * (1.0 + lax.erf(hidden * ROOT_HALF))


def gelu_slope(hidden):
    return (
        0.5 * (1.0 + lax.erf(hidden * ROOT_HALF))
        + hidden * jnp.exp(-0.5 * hidden * hidden) * INVERSE_ROOT_TAU
    )


def bit_groups(mesh):
    flat = list(mesh.devices.reshape(-1))
    n_bits = len(flat).bit_length() - 1
    first = flat[0]
    core_bit = None
    groups = {}
    for bit in range(n_bits):
        other = flat[1 << bit]
        if other.core_on_chip != first.core_on_chip:
            core_bit = bit
            continue
        axis = [a for a in range(len(first.coords)) if first.coords[a] != other.coords[a]]
        groups.setdefault(axis[0] if axis else -1, []).append(bit)
    return core_bit, [sorted(bits) for _, bits in sorted(groups.items())]


def halving_orders(core_bit, groups):
    head = [] if core_bit is None else [core_bit]
    orders = []
    for turn in range(max(1, len(groups))):
        rest = []
        for i in range(len(groups)):
            rest.extend(groups[(i + turn) % len(groups)])
        orders.append(head + rest)
    if len(groups) >= 2:
        swapped = [groups[1], groups[0]] + groups[2:]
        orders.insert(0, head + [b for g in swapped for b in g])
    return orders


def rs_chain(grad, n_bits, order):
    n_dev = 2 ** n_bits
    me = lax.axis_index(AX)
    rows = grad.shape[0] // n_dev
    current = grad.reshape((2,) * n_bits + (rows,) + grad.shape[1:])
    for bit in order:
        axis = n_bits - 1 - bit
        mine = (me >> bit) & 1
        keep = lax.dynamic_slice_in_dim(current, mine, 1, axis=axis)
        send = lax.dynamic_slice_in_dim(current, 1 - mine, 1, axis=axis)
        moved = lax.ppermute(
            send.astype(jnp.bfloat16), AX, [(i, i ^ (1 << bit)) for i in range(n_dev)]
        )
        current = keep + moved.astype(jnp.float32)
    return current.reshape((rows,) + grad.shape[1:])


def ag_chain(block, n_bits, order):
    me = lax.axis_index(AX)
    n_dev = 2 ** n_bits
    current = block.reshape((1,) * n_bits + block.shape)
    for bit in reversed(order):
        axis = n_bits - 1 - bit
        mine = ((me >> bit) & 1) == 1
        moved = lax.ppermute(current, AX, [(i, i ^ (1 << bit)) for i in range(n_dev)])
        low = jnp.where(mine, moved, current)
        high = jnp.where(mine, current, moved)
        current = jnp.concatenate([low, high], axis=axis)
    return current.reshape((n_dev * block.shape[0],) + block.shape[1:])


def pack_rows(arrays, n_dev, dtype):
    flat = [a.reshape(n_dev, -1).astype(dtype) for a in arrays]
    widths = [f.shape[1] for f in flat]
    padded = -sum(widths) % 1024
    flat.append(jnp.zeros((n_dev, padded), dtype))
    packed = jnp.concatenate(flat, axis=1)
    return packed.reshape(n_dev, 8, -1), widths


def unpack_rows(packed, arrays, widths, n_dev, leading):
    flat = packed.reshape(packed.shape[0], -1)
    out = []
    offset = 0
    for a, width in zip(arrays, widths):
        piece = flat[:, offset : offset + width]
        out.append(piece.reshape((leading * a.shape[0] // n_dev,) + a.shape[1:]))
        offset += width
    return out


def attend(queries, key_rows, value_rows):
    score_scale = HD ** (-0.5)
    scores = (
        jnp.einsum("cqhd,ckhd->chqk", queries, key_rows, preferred_element_type=jnp.float32)
        * score_scale
    )
    row_peak = jnp.max(scores, axis=-1, keepdims=True)
    exponents = jnp.exp(scores - row_peak)
    row_total = jnp.sum(exponents, axis=-1, keepdims=True)
    soft_full = exponents / row_total
    soft_low = soft_full.astype(jnp.bfloat16)
    mixture = jnp.einsum(
        "chqk,ckhd->cqhd", soft_low, value_rows, preferred_element_type=jnp.float32
    )
    return mixture.astype(jnp.bfloat16), soft_full, soft_low


def attend_back(queries, key_rows, value_rows, soft_full, soft_low, grad_mixture):
    score_scale = HD ** (-0.5)
    grad_values = jnp.einsum(
        "chqk,cqhd->ckhd", soft_low, grad_mixture, preferred_element_type=jnp.float32
    )
    grad_soft = jnp.einsum(
        "cqhd,ckhd->chqk", grad_mixture, value_rows, preferred_element_type=jnp.float32
    )
    row_delta = jnp.sum(grad_soft * soft_full, axis=-1, keepdims=True)
    grad_scores = (soft_full * (grad_soft - row_delta)).astype(jnp.bfloat16)
    grad_queries = (
        jnp.einsum("chqk,ckhd->cqhd", grad_scores, key_rows, preferred_element_type=jnp.float32)
        * score_scale
    )
    grad_keys = (
        jnp.einsum("chqk,cqhd->ckhd", grad_scores, queries, preferred_element_type=jnp.float32)
        * score_scale
    )
    return grad_queries, grad_keys, grad_values


def make_local(n_bits, orders):
    n_dev = 2 ** n_bits

    def local(
        tokens,
        band_waves,
        visible_slot,
        wave_table,
        norm1_gain,
        norm1_bias,
        qkv_weight,
        out_weight,
        norm2_gain,
        norm2_bias,
        mlp_in,
        mlp_in_bias,
        mlp_out,
        mlp_out_bias,
        dec_weight,
        dec_bias,
        mask_token,
        cot_decoded,
    ):
        shards = (
            wave_table,
            norm1_gain,
            norm1_bias,
            qkv_weight,
            out_weight,
            norm2_gain,
            norm2_bias,
            mlp_in,
            mlp_in_bias,
            mlp_out,
            mlp_out_bias,
            dec_weight,
            dec_bias,
            mask_token,
        )
        small = (wave_table, norm1_gain, norm1_bias, norm2_gain, norm2_bias, mlp_in_bias,
                 mlp_out_bias, dec_bias, mask_token)
        small_flat = [a.reshape(-1) for a in small]
        small_widths = [f.shape[0] for f in small_flat]
        rows_here = qkv_weight.shape[0]
        small_cols = -(-sum(small_widths) // (rows_here * 128)) * 128
        small_pad = rows_here * small_cols - sum(small_widths)
        small_block = jnp.concatenate(
            small_flat + [jnp.zeros((small_pad,), jnp.bfloat16)]
        ).reshape(rows_here, small_cols)
        wide = (qkv_weight, out_weight, mlp_in, dec_weight, small_block)
        wide_cols = [a.shape[1] for a in wide]
        gathered_wide = lax.all_gather(jnp.concatenate(wide, axis=1), AX, axis=0, tiled=True)
        wide_full = []
        offset = 0
        for cols in wide_cols:
            wide_full.append(gathered_wide[:, offset : offset + cols])
            offset += cols
        qkv_full, out_full, inner_full, dec_full, small_full = wide_full
        small_rows = small_full.reshape(n_dev, rows_here * small_cols)
        small_parts = []
        offset = 0
        for a, width in zip(small, small_widths):
            piece = small_rows[:, offset : offset + width]
            small_parts.append(piece.reshape((n_dev * a.shape[0],) + a.shape[1:]))
            offset += width
        (wave_full, gain_one, shift_one, gain_two, shift_two, inner_bias, outer_bias,
         dec_shift, mask_full) = small_parts
        outer_full = ag_chain(mlp_out, n_bits, orders[1])

        chip_count, vis_len, feature_width = tokens.shape
        row_count = chip_count * vis_len
        heads = feature_width // HD
        counts = jnp.sum(
            (band_waves[:, :, None] == jnp.arange(WAVES, dtype=jnp.int32)[None, None, :]).astype(
                jnp.float32
            ),
            axis=1,
        )
        spectral = jnp.dot(
            counts.astype(jnp.bfloat16), wave_full, preferred_element_type=jnp.float32
        )
        residual = (tokens.astype(jnp.float32) + spectral[:, None, :]).reshape(row_count, D)
        norm_out_one, normed_one, inverse_one = norm_forward(
            residual, gain_one.astype(jnp.float32), shift_one.astype(jnp.float32)
        )
        act_one = norm_out_one.astype(jnp.bfloat16)
        qkv_vals = product(act_one, qkv_full).astype(jnp.bfloat16)
        head_shape = (chip_count, vis_len, heads, HD)
        queries = qkv_vals[:, :D].reshape(head_shape)
        key_rows = qkv_vals[:, D : 2 * D].reshape(head_shape)
        value_rows = qkv_vals[:, 2 * D :].reshape(head_shape)
        mixture4, soft_full, soft_low = attend(queries, key_rows, value_rows)
        mixture = mixture4.reshape(row_count, D)
        res_one = residual + product(mixture, out_full)
        norm_out_two, normed_two, inverse_two = norm_forward(
            res_one, gain_two.astype(jnp.float32), shift_two.astype(jnp.float32)
        )
        act_two = norm_out_two.astype(jnp.bfloat16)
        hidden = product(act_two, inner_full) + inner_bias.astype(jnp.float32)
        active = gelu_value(hidden).astype(jnp.bfloat16)
        res_two = res_one + (product(active, outer_full) + outer_bias.astype(jnp.float32))
        enc_low = res_two.astype(jnp.bfloat16)
        projected = (product(enc_low, dec_full) + dec_shift.astype(jnp.float32)).astype(
            jnp.bfloat16
        )
        slot_ids = jnp.arange(L, dtype=jnp.int32)
        one_hot = (visible_slot[:, None, :] == slot_ids[None, :, None]).astype(jnp.bfloat16)
        filled_vis = jnp.einsum(
            "csi,cie->cse",
            one_hot,
            projected.reshape(chip_count, vis_len, DEC),
            preferred_element_type=jnp.float32,
        )
        has_row = jnp.sum(one_hot.astype(jnp.float32), axis=2, keepdims=True) > 0.5
        filled = jnp.where(has_row, filled_vis, mask_full.astype(jnp.float32)[None, None, :])
        filled = filled.astype(jnp.bfloat16)
        decoded = lax.all_to_all(filled, AX, split_axis=1, concat_axis=0, tiled=True)
        grad_full = lax.all_to_all(cot_decoded, AX, split_axis=0, concat_axis=1, tiled=True)

        grad_vis_low = (
            jnp.einsum("csi,cse->cie", one_hot, grad_full, preferred_element_type=jnp.float32)
            .astype(jnp.bfloat16)
            .reshape(row_count, DEC)
        )
        grad_vis = grad_vis_low.astype(jnp.float32)
        grad_mask_token = jnp.sum(
            jnp.where(has_row, 0.0, grad_full.astype(jnp.float32)), axis=(0, 1)
        )
        grad_dec_bias = jnp.sum(grad_vis, axis=0)
        grad_dec_weight = inner_rows(enc_low, grad_vis_low)
        grad_res_two = outer_cols(grad_vis_low, dec_full)
        grad_ffo = grad_res_two.astype(jnp.bfloat16)
        grad_mlp_out_bias = jnp.sum(grad_ffo.astype(jnp.float32), axis=0)
        grad_mlp_out = inner_rows(active, grad_ffo)
        grad_hidden = (outer_cols(grad_ffo, outer_full) * gelu_slope(hidden)).astype(jnp.bfloat16)
        grad_mlp_in_bias = jnp.sum(grad_hidden.astype(jnp.float32), axis=0)
        grad_mlp_in = inner_rows(act_two, grad_hidden)
        grad_act_two = outer_cols(grad_hidden, inner_full)
        grad_norm_two, grad_norm2_gain, grad_norm2_bias = norm_backward(
            grad_act_two, normed_two, inverse_two, gain_two.astype(jnp.float32)
        )
        grad_res_one = grad_res_two + grad_norm_two
        grad_att = grad_res_one.astype(jnp.bfloat16)
        grad_out_weight = inner_rows(mixture, grad_att)
        grad_mixed = outer_cols(grad_att, out_full).astype(jnp.bfloat16).reshape(head_shape)
        grad_queries, grad_keys, grad_values = attend_back(
            queries, key_rows, value_rows, soft_full, soft_low, grad_mixed
        )
        grad_qkv = jnp.concatenate(
            [
                grad_queries.reshape(row_count, D),
                grad_keys.reshape(row_count, D),
                grad_values.reshape(row_count, D),
            ],
            axis=1,
        ).astype(jnp.bfloat16)
        grad_qkv_weight = inner_rows(act_one, grad_qkv)
        grad_act_one = outer_cols(grad_qkv, qkv_full)
        grad_norm_one, grad_norm1_gain, grad_norm1_bias = norm_backward(
            grad_act_one, normed_one, inverse_one, gain_one.astype(jnp.float32)
        )
        grad_tokens = (grad_res_one + grad_norm_one).reshape(chip_count, vis_len, D)
        chip_sums = jnp.sum(grad_tokens, axis=1)
        grad_wave_table = lax.dot_general(
            counts, chip_sums, (((0,), (0,)), ((), ())), precision=HIGH_PRECISION
        )
        small_grads = (grad_wave_table, grad_norm1_gain, grad_norm1_bias, grad_norm2_gain,
                       grad_norm2_bias, grad_mlp_in_bias, grad_mlp_out_bias, grad_dec_bias,
                       grad_mask_token)
        packed_sg, sg_widths = pack_rows(small_grads, n_dev, jnp.float32)
        turn = lambda k: orders[k % len(orders)]
        reduced_sg = rs_chain(packed_sg, n_bits, orders[0])
        (sum_wave, sum_g1, sum_b1, sum_g2, sum_b2, sum_ib, sum_ob, sum_db,
         sum_mask) = unpack_rows(reduced_sg, small_grads, sg_widths, n_dev, 1)
        sum_dec = rs_chain(grad_dec_weight, n_bits, orders[0])
        sum_mlp_out = rs_chain(grad_mlp_out, n_bits, orders[0])
        sum_mlp_in = rs_chain(grad_mlp_in, n_bits, orders[0])
        sum_out = rs_chain(grad_out_weight, n_bits, orders[0])
        sum_qkv = rs_chain(grad_qkv_weight, n_bits, orders[0])
        summed = (sum_wave, sum_g1, sum_b1, sum_qkv, sum_out, sum_g2, sum_b2, sum_mlp_in,
                  sum_ib, sum_mlp_out, sum_ob, sum_dec, sum_db, sum_mask)
        return (decoded, grad_tokens, *summed)

    return local


def solution(mesh):
    n_dev = mesh.devices.size
    n_bits = n_dev.bit_length() - 1
    orders = halving_orders(*bit_groups(mesh))
    placed = (
        P(AX, None, None),
        P(AX, None),
        P(AX, None),
        P(AX, None),
        P(AX),
        P(AX),
        P(AX, None),
        P(AX, None),
        P(AX),
        P(AX),
        P(AX, None),
        P(AX),
        P(AX, None),
        P(AX),
        P(AX, None),
        P(AX),
        P(AX),
        P(None, AX, None),
    )
    return jax.shard_map(
        make_local(n_bits, orders),
        mesh=mesh,
        in_specs=placed,
        out_specs=(
            P(None, AX, None),
            P(AX, None, None),
            P(AX, None),
            P(AX),
            P(AX),
            P(AX, None),
            P(AX, None),
            P(AX),
            P(AX),
            P(AX, None),
            P(AX),
            P(AX, None),
            P(AX),
            P(AX, None),
            P(AX),
            P(AX),
        ),
        check_vma=False,
    )
```

```python
import jax
import jax.numpy as jnp
from jax import lax
from jax.sharding import PartitionSpec as P

D = 768
HD = 64
DEC = 512
WAVES = 128
L = 1024

NORM_EPSILON = 1e-05
ROOT_HALF = 0.7071067811865476
INVERSE_ROOT_TAU = 0.3989422804014327
HIGH_PRECISION = lax.Precision.HIGHEST
AX = ("dp", "fsdp")


def product(left_op, right_op):
    return jnp.dot(left_op, right_op, preferred_element_type=jnp.float32)


def inner_rows(left_op, right_op):
    return lax.dot_general(
        left_op, right_op, (((0,), (0,)), ((), ())), preferred_element_type=jnp.float32
    )


def outer_cols(left_op, right_op):
    return lax.dot_general(
        left_op, right_op, (((1,), (1,)), ((), ())), preferred_element_type=jnp.float32
    )


def norm_forward(residual, gain, shift):
    mean_val = jnp.mean(residual, axis=-1, keepdims=True)
    centered = residual - mean_val
    variance = jnp.mean(centered * centered, axis=-1, keepdims=True)
    inverse = lax.rsqrt(variance + NORM_EPSILON)
    normed = centered * inverse
    return (normed * gain + shift, normed, inverse)


def norm_backward(incoming, normed, inverse, gain):
    scaled = incoming * gain
    first_mean = jnp.mean(scaled, axis=-1, keepdims=True)
    second_mean = jnp.mean(scaled * normed, axis=-1, keepdims=True)
    grad_input = inverse * (scaled - first_mean - normed * second_mean)
    return (grad_input, jnp.sum(incoming * normed, axis=0), jnp.sum(incoming, axis=0))


def gelu_value(hidden):
    return 0.5 * hidden * (1.0 + lax.erf(hidden * ROOT_HALF))


def gelu_slope(hidden):
    return (
        0.5 * (1.0 + lax.erf(hidden * ROOT_HALF))
        + hidden * jnp.exp(-0.5 * hidden * hidden) * INVERSE_ROOT_TAU
    )


def bit_groups(mesh):
    flat = list(mesh.devices.reshape(-1))
    n_bits = len(flat).bit_length() - 1
    first = flat[0]
    core_bit = None
    groups = {}
    for bit in range(n_bits):
        other = flat[1 << bit]
        if other.core_on_chip != first.core_on_chip:
            core_bit = bit
            continue
        axis = [a for a in range(len(first.coords)) if first.coords[a] != other.coords[a]]
        groups.setdefault(axis[0] if axis else -1, []).append(bit)
    return core_bit, [sorted(bits) for _, bits in sorted(groups.items())]


def halving_orders(core_bit, groups):
    head = [] if core_bit is None else [core_bit]
    orders = []
    for turn in range(max(1, len(groups))):
        rest = []
        for i in range(len(groups)):
            rest.extend(groups[(i + turn) % len(groups)])
        orders.append(head + rest)
    if len(groups) >= 2:
        swapped = [groups[1], groups[0]] + groups[2:]
        orders.insert(0, head + [b for g in swapped for b in g])
    return orders


def rs_chain(grad, n_bits, order):
    n_dev = 2 ** n_bits
    me = lax.axis_index(AX)
    rows = grad.shape[0] // n_dev
    current = grad.reshape((2,) * n_bits + (rows,) + grad.shape[1:])
    for bit in order:
        axis = n_bits - 1 - bit
        mine = (me >> bit) & 1
        keep = lax.dynamic_slice_in_dim(current, mine, 1, axis=axis)
        send = lax.dynamic_slice_in_dim(current, 1 - mine, 1, axis=axis)
        moved = lax.ppermute(
            send.astype(jnp.bfloat16), AX, [(i, i ^ (1 << bit)) for i in range(n_dev)]
        )
        current = keep + moved.astype(jnp.float32)
    return current.reshape((rows,) + grad.shape[1:])


def pack_rows(arrays, n_dev, dtype):
    flat = [a.reshape(n_dev, -1).astype(dtype) for a in arrays]
    widths = [f.shape[1] for f in flat]
    padded = -sum(widths) % 1024
    flat.append(jnp.zeros((n_dev, padded), dtype))
    packed = jnp.concatenate(flat, axis=1)
    return packed.reshape(n_dev, 8, -1), widths


def unpack_rows(packed, arrays, widths, n_dev, leading):
    flat = packed.reshape(packed.shape[0], -1)
    out = []
    offset = 0
    for a, width in zip(arrays, widths):
        piece = flat[:, offset : offset + width]
        out.append(piece.reshape((leading * a.shape[0] // n_dev,) + a.shape[1:]))
        offset += width
    return out


def attend(queries, key_rows, value_rows):
    score_scale = HD ** (-0.5)
    scores = (
        jnp.einsum("cqhd,ckhd->chqk", queries, key_rows, preferred_element_type=jnp.float32)
        * score_scale
    )
    row_peak = jnp.max(scores, axis=-1, keepdims=True)
    exponents = jnp.exp(scores - row_peak)
    row_total = jnp.sum(exponents, axis=-1, keepdims=True)
    soft_full = exponents / row_total
    soft_low = soft_full.astype(jnp.bfloat16)
    mixture = jnp.einsum(
        "chqk,ckhd->cqhd", soft_low, value_rows, preferred_element_type=jnp.float32
    )
    return mixture.astype(jnp.bfloat16), soft_full, soft_low


def attend_back(queries, key_rows, value_rows, soft_full, soft_low, grad_mixture):
    score_scale = HD ** (-0.5)
    grad_values = jnp.einsum(
        "chqk,cqhd->ckhd", soft_low, grad_mixture, preferred_element_type=jnp.float32
    )
    grad_soft = jnp.einsum(
        "cqhd,ckhd->chqk", grad_mixture, value_rows, preferred_element_type=jnp.float32
    )
    row_delta = jnp.sum(grad_soft * soft_full, axis=-1, keepdims=True)
    grad_scores = (soft_full * (grad_soft - row_delta)).astype(jnp.bfloat16)
    grad_queries = (
        jnp.einsum("chqk,ckhd->cqhd", grad_scores, key_rows, preferred_element_type=jnp.float32)
        * score_scale
    )
    grad_keys = (
        jnp.einsum("chqk,cqhd->ckhd", grad_scores, queries, preferred_element_type=jnp.float32)
        * score_scale
    )
    return grad_queries, grad_keys, grad_values


def make_local(n_bits, orders):
    n_dev = 2 ** n_bits

    def local(
        tokens,
        band_waves,
        visible_slot,
        wave_table,
        norm1_gain,
        norm1_bias,
        qkv_weight,
        out_weight,
        norm2_gain,
        norm2_bias,
        mlp_in,
        mlp_in_bias,
        mlp_out,
        mlp_out_bias,
        dec_weight,
        dec_bias,
        mask_token,
        cot_decoded,
    ):
        small = (wave_table, norm1_gain, norm1_bias, norm2_gain, norm2_bias, mlp_in_bias,
                 mlp_out_bias, dec_bias, mask_token)
        small_flat = [a.reshape(-1) for a in small]
        small_widths = [f.shape[0] for f in small_flat]
        rows_here = qkv_weight.shape[0]
        small_cols = -(-sum(small_widths) // (rows_here * 128)) * 128
        small_pad = rows_here * small_cols - sum(small_widths)
        small_block = jnp.concatenate(
            small_flat + [jnp.zeros((small_pad,), jnp.bfloat16)]
        ).reshape(rows_here, small_cols)
        wide = (qkv_weight, out_weight, mlp_in, dec_weight, small_block)
        wide_cols = [a.shape[1] for a in wide]
        gathered_wide = lax.all_gather(jnp.concatenate(wide, axis=1), AX, axis=0, tiled=True)
        wide_full = []
        offset = 0
        for cols in wide_cols:
            wide_full.append(gathered_wide[:, offset : offset + cols])
            offset += cols
        qkv_full, out_full, inner_full, dec_full, small_full = wide_full
        small_rows = small_full.reshape(n_dev, rows_here * small_cols)
        small_parts = []
        offset = 0
        for a, width in zip(small, small_widths):
            piece = small_rows[:, offset : offset + width]
            small_parts.append(piece.reshape((n_dev * a.shape[0],) + a.shape[1:]))
            offset += width
        (wave_full, gain_one, shift_one, gain_two, shift_two, inner_bias, outer_bias,
         dec_shift, mask_full) = small_parts
        outer_full = lax.all_gather(mlp_out, AX, axis=0, tiled=True)

        chip_count, vis_len, feature_width = tokens.shape
        row_count = chip_count * vis_len
        heads = feature_width // HD
        counts = jnp.sum(
            (band_waves[:, :, None] == jnp.arange(WAVES, dtype=jnp.int32)[None, None, :]).astype(
                jnp.float32
            ),
            axis=1,
        )
        spectral = jnp.dot(
            counts.astype(jnp.bfloat16), wave_full, preferred_element_type=jnp.float32
        )
        residual = (tokens.astype(jnp.float32) + spectral[:, None, :]).reshape(row_count, D)
        norm_out_one, normed_one, inverse_one = norm_forward(
            residual, gain_one.astype(jnp.float32), shift_one.astype(jnp.float32)
        )
        act_one = norm_out_one.astype(jnp.bfloat16)
        qkv_vals = product(act_one, qkv_full).astype(jnp.bfloat16)
        head_shape = (chip_count, vis_len, heads, HD)
        queries = qkv_vals[:, :D].reshape(head_shape)
        key_rows = qkv_vals[:, D : 2 * D].reshape(head_shape)
        value_rows = qkv_vals[:, 2 * D :].reshape(head_shape)
        mixture4, soft_full, soft_low = attend(queries, key_rows, value_rows)
        mixture = mixture4.reshape(row_count, D)
        res_one = residual + product(mixture, out_full)
        norm_out_two, normed_two, inverse_two = norm_forward(
            res_one, gain_two.astype(jnp.float32), shift_two.astype(jnp.float32)
        )
        act_two = norm_out_two.astype(jnp.bfloat16)
        hidden = product(act_two, inner_full) + inner_bias.astype(jnp.float32)
        active = gelu_value(hidden).astype(jnp.bfloat16)
        res_two = res_one + (product(active, outer_full) + outer_bias.astype(jnp.float32))
        enc_low = res_two.astype(jnp.bfloat16)
        projected = (product(enc_low, dec_full) + dec_shift.astype(jnp.float32)).astype(
            jnp.bfloat16
        )
        slot_ids = jnp.arange(L, dtype=jnp.int32)
        one_hot = (visible_slot[:, None, :] == slot_ids[None, :, None]).astype(jnp.bfloat16)
        filled_vis = jnp.einsum(
            "csi,cie->cse",
            one_hot,
            projected.reshape(chip_count, vis_len, DEC),
            preferred_element_type=jnp.float32,
        )
        has_row = jnp.sum(one_hot.astype(jnp.float32), axis=2, keepdims=True) > 0.5
        filled = jnp.where(has_row, filled_vis, mask_full.astype(jnp.float32)[None, None, :])
        filled = filled.astype(jnp.bfloat16)
        decoded = lax.all_to_all(filled, AX, split_axis=1, concat_axis=0, tiled=True)
        grad_full = lax.all_to_all(cot_decoded, AX, split_axis=0, concat_axis=1, tiled=True)

        grad_vis_low = (
            jnp.einsum("csi,cse->cie", one_hot, grad_full, preferred_element_type=jnp.float32)
            .astype(jnp.bfloat16)
            .reshape(row_count, DEC)
        )
        grad_vis = grad_vis_low.astype(jnp.float32)
        grad_mask_token = jnp.sum(
            jnp.where(has_row, 0.0, grad_full.astype(jnp.float32)), axis=(0, 1)
        )
        grad_dec_bias = jnp.sum(grad_vis, axis=0)
        grad_dec_weight = inner_rows(enc_low, grad_vis_low)
        sum_dec = rs_chain(grad_dec_weight, n_bits, orders[0])
        grad_res_two = outer_cols(grad_vis_low, dec_full)
        grad_ffo = grad_res_two.astype(jnp.bfloat16)
        grad_mlp_out_bias = jnp.sum(grad_ffo.astype(jnp.float32), axis=0)
        grad_mlp_out = inner_rows(active, grad_ffo)
        sum_mlp_out = rs_chain(grad_mlp_out, n_bits, orders[0])
        grad_hidden = (outer_cols(grad_ffo, outer_full) * gelu_slope(hidden)).astype(jnp.bfloat16)
        grad_mlp_in_bias = jnp.sum(grad_hidden.astype(jnp.float32), axis=0)
        grad_mlp_in = inner_rows(act_two, grad_hidden)
        sum_mlp_in = rs_chain(grad_mlp_in, n_bits, orders[0])
        grad_act_two = outer_cols(grad_hidden, inner_full)
        grad_norm_two, grad_norm2_gain, grad_norm2_bias = norm_backward(
            grad_act_two, normed_two, inverse_two, gain_two.astype(jnp.float32)
        )
        grad_res_one = grad_res_two + grad_norm_two
        grad_att = grad_res_one.astype(jnp.bfloat16)
        grad_out_weight = inner_rows(mixture, grad_att)
        sum_out = rs_chain(grad_out_weight, n_bits, orders[0])
        grad_mixed = outer_cols(grad_att, out_full).astype(jnp.bfloat16).reshape(head_shape)
        grad_queries, grad_keys, grad_values = attend_back(
            queries, key_rows, value_rows, soft_full, soft_low, grad_mixed
        )
        grad_qkv = jnp.concatenate(
            [
                grad_queries.reshape(row_count, D),
                grad_keys.reshape(row_count, D),
                grad_values.reshape(row_count, D),
            ],
            axis=1,
        ).astype(jnp.bfloat16)
        grad_qkv_weight = inner_rows(act_one, grad_qkv)
        sum_qkv = rs_chain(grad_qkv_weight, n_bits, orders[0])
        grad_act_one = outer_cols(grad_qkv, qkv_full)
        grad_norm_one, grad_norm1_gain, grad_norm1_bias = norm_backward(
            grad_act_one, normed_one, inverse_one, gain_one.astype(jnp.float32)
        )
        grad_tokens = (grad_res_one + grad_norm_one).reshape(chip_count, vis_len, D)
        chip_sums = jnp.sum(grad_tokens, axis=1)
        grad_wave_table = lax.dot_general(
            counts, chip_sums, (((0,), (0,)), ((), ())), precision=HIGH_PRECISION
        )
        small_grads = (grad_wave_table, grad_norm1_gain, grad_norm1_bias, grad_norm2_gain,
                       grad_norm2_bias, grad_mlp_in_bias, grad_mlp_out_bias, grad_dec_bias,
                       grad_mask_token)
        packed_sg, sg_widths = pack_rows(small_grads, n_dev, jnp.float32)
        reduced_sg = rs_chain(packed_sg, n_bits, orders[0])
        (sum_wave, sum_g1, sum_b1, sum_g2, sum_b2, sum_ib, sum_ob, sum_db,
         sum_mask) = unpack_rows(reduced_sg, small_grads, sg_widths, n_dev, 1)
        summed = (sum_wave, sum_g1, sum_b1, sum_qkv, sum_out, sum_g2, sum_b2, sum_mlp_in,
                  sum_ib, sum_mlp_out, sum_ob, sum_dec, sum_db, sum_mask)
        return (decoded, grad_tokens, *summed)

    return local


def solution(mesh):
    n_dev = mesh.devices.size
    n_bits = n_dev.bit_length() - 1
    orders = halving_orders(*bit_groups(mesh))
    placed = (
        P(AX, None, None),
        P(AX, None),
        P(AX, None),
        P(AX, None),
        P(AX),
        P(AX),
        P(AX, None),
        P(AX, None),
        P(AX),
        P(AX),
        P(AX, None),
        P(AX),
        P(AX, None),
        P(AX),
        P(AX, None),
        P(AX),
        P(AX),
        P(None, AX, None),
    )
    body = make_local(n_bits, orders)

    return jax.shard_map(
        body,
        mesh=mesh,
        in_specs=placed,
        out_specs=(
            P(None, AX, None),
            P(AX, None, None),
            P(AX, None),
            P(AX),
            P(AX),
            P(AX, None),
            P(AX, None),
            P(AX),
            P(AX),
            P(AX, None),
            P(AX),
            P(AX, None),
            P(AX),
            P(AX, None),
            P(AX),
            P(AX),
        ),
        check_vma=False,
    )
```

```python
import numpy as np
import jax
import jax.numpy as jnp
from jax import lax
from jax.sharding import PartitionSpec as P

D = 768
HD = 64
DEC = 512
WAVES = 128
L = 1024

NORM_EPSILON = 1e-05
ROOT_HALF = 0.7071067811865476
INVERSE_ROOT_TAU = 0.3989422804014327
HIGH_PRECISION = lax.Precision.HIGHEST
AX = ("dp", "fsdp")


def product(left_op, right_op):
    return jnp.dot(left_op, right_op, preferred_element_type=jnp.float32)


def inner_rows(left_op, right_op):
    return lax.dot_general(
        left_op, right_op, (((0,), (0,)), ((), ())), preferred_element_type=jnp.float32
    )


def outer_cols(left_op, right_op):
    return lax.dot_general(
        left_op, right_op, (((1,), (1,)), ((), ())), preferred_element_type=jnp.float32
    )


def norm_forward(residual, gain, shift):
    mean_val = jnp.mean(residual, axis=-1, keepdims=True)
    centered = residual - mean_val
    variance = jnp.mean(centered * centered, axis=-1, keepdims=True)
    inverse = lax.rsqrt(variance + NORM_EPSILON)
    normed = centered * inverse
    return (normed * gain + shift, normed, inverse)


def norm_backward(incoming, normed, inverse, gain):
    scaled = incoming * gain
    first_mean = jnp.mean(scaled, axis=-1, keepdims=True)
    second_mean = jnp.mean(scaled * normed, axis=-1, keepdims=True)
    grad_input = inverse * (scaled - first_mean - normed * second_mean)
    return (grad_input, jnp.sum(incoming * normed, axis=0), jnp.sum(incoming, axis=0))


def gelu_value(hidden):
    return 0.5 * hidden * (1.0 + lax.erf(hidden * ROOT_HALF))


def gelu_slope(hidden):
    return (
        0.5 * (1.0 + lax.erf(hidden * ROOT_HALF))
        + hidden * jnp.exp(-0.5 * hidden * hidden) * INVERSE_ROOT_TAU
    )


def core_bit_of(mesh):
    flat = list(mesh.devices.reshape(-1))
    cores = [d.core_on_chip for d in flat]
    stride = 1
    while stride < len(flat) and cores[stride] == cores[0]:
        stride *= 2
    return stride.bit_length() - 1


def halving_order(n_bits, core_bit):
    rest = [b for b in reversed(range(n_bits)) if b != core_bit]
    if len(rest) >= 2:
        rest[-2:] = rest[-2:][::-1]
    return [core_bit] + rest


def rs_chain(grad, n_bits, order):
    n_dev = 2 ** n_bits
    me = lax.axis_index(AX)
    rows = grad.shape[0] // n_dev
    current = grad.reshape((2,) * n_bits + (rows,) + grad.shape[1:])
    for bit in order:
        axis = n_bits - 1 - bit
        mine = (me >> bit) & 1
        keep = lax.dynamic_slice_in_dim(current, mine, 1, axis=axis)
        send = lax.dynamic_slice_in_dim(current, 1 - mine, 1, axis=axis)
        moved = lax.ppermute(
            send.astype(jnp.bfloat16), AX, [(i, i ^ (1 << bit)) for i in range(n_dev)]
        )
        current = keep + moved.astype(jnp.float32)
    return current.reshape((rows,) + grad.shape[1:])


def pack_rows(arrays, n_dev, dtype):
    flat = [a.reshape(n_dev, -1).astype(dtype) for a in arrays]
    widths = [f.shape[1] for f in flat]
    padded = -sum(widths) % 1024
    flat.append(jnp.zeros((n_dev, padded), dtype))
    packed = jnp.concatenate(flat, axis=1)
    return packed.reshape(n_dev, 8, -1), widths


def unpack_rows(packed, arrays, widths, n_dev, leading):
    flat = packed.reshape(packed.shape[0], -1)
    out = []
    offset = 0
    for a, width in zip(arrays, widths):
        piece = flat[:, offset : offset + width]
        out.append(piece.reshape((leading * a.shape[0] // n_dev,) + a.shape[1:]))
        offset += width
    return out


def attend(queries, key_rows, value_rows):
    score_scale = HD ** (-0.5)
    scores = (
        jnp.einsum("cqhd,ckhd->chqk", queries, key_rows, preferred_element_type=jnp.float32)
        * score_scale
    )
    row_peak = jnp.max(scores, axis=-1, keepdims=True)
    exponents = jnp.exp(scores - row_peak)
    row_total = jnp.sum(exponents, axis=-1, keepdims=True)
    soft_full = exponents / row_total
    soft_low = soft_full.astype(jnp.bfloat16)
    mixture = jnp.einsum(
        "chqk,ckhd->cqhd", soft_low, value_rows, preferred_element_type=jnp.float32
    )
    return mixture.astype(jnp.bfloat16), soft_full, soft_low


def attend_back(queries, key_rows, value_rows, soft_full, soft_low, grad_mixture):
    score_scale = HD ** (-0.5)
    grad_values = jnp.einsum(
        "chqk,cqhd->ckhd", soft_low, grad_mixture, preferred_element_type=jnp.float32
    )
    grad_soft = jnp.einsum(
        "cqhd,ckhd->chqk", grad_mixture, value_rows, preferred_element_type=jnp.float32
    )
    row_delta = jnp.sum(grad_soft * soft_full, axis=-1, keepdims=True)
    grad_scores = (soft_full * (grad_soft - row_delta)).astype(jnp.bfloat16)
    grad_queries = (
        jnp.einsum("chqk,ckhd->cqhd", grad_scores, key_rows, preferred_element_type=jnp.float32)
        * score_scale
    )
    grad_keys = (
        jnp.einsum("chqk,cqhd->ckhd", grad_scores, queries, preferred_element_type=jnp.float32)
        * score_scale
    )
    return grad_queries, grad_keys, grad_values


def make_local(n_bits, order):
    n_dev = 2 ** n_bits

    def local(
        tokens,
        band_waves,
        visible_slot,
        wave_table,
        norm1_gain,
        norm1_bias,
        qkv_weight,
        out_weight,
        norm2_gain,
        norm2_bias,
        mlp_in,
        mlp_in_bias,
        mlp_out,
        mlp_out_bias,
        dec_weight,
        dec_bias,
        mask_token,
        cot_decoded,
    ):
        shards = (
            wave_table,
            norm1_gain,
            norm1_bias,
            qkv_weight,
            out_weight,
            norm2_gain,
            norm2_bias,
            mlp_in,
            mlp_in_bias,
            mlp_out,
            mlp_out_bias,
            dec_weight,
            dec_bias,
            mask_token,
        )
        small = (wave_table, norm1_gain, norm1_bias, norm2_gain, norm2_bias, mlp_in_bias,
                 mlp_out_bias, dec_bias, mask_token)
        packed_small, small_widths = pack_rows(
            [a.reshape(1, -1) for a in small], 1, jnp.bfloat16
        )
        gathered_small = lax.all_gather(packed_small, AX, axis=0, tiled=True)
        (wave_full, gain_one, shift_one, gain_two, shift_two, inner_bias, outer_bias,
         dec_shift, mask_full) = unpack_rows(gathered_small, small, small_widths, 1, n_dev)
        wide = (qkv_weight, out_weight, mlp_in, dec_weight)
        wide_cols = [a.shape[1] for a in wide]
        gathered_wide = lax.all_gather(jnp.concatenate(wide, axis=1), AX, axis=0, tiled=True)
        wide_full = []
        offset = 0
        for cols in wide_cols:
            wide_full.append(gathered_wide[:, offset : offset + cols])
            offset += cols
        qkv_full, out_full, inner_full, dec_full = wide_full
        outer_full = lax.all_gather(mlp_out, AX, axis=0, tiled=True)

        chip_count, vis_len, feature_width = tokens.shape
        row_count = chip_count * vis_len
        heads = feature_width // HD
        counts = jnp.sum(
            (band_waves[:, :, None] == jnp.arange(WAVES, dtype=jnp.int32)[None, None, :]).astype(
                jnp.float32
            ),
            axis=1,
        )
        spectral = jnp.dot(
            counts.astype(jnp.bfloat16), wave_full, preferred_element_type=jnp.float32
        )
        residual = (tokens.astype(jnp.float32) + spectral[:, None, :]).reshape(row_count, D)
        norm_out_one, normed_one, inverse_one = norm_forward(
            residual, gain_one.astype(jnp.float32), shift_one.astype(jnp.float32)
        )
        act_one = norm_out_one.astype(jnp.bfloat16)
        qkv_vals = product(act_one, qkv_full).astype(jnp.bfloat16)
        head_shape = (chip_count, vis_len, heads, HD)
        queries = qkv_vals[:, :D].reshape(head_shape)
        key_rows = qkv_vals[:, D : 2 * D].reshape(head_shape)
        value_rows = qkv_vals[:, 2 * D :].reshape(head_shape)
        mixture4, soft_full, soft_low = attend(queries, key_rows, value_rows)
        mixture = mixture4.reshape(row_count, D)
        res_one = residual + product(mixture, out_full)
        norm_out_two, normed_two, inverse_two = norm_forward(
            res_one, gain_two.astype(jnp.float32), shift_two.astype(jnp.float32)
        )
        act_two = norm_out_two.astype(jnp.bfloat16)
        hidden = product(act_two, inner_full) + inner_bias.astype(jnp.float32)
        active = gelu_value(hidden).astype(jnp.bfloat16)
        res_two = res_one + (product(active, outer_full) + outer_bias.astype(jnp.float32))
        enc_low = res_two.astype(jnp.bfloat16)
        projected = (product(enc_low, dec_full) + dec_shift.astype(jnp.float32)).astype(
            jnp.bfloat16
        )
        slot_ids = jnp.arange(L, dtype=jnp.int32)
        one_hot = (visible_slot[:, None, :] == slot_ids[None, :, None]).astype(jnp.bfloat16)
        filled_vis = jnp.einsum(
            "csi,cie->cse",
            one_hot,
            projected.reshape(chip_count, vis_len, DEC),
            preferred_element_type=jnp.float32,
        )
        has_row = jnp.sum(one_hot.astype(jnp.float32), axis=2, keepdims=True) > 0.5
        filled = jnp.where(has_row, filled_vis, mask_full.astype(jnp.float32)[None, None, :])
        filled = filled.astype(jnp.bfloat16)
        decoded = lax.all_to_all(filled, AX, split_axis=1, concat_axis=0, tiled=True)
        grad_full = lax.all_to_all(cot_decoded, AX, split_axis=0, concat_axis=1, tiled=True)

        grad_vis_low = (
            jnp.einsum("csi,cse->cie", one_hot, grad_full, preferred_element_type=jnp.float32)
            .astype(jnp.bfloat16)
            .reshape(row_count, DEC)
        )
        grad_vis = grad_vis_low.astype(jnp.float32)
        grad_mask_token = jnp.sum(
            jnp.where(has_row, 0.0, grad_full.astype(jnp.float32)), axis=(0, 1)
        )
        grad_dec_bias = jnp.sum(grad_vis, axis=0)
        grad_dec_weight = inner_rows(enc_low, grad_vis_low)
        grad_res_two = outer_cols(grad_vis_low, dec_full)
        grad_ffo = grad_res_two.astype(jnp.bfloat16)
        grad_mlp_out_bias = jnp.sum(grad_ffo.astype(jnp.float32), axis=0)
        grad_mlp_out = inner_rows(active, grad_ffo)
        grad_hidden = (outer_cols(grad_ffo, outer_full) * gelu_slope(hidden)).astype(jnp.bfloat16)
        grad_mlp_in_bias = jnp.sum(grad_hidden.astype(jnp.float32), axis=0)
        grad_mlp_in = inner_rows(act_two, grad_hidden)
        grad_act_two = outer_cols(grad_hidden, inner_full)
        grad_norm_two, grad_norm2_gain, grad_norm2_bias = norm_backward(
            grad_act_two, normed_two, inverse_two, gain_two.astype(jnp.float32)
        )
        grad_res_one = grad_res_two + grad_norm_two
        grad_att = grad_res_one.astype(jnp.bfloat16)
        grad_out_weight = inner_rows(mixture, grad_att)
        grad_mixed = outer_cols(grad_att, out_full).astype(jnp.bfloat16).reshape(head_shape)
        grad_queries, grad_keys, grad_values = attend_back(
            queries, key_rows, value_rows, soft_full, soft_low, grad_mixed
        )
        grad_qkv = jnp.concatenate(
            [
                grad_queries.reshape(row_count, D),
                grad_keys.reshape(row_count, D),
                grad_values.reshape(row_count, D),
            ],
            axis=1,
        ).astype(jnp.bfloat16)
        grad_qkv_weight = inner_rows(act_one, grad_qkv)
        grad_act_one = outer_cols(grad_qkv, qkv_full)
        grad_norm_one, grad_norm1_gain, grad_norm1_bias = norm_backward(
            grad_act_one, normed_one, inverse_one, gain_one.astype(jnp.float32)
        )
        grad_tokens = (grad_res_one + grad_norm_one).reshape(chip_count, vis_len, D)
        chip_sums = jnp.sum(grad_tokens, axis=1)
        grad_wave_table = lax.dot_general(
            counts, chip_sums, (((0,), (0,)), ((), ())), precision=HIGH_PRECISION
        )
        small_grads = (grad_wave_table, grad_norm1_gain, grad_norm1_bias, grad_norm2_gain,
                       grad_norm2_bias, grad_mlp_in_bias, grad_mlp_out_bias, grad_dec_bias,
                       grad_mask_token)
        packed_sg, sg_widths = pack_rows(small_grads, n_dev, jnp.float32)
        reduced_sg = rs_chain(packed_sg, n_bits, order)
        (sum_wave, sum_g1, sum_b1, sum_g2, sum_b2, sum_ib, sum_ob, sum_db,
         sum_mask) = unpack_rows(reduced_sg, small_grads, sg_widths, n_dev, 1)
        sum_dec = rs_chain(grad_dec_weight, n_bits, order)
        sum_mlp_out = lax.psum_scatter(grad_mlp_out, AX, scatter_dimension=0, tiled=True)
        sum_mlp_in = rs_chain(grad_mlp_in, n_bits, order)
        sum_out = rs_chain(grad_out_weight, n_bits, order)
        sum_qkv = rs_chain(grad_qkv_weight, n_bits, order)
        summed = (sum_wave, sum_g1, sum_b1, sum_qkv, sum_out, sum_g2, sum_b2, sum_mlp_in,
                  sum_ib, sum_mlp_out, sum_ob, sum_dec, sum_db, sum_mask)
        return (decoded, grad_tokens, *summed)

    return local


def solution(mesh):
    n_dev = mesh.devices.size
    n_bits = n_dev.bit_length() - 1
    order = halving_order(n_bits, core_bit_of(mesh))
    placed = (
        P(AX, None, None),
        P(AX, None),
        P(AX, None),
        P(AX, None),
        P(AX),
        P(AX),
        P(AX, None),
        P(AX, None),
        P(AX),
        P(AX),
        P(AX, None),
        P(AX),
        P(AX, None),
        P(AX),
        P(AX, None),
        P(AX),
        P(AX),
        P(None, AX, None),
    )
    return jax.shard_map(
        make_local(n_bits, order),
        mesh=mesh,
        in_specs=placed,
        out_specs=(
            P(None, AX, None),
            P(AX, None, None),
            P(AX, None),
            P(AX),
            P(AX),
            P(AX, None),
            P(AX, None),
            P(AX),
            P(AX),
            P(AX, None),
            P(AX),
            P(AX, None),
            P(AX),
            P(AX, None),
            P(AX),
            P(AX),
        ),
        check_vma=False,
    )
```

```python
import numpy as np
import jax
import jax.numpy as jnp
from jax import lax
from jax.sharding import PartitionSpec as P

D = 768
HD = 64
DEC = 512
WAVES = 128
L = 1024

NORM_EPSILON = 1e-05
ROOT_HALF = 0.7071067811865476
INVERSE_ROOT_TAU = 0.3989422804014327
HIGH_PRECISION = lax.Precision.HIGHEST
AX = ("dp", "fsdp")


def product(left_op, right_op):
    return jnp.dot(left_op, right_op, preferred_element_type=jnp.float32)


def inner_rows(left_op, right_op):
    return lax.dot_general(
        left_op, right_op, (((0,), (0,)), ((), ())), preferred_element_type=jnp.float32
    )


def outer_cols(left_op, right_op):
    return lax.dot_general(
        left_op, right_op, (((1,), (1,)), ((), ())), preferred_element_type=jnp.float32
    )


def norm_forward(residual, gain, shift):
    mean_val = jnp.mean(residual, axis=-1, keepdims=True)
    centered = residual - mean_val
    variance = jnp.mean(centered * centered, axis=-1, keepdims=True)
    inverse = lax.rsqrt(variance + NORM_EPSILON)
    normed = centered * inverse
    return (normed * gain + shift, normed, inverse)


def norm_backward(incoming, normed, inverse, gain):
    scaled = incoming * gain
    first_mean = jnp.mean(scaled, axis=-1, keepdims=True)
    second_mean = jnp.mean(scaled * normed, axis=-1, keepdims=True)
    grad_input = inverse * (scaled - first_mean - normed * second_mean)
    return (grad_input, jnp.sum(incoming * normed, axis=0), jnp.sum(incoming, axis=0))


def gelu_value(hidden):
    return 0.5 * hidden * (1.0 + lax.erf(hidden * ROOT_HALF))


def gelu_slope(hidden):
    return (
        0.5 * (1.0 + lax.erf(hidden * ROOT_HALF))
        + hidden * jnp.exp(-0.5 * hidden * hidden) * INVERSE_ROOT_TAU
    )


def core_bit_of(mesh):
    flat = list(mesh.devices.reshape(-1))
    cores = [d.core_on_chip for d in flat]
    stride = 1
    while stride < len(flat) and cores[stride] == cores[0]:
        stride *= 2
    return stride.bit_length() - 1


def halving_order(n_bits, core_bit):
    rest = [b for b in reversed(range(n_bits)) if b != core_bit]
    if len(rest) >= 2:
        rest[-2:] = rest[-2:][::-1]
    return [core_bit] + rest


def rs_chain(grad, n_bits, order):
    n_dev = 2 ** n_bits
    me = lax.axis_index(AX)
    rows = grad.shape[0] // n_dev
    current = grad.reshape((2,) * n_bits + (rows,) + grad.shape[1:])
    for bit in order:
        axis = n_bits - 1 - bit
        mine = (me >> bit) & 1
        keep = lax.dynamic_slice_in_dim(current, mine, 1, axis=axis)
        send = lax.dynamic_slice_in_dim(current, 1 - mine, 1, axis=axis)
        moved = lax.ppermute(
            send.astype(jnp.bfloat16), AX, [(i, i ^ (1 << bit)) for i in range(n_dev)]
        )
        current = keep + moved.astype(jnp.float32)
    return current.reshape((rows,) + grad.shape[1:])


def pack_rows(arrays, n_dev, dtype):
    flat = [a.reshape(n_dev, -1).astype(dtype) for a in arrays]
    widths = [f.shape[1] for f in flat]
    padded = -sum(widths) % 1024
    flat.append(jnp.zeros((n_dev, padded), dtype))
    packed = jnp.concatenate(flat, axis=1)
    return packed.reshape(n_dev, 8, -1), widths


def unpack_rows(packed, arrays, widths, n_dev, leading):
    flat = packed.reshape(packed.shape[0], -1)
    out = []
    offset = 0
    for a, width in zip(arrays, widths):
        piece = flat[:, offset : offset + width]
        out.append(piece.reshape((leading * a.shape[0] // n_dev,) + a.shape[1:]))
        offset += width
    return out


def attend(queries, key_rows, value_rows):
    score_scale = HD ** (-0.5)
    scores = (
        jnp.einsum("cqhd,ckhd->chqk", queries, key_rows, preferred_element_type=jnp.float32)
        * score_scale
    )
    row_peak = jnp.max(scores, axis=-1, keepdims=True)
    exponents = jnp.exp(scores - row_peak)
    row_total = jnp.sum(exponents, axis=-1, keepdims=True)
    soft_full = exponents / row_total
    soft_low = soft_full.astype(jnp.bfloat16)
    mixture = jnp.einsum(
        "chqk,ckhd->cqhd", soft_low, value_rows, preferred_element_type=jnp.float32
    )
    return mixture.astype(jnp.bfloat16), soft_full, soft_low


def attend_back(queries, key_rows, value_rows, soft_full, soft_low, grad_mixture):
    score_scale = HD ** (-0.5)
    grad_values = jnp.einsum(
        "chqk,cqhd->ckhd", soft_low, grad_mixture, preferred_element_type=jnp.float32
    )
    grad_soft = jnp.einsum(
        "cqhd,ckhd->chqk", grad_mixture, value_rows, preferred_element_type=jnp.float32
    )
    row_delta = jnp.sum(grad_soft * soft_full, axis=-1, keepdims=True)
    grad_scores = (soft_full * (grad_soft - row_delta)).astype(jnp.bfloat16)
    grad_queries = (
        jnp.einsum("chqk,ckhd->cqhd", grad_scores, key_rows, preferred_element_type=jnp.float32)
        * score_scale
    )
    grad_keys = (
        jnp.einsum("chqk,cqhd->ckhd", grad_scores, queries, preferred_element_type=jnp.float32)
        * score_scale
    )
    return grad_queries, grad_keys, grad_values


def make_local(n_bits, order):
    n_dev = 2 ** n_bits

    def local(
        tokens,
        band_waves,
        visible_slot,
        wave_table,
        norm1_gain,
        norm1_bias,
        qkv_weight,
        out_weight,
        norm2_gain,
        norm2_bias,
        mlp_in,
        mlp_in_bias,
        mlp_out,
        mlp_out_bias,
        dec_weight,
        dec_bias,
        mask_token,
        cot_decoded,
    ):
        shards = (
            wave_table,
            norm1_gain,
            norm1_bias,
            qkv_weight,
            out_weight,
            norm2_gain,
            norm2_bias,
            mlp_in,
            mlp_in_bias,
            mlp_out,
            mlp_out_bias,
            dec_weight,
            dec_bias,
            mask_token,
        )
        small = (wave_table, norm1_gain, norm1_bias, norm2_gain, norm2_bias, mlp_in_bias,
                 mlp_out_bias, dec_bias, mask_token)
        packed_small, small_widths = pack_rows(
            [a.reshape(1, -1) for a in small], 1, jnp.bfloat16
        )
        gathered_small = lax.all_gather(packed_small, AX, axis=0, tiled=True)
        (wave_full, gain_one, shift_one, gain_two, shift_two, inner_bias, outer_bias,
         dec_shift, mask_full) = unpack_rows(gathered_small, small, small_widths, 1, n_dev)
        wide = (qkv_weight, out_weight, mlp_in, dec_weight)
        wide_cols = [a.shape[1] for a in wide]
        gathered_wide = lax.all_gather(jnp.concatenate(wide, axis=1), AX, axis=0, tiled=True)
        wide_full = []
        offset = 0
        for cols in wide_cols:
            wide_full.append(gathered_wide[:, offset : offset + cols])
            offset += cols
        qkv_full, out_full, inner_full, dec_full = wide_full
        outer_full = lax.all_gather(mlp_out, AX, axis=0, tiled=True)

        chip_count, vis_len, feature_width = tokens.shape
        row_count = chip_count * vis_len
        heads = feature_width // HD
        counts = jnp.sum(
            (band_waves[:, :, None] == jnp.arange(WAVES, dtype=jnp.int32)[None, None, :]).astype(
                jnp.float32
            ),
            axis=1,
        )
        spectral = jnp.dot(
            counts.astype(jnp.bfloat16), wave_full, preferred_element_type=jnp.float32
        )
        residual = (tokens.astype(jnp.float32) + spectral[:, None, :]).reshape(row_count, D)
        norm_out_one, normed_one, inverse_one = norm_forward(
            residual, gain_one.astype(jnp.float32), shift_one.astype(jnp.float32)
        )
        act_one = norm_out_one.astype(jnp.bfloat16)
        qkv_vals = product(act_one, qkv_full).astype(jnp.bfloat16)
        head_shape = (chip_count, vis_len, heads, HD)
        queries = qkv_vals[:, :D].reshape(head_shape)
        key_rows = qkv_vals[:, D : 2 * D].reshape(head_shape)
        value_rows = qkv_vals[:, 2 * D :].reshape(head_shape)
        mixture4, soft_full, soft_low = attend(queries, key_rows, value_rows)
        mixture = mixture4.reshape(row_count, D)
        res_one = residual + product(mixture, out_full)
        norm_out_two, normed_two, inverse_two = norm_forward(
            res_one, gain_two.astype(jnp.float32), shift_two.astype(jnp.float32)
        )
        act_two = norm_out_two.astype(jnp.bfloat16)
        hidden = product(act_two, inner_full) + inner_bias.astype(jnp.float32)
        active = gelu_value(hidden).astype(jnp.bfloat16)
        res_two = res_one + (product(active, outer_full) + outer_bias.astype(jnp.float32))
        enc_low = res_two.astype(jnp.bfloat16)
        projected = (product(enc_low, dec_full) + dec_shift.astype(jnp.float32)).astype(
            jnp.bfloat16
        )
        slot_ids = jnp.arange(L, dtype=jnp.int32)
        one_hot = (visible_slot[:, None, :] == slot_ids[None, :, None]).astype(jnp.bfloat16)
        filled_vis = jnp.einsum(
            "csi,cie->cse",
            one_hot,
            projected.reshape(chip_count, vis_len, DEC),
            preferred_element_type=jnp.float32,
        )
        has_row = jnp.sum(one_hot.astype(jnp.float32), axis=2, keepdims=True) > 0.5
        filled = jnp.where(has_row, filled_vis, mask_full.astype(jnp.float32)[None, None, :])
        filled = filled.astype(jnp.bfloat16)
        decoded = lax.all_to_all(filled, AX, split_axis=1, concat_axis=0, tiled=True)
        grad_full = lax.all_to_all(cot_decoded, AX, split_axis=0, concat_axis=1, tiled=True)

        grad_vis_low = (
            jnp.einsum("csi,cse->cie", one_hot, grad_full, preferred_element_type=jnp.float32)
            .astype(jnp.bfloat16)
            .reshape(row_count, DEC)
        )
        grad_vis = grad_vis_low.astype(jnp.float32)
        grad_mask_token = jnp.sum(
            jnp.where(has_row, 0.0, grad_full.astype(jnp.float32)), axis=(0, 1)
        )
        grad_dec_bias = jnp.sum(grad_vis, axis=0)
        grad_dec_weight = inner_rows(enc_low, grad_vis_low)
        grad_res_two = outer_cols(grad_vis_low, dec_full)
        grad_ffo = grad_res_two.astype(jnp.bfloat16)
        grad_mlp_out_bias = jnp.sum(grad_ffo.astype(jnp.float32), axis=0)
        grad_mlp_out = inner_rows(active, grad_ffo)
        grad_ffo, grad_mlp_out = lax.optimization_barrier((grad_ffo, grad_mlp_out))
        sum_mlp_out = lax.psum_scatter(grad_mlp_out, AX, scatter_dimension=0, tiled=True)
        grad_hidden = (outer_cols(grad_ffo, outer_full) * gelu_slope(hidden)).astype(jnp.bfloat16)
        grad_mlp_in_bias = jnp.sum(grad_hidden.astype(jnp.float32), axis=0)
        grad_mlp_in = inner_rows(act_two, grad_hidden)
        grad_act_two = outer_cols(grad_hidden, inner_full)
        grad_norm_two, grad_norm2_gain, grad_norm2_bias = norm_backward(
            grad_act_two, normed_two, inverse_two, gain_two.astype(jnp.float32)
        )
        grad_res_one = grad_res_two + grad_norm_two
        grad_att = grad_res_one.astype(jnp.bfloat16)
        grad_out_weight = inner_rows(mixture, grad_att)
        grad_mixed = outer_cols(grad_att, out_full).astype(jnp.bfloat16).reshape(head_shape)
        grad_queries, grad_keys, grad_values = attend_back(
            queries, key_rows, value_rows, soft_full, soft_low, grad_mixed
        )
        grad_qkv = jnp.concatenate(
            [
                grad_queries.reshape(row_count, D),
                grad_keys.reshape(row_count, D),
                grad_values.reshape(row_count, D),
            ],
            axis=1,
        ).astype(jnp.bfloat16)
        grad_qkv_weight = inner_rows(act_one, grad_qkv)
        grad_act_one = outer_cols(grad_qkv, qkv_full)
        grad_norm_one, grad_norm1_gain, grad_norm1_bias = norm_backward(
            grad_act_one, normed_one, inverse_one, gain_one.astype(jnp.float32)
        )
        grad_tokens = (grad_res_one + grad_norm_one).reshape(chip_count, vis_len, D)
        chip_sums = jnp.sum(grad_tokens, axis=1)
        grad_wave_table = lax.dot_general(
            counts, chip_sums, (((0,), (0,)), ((), ())), precision=HIGH_PRECISION
        )
        small_grads = (grad_wave_table, grad_norm1_gain, grad_norm1_bias, grad_norm2_gain,
                       grad_norm2_bias, grad_mlp_in_bias, grad_mlp_out_bias, grad_dec_bias,
                       grad_mask_token)
        packed_sg, sg_widths = pack_rows(small_grads, n_dev, jnp.float32)
        reduced_sg = rs_chain(packed_sg, n_bits, order)
        (sum_wave, sum_g1, sum_b1, sum_g2, sum_b2, sum_ib, sum_ob, sum_db,
         sum_mask) = unpack_rows(reduced_sg, small_grads, sg_widths, n_dev, 1)
        sum_dec = rs_chain(grad_dec_weight, n_bits, order)
        sum_mlp_in = rs_chain(grad_mlp_in, n_bits, order)
        sum_out = rs_chain(grad_out_weight, n_bits, order)
        sum_qkv = rs_chain(grad_qkv_weight, n_bits, order)
        summed = (sum_wave, sum_g1, sum_b1, sum_qkv, sum_out, sum_g2, sum_b2, sum_mlp_in,
                  sum_ib, sum_mlp_out, sum_ob, sum_dec, sum_db, sum_mask)
        return (decoded, grad_tokens, *summed)

    return local


def solution(mesh):
    n_dev = mesh.devices.size
    n_bits = n_dev.bit_length() - 1
    order = halving_order(n_bits, core_bit_of(mesh))
    placed = (
        P(AX, None, None),
        P(AX, None),
        P(AX, None),
        P(AX, None),
        P(AX),
        P(AX),
        P(AX, None),
        P(AX, None),
        P(AX),
        P(AX),
        P(AX, None),
        P(AX),
        P(AX, None),
        P(AX),
        P(AX, None),
        P(AX),
        P(AX),
        P(None, AX, None),
    )
    return jax.shard_map(
        make_local(n_bits, order),
        mesh=mesh,
        in_specs=placed,
        out_specs=(
            P(None, AX, None),
            P(AX, None, None),
            P(AX, None),
            P(AX),
            P(AX),
            P(AX, None),
            P(AX, None),
            P(AX),
            P(AX),
            P(AX, None),
            P(AX),
            P(AX, None),
            P(AX),
            P(AX, None),
            P(AX),
            P(AX),
        ),
        check_vma=False,
    )
```

```python
import numpy as np
import jax
import jax.numpy as jnp
from jax import lax
from jax.sharding import PartitionSpec as P

D = 768
HD = 64
DEC = 512
WAVES = 128
L = 1024

NORM_EPSILON = 1e-05
ROOT_HALF = 0.7071067811865476
INVERSE_ROOT_TAU = 0.3989422804014327
HIGH_PRECISION = lax.Precision.HIGHEST
AX = ("dp", "fsdp")


def product(left_op, right_op):
    return jnp.dot(left_op, right_op, preferred_element_type=jnp.float32)


def inner_rows(left_op, right_op):
    return lax.dot_general(
        left_op, right_op, (((0,), (0,)), ((), ())), preferred_element_type=jnp.float32
    )


def outer_cols(left_op, right_op):
    return lax.dot_general(
        left_op, right_op, (((1,), (1,)), ((), ())), preferred_element_type=jnp.float32
    )


def norm_forward(residual, gain, shift):
    mean_val = jnp.mean(residual, axis=-1, keepdims=True)
    centered = residual - mean_val
    variance = jnp.mean(centered * centered, axis=-1, keepdims=True)
    inverse = lax.rsqrt(variance + NORM_EPSILON)
    normed = centered * inverse
    return (normed * gain + shift, normed, inverse)


def norm_backward(incoming, normed, inverse, gain):
    scaled = incoming * gain
    first_mean = jnp.mean(scaled, axis=-1, keepdims=True)
    second_mean = jnp.mean(scaled * normed, axis=-1, keepdims=True)
    grad_input = inverse * (scaled - first_mean - normed * second_mean)
    return (grad_input, jnp.sum(incoming * normed, axis=0), jnp.sum(incoming, axis=0))


def gelu_value(hidden):
    return 0.5 * hidden * (1.0 + lax.erf(hidden * ROOT_HALF))


def gelu_slope(hidden):
    return (
        0.5 * (1.0 + lax.erf(hidden * ROOT_HALF))
        + hidden * jnp.exp(-0.5 * hidden * hidden) * INVERSE_ROOT_TAU
    )


def core_bit_of(mesh):
    flat = list(mesh.devices.reshape(-1))
    cores = [d.core_on_chip for d in flat]
    stride = 1
    while stride < len(flat) and cores[stride] == cores[0]:
        stride *= 2
    return stride.bit_length() - 1


def bit_groups(mesh):
    flat = list(mesh.devices.reshape(-1))
    n_bits = len(flat).bit_length() - 1
    first = flat[0]
    core_bit = None
    groups = {}
    for bit in range(n_bits):
        other = flat[1 << bit]
        if other.core_on_chip != first.core_on_chip:
            core_bit = bit
            continue
        axis = [a for a in range(len(first.coords)) if first.coords[a] != other.coords[a]]
        groups.setdefault(axis[0] if axis else -1, []).append(bit)
    return core_bit, [sorted(bits) for _, bits in sorted(groups.items())]


def chain_orders(core_bit, groups):
    head = [] if core_bit is None else [core_bit]
    if len(groups) < 3:
        flat = head + [b for g in reversed(groups) for b in g]
        return {"y": flat, "x": flat, "yz": flat}
    x_bits, y_bits, z_bits = groups[0], groups[1], [b for g in groups[2:] for b in g]
    return {
        "y": head + y_bits + x_bits + z_bits,
        "x": head + x_bits + y_bits + z_bits,
        "yz": head + y_bits + z_bits + x_bits,
    }


def halving_order(n_bits, core_bit):
    rest = [b for b in reversed(range(n_bits)) if b != core_bit]
    if len(rest) >= 2:
        rest[-2:] = rest[-2:][::-1]
    return [core_bit] + rest


def rs_chain(grad, n_bits, order):
    n_dev = 2 ** n_bits
    me = lax.axis_index(AX)
    rows = grad.shape[0] // n_dev
    current = grad.reshape((2,) * n_bits + (rows,) + grad.shape[1:])
    for bit in order:
        axis = n_bits - 1 - bit
        mine = (me >> bit) & 1
        keep = lax.dynamic_slice_in_dim(current, mine, 1, axis=axis)
        send = lax.dynamic_slice_in_dim(current, 1 - mine, 1, axis=axis)
        moved = lax.ppermute(
            send.astype(jnp.bfloat16), AX, [(i, i ^ (1 << bit)) for i in range(n_dev)]
        )
        current = keep + moved.astype(jnp.float32)
    return current.reshape((rows,) + grad.shape[1:])


def pack_rows(arrays, n_dev, dtype):
    flat = [a.reshape(n_dev, -1).astype(dtype) for a in arrays]
    widths = [f.shape[1] for f in flat]
    padded = -sum(widths) % 1024
    flat.append(jnp.zeros((n_dev, padded), dtype))
    packed = jnp.concatenate(flat, axis=1)
    return packed.reshape(n_dev, 8, -1), widths


def unpack_rows(packed, arrays, widths, n_dev, leading):
    flat = packed.reshape(packed.shape[0], -1)
    out = []
    offset = 0
    for a, width in zip(arrays, widths):
        piece = flat[:, offset : offset + width]
        out.append(piece.reshape((leading * a.shape[0] // n_dev,) + a.shape[1:]))
        offset += width
    return out


def attend(queries, key_rows, value_rows):
    score_scale = HD ** (-0.5)
    scores = (
        jnp.einsum("cqhd,ckhd->chqk", queries, key_rows, preferred_element_type=jnp.float32)
        * score_scale
    )
    row_peak = jnp.max(scores, axis=-1, keepdims=True)
    exponents = jnp.exp(scores - row_peak)
    row_total = jnp.sum(exponents, axis=-1, keepdims=True)
    soft_full = exponents / row_total
    soft_low = soft_full.astype(jnp.bfloat16)
    mixture = jnp.einsum(
        "chqk,ckhd->cqhd", soft_low, value_rows, preferred_element_type=jnp.float32
    )
    return mixture.astype(jnp.bfloat16), soft_full, soft_low


def attend_back(queries, key_rows, value_rows, soft_full, soft_low, grad_mixture):
    score_scale = HD ** (-0.5)
    grad_values = jnp.einsum(
        "chqk,cqhd->ckhd", soft_low, grad_mixture, preferred_element_type=jnp.float32
    )
    grad_soft = jnp.einsum(
        "cqhd,ckhd->chqk", grad_mixture, value_rows, preferred_element_type=jnp.float32
    )
    row_delta = jnp.sum(grad_soft * soft_full, axis=-1, keepdims=True)
    grad_scores = (soft_full * (grad_soft - row_delta)).astype(jnp.bfloat16)
    grad_queries = (
        jnp.einsum("chqk,ckhd->cqhd", grad_scores, key_rows, preferred_element_type=jnp.float32)
        * score_scale
    )
    grad_keys = (
        jnp.einsum("chqk,cqhd->ckhd", grad_scores, queries, preferred_element_type=jnp.float32)
        * score_scale
    )
    return grad_queries, grad_keys, grad_values


def make_local(n_bits, order, orders):
    n_dev = 2 ** n_bits

    def local(
        tokens,
        band_waves,
        visible_slot,
        wave_table,
        norm1_gain,
        norm1_bias,
        qkv_weight,
        out_weight,
        norm2_gain,
        norm2_bias,
        mlp_in,
        mlp_in_bias,
        mlp_out,
        mlp_out_bias,
        dec_weight,
        dec_bias,
        mask_token,
        cot_decoded,
    ):
        shards = (
            wave_table,
            norm1_gain,
            norm1_bias,
            qkv_weight,
            out_weight,
            norm2_gain,
            norm2_bias,
            mlp_in,
            mlp_in_bias,
            mlp_out,
            mlp_out_bias,
            dec_weight,
            dec_bias,
            mask_token,
        )
        small = (wave_table, norm1_gain, norm1_bias, norm2_gain, norm2_bias, mlp_in_bias,
                 mlp_out_bias, dec_bias, mask_token)
        packed_small, small_widths = pack_rows(
            [a.reshape(1, -1) for a in small], 1, jnp.bfloat16
        )
        gathered_small = lax.all_gather(packed_small, AX, axis=0, tiled=True)
        (wave_full, gain_one, shift_one, gain_two, shift_two, inner_bias, outer_bias,
         dec_shift, mask_full) = unpack_rows(gathered_small, small, small_widths, 1, n_dev)
        wide = (qkv_weight, out_weight, mlp_in, dec_weight)
        wide_cols = [a.shape[1] for a in wide]
        gathered_wide = lax.all_gather(jnp.concatenate(wide, axis=1), AX, axis=0, tiled=True)
        wide_full = []
        offset = 0
        for cols in wide_cols:
            wide_full.append(gathered_wide[:, offset : offset + cols])
            offset += cols
        qkv_full, out_full, inner_full, dec_full = wide_full
        outer_full = lax.all_gather(mlp_out, AX, axis=0, tiled=True)

        chip_count, vis_len, feature_width = tokens.shape
        row_count = chip_count * vis_len
        heads = feature_width // HD
        counts = jnp.sum(
            (band_waves[:, :, None] == jnp.arange(WAVES, dtype=jnp.int32)[None, None, :]).astype(
                jnp.float32
            ),
            axis=1,
        )
        spectral = jnp.dot(
            counts.astype(jnp.bfloat16), wave_full, preferred_element_type=jnp.float32
        )
        residual = (tokens.astype(jnp.float32) + spectral[:, None, :]).reshape(row_count, D)
        norm_out_one, normed_one, inverse_one = norm_forward(
            residual, gain_one.astype(jnp.float32), shift_one.astype(jnp.float32)
        )
        act_one = norm_out_one.astype(jnp.bfloat16)
        qkv_vals = product(act_one, qkv_full).astype(jnp.bfloat16)
        head_shape = (chip_count, vis_len, heads, HD)
        queries = qkv_vals[:, :D].reshape(head_shape)
        key_rows = qkv_vals[:, D : 2 * D].reshape(head_shape)
        value_rows = qkv_vals[:, 2 * D :].reshape(head_shape)
        mixture4, soft_full, soft_low = attend(queries, key_rows, value_rows)
        mixture = mixture4.reshape(row_count, D)
        res_one = residual + product(mixture, out_full)
        norm_out_two, normed_two, inverse_two = norm_forward(
            res_one, gain_two.astype(jnp.float32), shift_two.astype(jnp.float32)
        )
        act_two = norm_out_two.astype(jnp.bfloat16)
        hidden = product(act_two, inner_full) + inner_bias.astype(jnp.float32)
        active = gelu_value(hidden).astype(jnp.bfloat16)
        res_two = res_one + (product(active, outer_full) + outer_bias.astype(jnp.float32))
        enc_low = res_two.astype(jnp.bfloat16)
        projected = (product(enc_low, dec_full) + dec_shift.astype(jnp.float32)).astype(
            jnp.bfloat16
        )
        slot_ids = jnp.arange(L, dtype=jnp.int32)
        one_hot = (visible_slot[:, None, :] == slot_ids[None, :, None]).astype(jnp.bfloat16)
        filled_vis = jnp.einsum(
            "csi,cie->cse",
            one_hot,
            projected.reshape(chip_count, vis_len, DEC),
            preferred_element_type=jnp.float32,
        )
        has_row = jnp.sum(one_hot.astype(jnp.float32), axis=2, keepdims=True) > 0.5
        filled = jnp.where(has_row, filled_vis, mask_full.astype(jnp.float32)[None, None, :])
        filled = filled.astype(jnp.bfloat16)
        decoded = lax.all_to_all(filled, AX, split_axis=1, concat_axis=0, tiled=True)
        grad_full = lax.all_to_all(cot_decoded, AX, split_axis=0, concat_axis=1, tiled=True)

        grad_vis_low = (
            jnp.einsum("csi,cse->cie", one_hot, grad_full, preferred_element_type=jnp.float32)
            .astype(jnp.bfloat16)
            .reshape(row_count, DEC)
        )
        grad_vis = grad_vis_low.astype(jnp.float32)
        grad_mask_token = jnp.sum(
            jnp.where(has_row, 0.0, grad_full.astype(jnp.float32)), axis=(0, 1)
        )
        grad_dec_bias = jnp.sum(grad_vis, axis=0)
        grad_dec_weight = inner_rows(enc_low, grad_vis_low)
        grad_res_two = outer_cols(grad_vis_low, dec_full)
        grad_ffo = grad_res_two.astype(jnp.bfloat16)
        grad_mlp_out_bias = jnp.sum(grad_ffo.astype(jnp.float32), axis=0)
        grad_mlp_out = inner_rows(active, grad_ffo)
        grad_hidden = (outer_cols(grad_ffo, outer_full) * gelu_slope(hidden)).astype(jnp.bfloat16)
        grad_mlp_in_bias = jnp.sum(grad_hidden.astype(jnp.float32), axis=0)
        grad_mlp_in = inner_rows(act_two, grad_hidden)
        grad_act_two = outer_cols(grad_hidden, inner_full)
        grad_norm_two, grad_norm2_gain, grad_norm2_bias = norm_backward(
            grad_act_two, normed_two, inverse_two, gain_two.astype(jnp.float32)
        )
        grad_res_one = grad_res_two + grad_norm_two
        grad_att = grad_res_one.astype(jnp.bfloat16)
        grad_out_weight = inner_rows(mixture, grad_att)
        grad_mixed = outer_cols(grad_att, out_full).astype(jnp.bfloat16).reshape(head_shape)
        grad_queries, grad_keys, grad_values = attend_back(
            queries, key_rows, value_rows, soft_full, soft_low, grad_mixed
        )
        grad_qkv = jnp.concatenate(
            [
                grad_queries.reshape(row_count, D),
                grad_keys.reshape(row_count, D),
                grad_values.reshape(row_count, D),
            ],
            axis=1,
        ).astype(jnp.bfloat16)
        grad_qkv_weight = inner_rows(act_one, grad_qkv)
        grad_act_one = outer_cols(grad_qkv, qkv_full)
        grad_norm_one, grad_norm1_gain, grad_norm1_bias = norm_backward(
            grad_act_one, normed_one, inverse_one, gain_one.astype(jnp.float32)
        )
        grad_tokens = (grad_res_one + grad_norm_one).reshape(chip_count, vis_len, D)
        chip_sums = jnp.sum(grad_tokens, axis=1)
        grad_wave_table = lax.dot_general(
            counts, chip_sums, (((0,), (0,)), ((), ())), precision=HIGH_PRECISION
        )
        small_grads = (grad_wave_table, grad_norm1_gain, grad_norm1_bias, grad_norm2_gain,
                       grad_norm2_bias, grad_mlp_in_bias, grad_mlp_out_bias, grad_dec_bias,
                       grad_mask_token)
        packed_sg, sg_widths = pack_rows(small_grads, n_dev, jnp.float32)
        reduced_sg = rs_chain(packed_sg, n_bits, orders["yz"])
        (sum_wave, sum_g1, sum_b1, sum_g2, sum_b2, sum_ib, sum_ob, sum_db,
         sum_mask) = unpack_rows(reduced_sg, small_grads, sg_widths, n_dev, 1)
        sum_dec = rs_chain(grad_dec_weight, n_bits, orders["y"])
        sum_mlp_out = rs_chain(grad_mlp_out, n_bits, orders["x"])
        sum_mlp_in = rs_chain(grad_mlp_in, n_bits, orders["y"])
        sum_out = rs_chain(grad_out_weight, n_bits, orders["x"])
        sum_qkv = rs_chain(grad_qkv_weight, n_bits, orders["yz"])
        summed = (sum_wave, sum_g1, sum_b1, sum_qkv, sum_out, sum_g2, sum_b2, sum_mlp_in,
                  sum_ib, sum_mlp_out, sum_ob, sum_dec, sum_db, sum_mask)
        return (decoded, grad_tokens, *summed)

    return local


def solution(mesh):
    n_dev = mesh.devices.size
    n_bits = n_dev.bit_length() - 1
    order = halving_order(n_bits, core_bit_of(mesh))
    orders = chain_orders(*bit_groups(mesh))
    placed = (
        P(AX, None, None),
        P(AX, None),
        P(AX, None),
        P(AX, None),
        P(AX),
        P(AX),
        P(AX, None),
        P(AX, None),
        P(AX),
        P(AX),
        P(AX, None),
        P(AX),
        P(AX, None),
        P(AX),
        P(AX, None),
        P(AX),
        P(AX),
        P(None, AX, None),
    )
    return jax.shard_map(
        make_local(n_bits, order, orders),
        mesh=mesh,
        in_specs=placed,
        out_specs=(
            P(None, AX, None),
            P(AX, None, None),
            P(AX, None),
            P(AX),
            P(AX),
            P(AX, None),
            P(AX, None),
            P(AX),
            P(AX),
            P(AX, None),
            P(AX),
            P(AX, None),
            P(AX),
            P(AX, None),
            P(AX),
            P(AX),
        ),
        check_vma=False,
    )
```

```python
import numpy as np
import jax
import jax.numpy as jnp
from jax import lax
from jax.sharding import PartitionSpec as P

D = 768
HD = 64
DEC = 512
WAVES = 128
L = 1024

NORM_EPSILON = 1e-05
ROOT_HALF = 0.7071067811865476
INVERSE_ROOT_TAU = 0.3989422804014327
HIGH_PRECISION = lax.Precision.HIGHEST
AX = ("dp", "fsdp")


def product(left_op, right_op):
    return jnp.dot(left_op, right_op, preferred_element_type=jnp.float32)


def inner_rows(left_op, right_op):
    return lax.dot_general(
        left_op, right_op, (((0,), (0,)), ((), ())), preferred_element_type=jnp.float32
    )


def outer_cols(left_op, right_op):
    return lax.dot_general(
        left_op, right_op, (((1,), (1,)), ((), ())), preferred_element_type=jnp.float32
    )


def norm_forward(residual, gain, shift):
    mean_val = jnp.mean(residual, axis=-1, keepdims=True)
    centered = residual - mean_val
    variance = jnp.mean(centered * centered, axis=-1, keepdims=True)
    inverse = lax.rsqrt(variance + NORM_EPSILON)
    normed = centered * inverse
    return (normed * gain + shift, normed, inverse)


def norm_backward(incoming, normed, inverse, gain):
    scaled = incoming * gain
    first_mean = jnp.mean(scaled, axis=-1, keepdims=True)
    second_mean = jnp.mean(scaled * normed, axis=-1, keepdims=True)
    grad_input = inverse * (scaled - first_mean - normed * second_mean)
    return (grad_input, jnp.sum(incoming * normed, axis=0), jnp.sum(incoming, axis=0))


def gelu_value(hidden):
    return 0.5 * hidden * (1.0 + lax.erf(hidden * ROOT_HALF))


def gelu_slope(hidden):
    return (
        0.5 * (1.0 + lax.erf(hidden * ROOT_HALF))
        + hidden * jnp.exp(-0.5 * hidden * hidden) * INVERSE_ROOT_TAU
    )


def core_bit_of(mesh):
    flat = list(mesh.devices.reshape(-1))
    cores = [d.core_on_chip for d in flat]
    stride = 1
    while stride < len(flat) and cores[stride] == cores[0]:
        stride *= 2
    return stride.bit_length() - 1


def bit_groups(mesh):
    flat = list(mesh.devices.reshape(-1))
    n_bits = len(flat).bit_length() - 1
    first = flat[0]
    core_bit = None
    groups = {}
    for bit in range(n_bits):
        other = flat[1 << bit]
        if other.core_on_chip != first.core_on_chip:
            core_bit = bit
            continue
        axis = [a for a in range(len(first.coords)) if first.coords[a] != other.coords[a]]
        groups.setdefault(axis[0] if axis else -1, []).append(bit)
    return core_bit, [sorted(bits) for _, bits in sorted(groups.items())]


def chain_orders(core_bit, groups):
    head = [] if core_bit is None else [core_bit]
    if len(groups) < 3:
        flat = head + [b for g in reversed(groups) for b in g]
        return {"y": flat, "x": flat, "yz": flat}
    x_bits, y_bits, z_bits = groups[0], groups[1], [b for g in groups[2:] for b in g]
    return {
        "y": head + y_bits + x_bits + z_bits,
        "x": head + x_bits + y_bits + z_bits,
        "yz": head + y_bits + z_bits + x_bits,
    }


def halving_order(n_bits, core_bit):
    rest = [b for b in reversed(range(n_bits)) if b != core_bit]
    if len(rest) >= 2:
        rest[-2:] = rest[-2:][::-1]
    return [core_bit] + rest


def rs_chain(grad, n_bits, order):
    n_dev = 2 ** n_bits
    me = lax.axis_index(AX)
    rows = grad.shape[0] // n_dev
    current = grad.reshape((2,) * n_bits + (rows,) + grad.shape[1:])
    for bit in order:
        axis = n_bits - 1 - bit
        mine = (me >> bit) & 1
        keep = lax.dynamic_slice_in_dim(current, mine, 1, axis=axis)
        send = lax.dynamic_slice_in_dim(current, 1 - mine, 1, axis=axis)
        moved = lax.ppermute(
            send.astype(jnp.bfloat16), AX, [(i, i ^ (1 << bit)) for i in range(n_dev)]
        )
        current = keep + moved.astype(jnp.float32)
    return current.reshape((rows,) + grad.shape[1:])


def ag_chain(block, n_bits, order):
    me = lax.axis_index(AX)
    n_dev = 2 ** n_bits
    current = block.reshape((1,) * n_bits + block.shape)
    for bit in reversed(order):
        axis = n_bits - 1 - bit
        mine = ((me >> bit) & 1) == 1
        moved = lax.ppermute(current, AX, [(i, i ^ (1 << bit)) for i in range(n_dev)])
        low = jnp.where(mine, moved, current)
        high = jnp.where(mine, current, moved)
        current = jnp.concatenate([low, high], axis=axis)
    return current.reshape((n_dev * block.shape[0],) + block.shape[1:])


def pack_rows(arrays, n_dev, dtype):
    flat = [a.reshape(n_dev, -1).astype(dtype) for a in arrays]
    widths = [f.shape[1] for f in flat]
    padded = -sum(widths) % 1024
    flat.append(jnp.zeros((n_dev, padded), dtype))
    packed = jnp.concatenate(flat, axis=1)
    return packed.reshape(n_dev, 8, -1), widths


def unpack_rows(packed, arrays, widths, n_dev, leading):
    flat = packed.reshape(packed.shape[0], -1)
    out = []
    offset = 0
    for a, width in zip(arrays, widths):
        piece = flat[:, offset : offset + width]
        out.append(piece.reshape((leading * a.shape[0] // n_dev,) + a.shape[1:]))
        offset += width
    return out


def attend(queries, key_rows, value_rows):
    score_scale = HD ** (-0.5)
    scores = (
        jnp.einsum("cqhd,ckhd->chqk", queries, key_rows, preferred_element_type=jnp.float32)
        * score_scale
    )
    row_peak = jnp.max(scores, axis=-1, keepdims=True)
    exponents = jnp.exp(scores - row_peak)
    row_total = jnp.sum(exponents, axis=-1, keepdims=True)
    soft_full = exponents / row_total
    soft_low = soft_full.astype(jnp.bfloat16)
    mixture = jnp.einsum(
        "chqk,ckhd->cqhd", soft_low, value_rows, preferred_element_type=jnp.float32
    )
    return mixture.astype(jnp.bfloat16), soft_full, soft_low


def attend_back(queries, key_rows, value_rows, soft_full, soft_low, grad_mixture):
    score_scale = HD ** (-0.5)
    grad_values = jnp.einsum(
        "chqk,cqhd->ckhd", soft_low, grad_mixture, preferred_element_type=jnp.float32
    )
    grad_soft = jnp.einsum(
        "cqhd,ckhd->chqk", grad_mixture, value_rows, preferred_element_type=jnp.float32
    )
    row_delta = jnp.sum(grad_soft * soft_full, axis=-1, keepdims=True)
    grad_scores = (soft_full * (grad_soft - row_delta)).astype(jnp.bfloat16)
    grad_queries = (
        jnp.einsum("chqk,ckhd->cqhd", grad_scores, key_rows, preferred_element_type=jnp.float32)
        * score_scale
    )
    grad_keys = (
        jnp.einsum("chqk,cqhd->ckhd", grad_scores, queries, preferred_element_type=jnp.float32)
        * score_scale
    )
    return grad_queries, grad_keys, grad_values


def make_local(n_bits, order, orders):
    n_dev = 2 ** n_bits

    def local(
        tokens,
        band_waves,
        visible_slot,
        wave_table,
        norm1_gain,
        norm1_bias,
        qkv_weight,
        out_weight,
        norm2_gain,
        norm2_bias,
        mlp_in,
        mlp_in_bias,
        mlp_out,
        mlp_out_bias,
        dec_weight,
        dec_bias,
        mask_token,
        cot_decoded,
    ):
        shards = (
            wave_table,
            norm1_gain,
            norm1_bias,
            qkv_weight,
            out_weight,
            norm2_gain,
            norm2_bias,
            mlp_in,
            mlp_in_bias,
            mlp_out,
            mlp_out_bias,
            dec_weight,
            dec_bias,
            mask_token,
        )
        small = (wave_table, norm1_gain, norm1_bias, norm2_gain, norm2_bias, mlp_in_bias,
                 mlp_out_bias, dec_bias, mask_token)
        packed_small, small_widths = pack_rows(
            [a.reshape(1, -1) for a in small], 1, jnp.bfloat16
        )
        gathered_small = ag_chain(packed_small, n_bits, orders["x"])
        (wave_full, gain_one, shift_one, gain_two, shift_two, inner_bias, outer_bias,
         dec_shift, mask_full) = unpack_rows(gathered_small, small, small_widths, 1, n_dev)
        wide = (qkv_weight, out_weight, mlp_in, dec_weight)
        wide_cols = [a.shape[1] for a in wide]
        gathered_wide = lax.all_gather(jnp.concatenate(wide, axis=1), AX, axis=0, tiled=True)
        wide_full = []
        offset = 0
        for cols in wide_cols:
            wide_full.append(gathered_wide[:, offset : offset + cols])
            offset += cols
        qkv_full, out_full, inner_full, dec_full = wide_full
        outer_full = lax.all_gather(mlp_out, AX, axis=0, tiled=True)

        chip_count, vis_len, feature_width = tokens.shape
        row_count = chip_count * vis_len
        heads = feature_width // HD
        counts = jnp.sum(
            (band_waves[:, :, None] == jnp.arange(WAVES, dtype=jnp.int32)[None, None, :]).astype(
                jnp.float32
            ),
            axis=1,
        )
        spectral = jnp.dot(
            counts.astype(jnp.bfloat16), wave_full, preferred_element_type=jnp.float32
        )
        residual = (tokens.astype(jnp.float32) + spectral[:, None, :]).reshape(row_count, D)
        norm_out_one, normed_one, inverse_one = norm_forward(
            residual, gain_one.astype(jnp.float32), shift_one.astype(jnp.float32)
        )
        act_one = norm_out_one.astype(jnp.bfloat16)
        qkv_vals = product(act_one, qkv_full).astype(jnp.bfloat16)
        head_shape = (chip_count, vis_len, heads, HD)
        queries = qkv_vals[:, :D].reshape(head_shape)
        key_rows = qkv_vals[:, D : 2 * D].reshape(head_shape)
        value_rows = qkv_vals[:, 2 * D :].reshape(head_shape)
        mixture4, soft_full, soft_low = attend(queries, key_rows, value_rows)
        mixture = mixture4.reshape(row_count, D)
        res_one = residual + product(mixture, out_full)
        norm_out_two, normed_two, inverse_two = norm_forward(
            res_one, gain_two.astype(jnp.float32), shift_two.astype(jnp.float32)
        )
        act_two = norm_out_two.astype(jnp.bfloat16)
        hidden = product(act_two, inner_full) + inner_bias.astype(jnp.float32)
        active = gelu_value(hidden).astype(jnp.bfloat16)
        res_two = res_one + (product(active, outer_full) + outer_bias.astype(jnp.float32))
        enc_low = res_two.astype(jnp.bfloat16)
        projected = (product(enc_low, dec_full) + dec_shift.astype(jnp.float32)).astype(
            jnp.bfloat16
        )
        slot_ids = jnp.arange(L, dtype=jnp.int32)
        one_hot = (visible_slot[:, None, :] == slot_ids[None, :, None]).astype(jnp.bfloat16)
        filled_vis = jnp.einsum(
            "csi,cie->cse",
            one_hot,
            projected.reshape(chip_count, vis_len, DEC),
            preferred_element_type=jnp.float32,
        )
        has_row = jnp.sum(one_hot.astype(jnp.float32), axis=2, keepdims=True) > 0.5
        filled = jnp.where(has_row, filled_vis, mask_full.astype(jnp.float32)[None, None, :])
        filled = filled.astype(jnp.bfloat16)
        decoded = lax.all_to_all(filled, AX, split_axis=1, concat_axis=0, tiled=True)
        grad_full = lax.all_to_all(cot_decoded, AX, split_axis=0, concat_axis=1, tiled=True)

        grad_vis_low = (
            jnp.einsum("csi,cse->cie", one_hot, grad_full, preferred_element_type=jnp.float32)
            .astype(jnp.bfloat16)
            .reshape(row_count, DEC)
        )
        grad_vis = grad_vis_low.astype(jnp.float32)
        grad_mask_token = jnp.sum(
            jnp.where(has_row, 0.0, grad_full.astype(jnp.float32)), axis=(0, 1)
        )
        grad_dec_bias = jnp.sum(grad_vis, axis=0)
        grad_dec_weight = inner_rows(enc_low, grad_vis_low)
        grad_res_two = outer_cols(grad_vis_low, dec_full)
        grad_ffo = grad_res_two.astype(jnp.bfloat16)
        grad_mlp_out_bias = jnp.sum(grad_ffo.astype(jnp.float32), axis=0)
        grad_mlp_out = inner_rows(active, grad_ffo)
        grad_hidden = (outer_cols(grad_ffo, outer_full) * gelu_slope(hidden)).astype(jnp.bfloat16)
        grad_mlp_in_bias = jnp.sum(grad_hidden.astype(jnp.float32), axis=0)
        grad_mlp_in = inner_rows(act_two, grad_hidden)
        grad_act_two = outer_cols(grad_hidden, inner_full)
        grad_norm_two, grad_norm2_gain, grad_norm2_bias = norm_backward(
            grad_act_two, normed_two, inverse_two, gain_two.astype(jnp.float32)
        )
        grad_res_one = grad_res_two + grad_norm_two
        grad_att = grad_res_one.astype(jnp.bfloat16)
        grad_out_weight = inner_rows(mixture, grad_att)
        grad_mixed = outer_cols(grad_att, out_full).astype(jnp.bfloat16).reshape(head_shape)
        grad_queries, grad_keys, grad_values = attend_back(
            queries, key_rows, value_rows, soft_full, soft_low, grad_mixed
        )
        grad_qkv = jnp.concatenate(
            [
                grad_queries.reshape(row_count, D),
                grad_keys.reshape(row_count, D),
                grad_values.reshape(row_count, D),
            ],
            axis=1,
        ).astype(jnp.bfloat16)
        grad_qkv_weight = inner_rows(act_one, grad_qkv)
        grad_act_one = outer_cols(grad_qkv, qkv_full)
        grad_norm_one, grad_norm1_gain, grad_norm1_bias = norm_backward(
            grad_act_one, normed_one, inverse_one, gain_one.astype(jnp.float32)
        )
        grad_tokens = (grad_res_one + grad_norm_one).reshape(chip_count, vis_len, D)
        chip_sums = jnp.sum(grad_tokens, axis=1)
        grad_wave_table = lax.dot_general(
            counts, chip_sums, (((0,), (0,)), ((), ())), precision=HIGH_PRECISION
        )
        small_grads = (grad_wave_table, grad_norm1_gain, grad_norm1_bias, grad_norm2_gain,
                       grad_norm2_bias, grad_mlp_in_bias, grad_mlp_out_bias, grad_dec_bias,
                       grad_mask_token)
        packed_sg, sg_widths = pack_rows(small_grads, n_dev, jnp.float32)
        reduced_sg = rs_chain(packed_sg, n_bits, orders["yz"])
        (sum_wave, sum_g1, sum_b1, sum_g2, sum_b2, sum_ib, sum_ob, sum_db,
         sum_mask) = unpack_rows(reduced_sg, small_grads, sg_widths, n_dev, 1)
        sum_dec = rs_chain(grad_dec_weight, n_bits, orders["y"])
        sum_mlp_out = rs_chain(grad_mlp_out, n_bits, orders["x"])
        sum_mlp_in = rs_chain(grad_mlp_in, n_bits, orders["y"])
        sum_out = rs_chain(grad_out_weight, n_bits, orders["x"])
        sum_qkv = rs_chain(grad_qkv_weight, n_bits, orders["yz"])
        summed = (sum_wave, sum_g1, sum_b1, sum_qkv, sum_out, sum_g2, sum_b2, sum_mlp_in,
                  sum_ib, sum_mlp_out, sum_ob, sum_dec, sum_db, sum_mask)
        return (decoded, grad_tokens, *summed)

    return local


def solution(mesh):
    n_dev = mesh.devices.size
    n_bits = n_dev.bit_length() - 1
    order = halving_order(n_bits, core_bit_of(mesh))
    orders = chain_orders(*bit_groups(mesh))
    placed = (
        P(AX, None, None),
        P(AX, None),
        P(AX, None),
        P(AX, None),
        P(AX),
        P(AX),
        P(AX, None),
        P(AX, None),
        P(AX),
        P(AX),
        P(AX, None),
        P(AX),
        P(AX, None),
        P(AX),
        P(AX, None),
        P(AX),
        P(AX),
        P(None, AX, None),
    )
    return jax.shard_map(
        make_local(n_bits, order, orders),
        mesh=mesh,
        in_specs=placed,
        out_specs=(
            P(None, AX, None),
            P(AX, None, None),
            P(AX, None),
            P(AX),
            P(AX),
            P(AX, None),
            P(AX, None),
            P(AX),
            P(AX),
            P(AX, None),
            P(AX),
            P(AX, None),
            P(AX),
            P(AX, None),
            P(AX),
            P(AX),
        ),
        check_vma=False,
    )
```

```python
import numpy as np
import jax
import jax.numpy as jnp
from jax import lax
from jax.sharding import PartitionSpec as P

D = 768
HD = 64
DEC = 512
WAVES = 128
L = 1024

NORM_EPSILON = 1e-05
ROOT_HALF = 0.7071067811865476
INVERSE_ROOT_TAU = 0.3989422804014327
HIGH_PRECISION = lax.Precision.HIGHEST
AX = ("dp", "fsdp")


def product(left_op, right_op):
    return jnp.dot(left_op, right_op, preferred_element_type=jnp.float32)


def inner_rows(left_op, right_op):
    return lax.dot_general(
        left_op, right_op, (((0,), (0,)), ((), ())), preferred_element_type=jnp.float32
    )


def outer_cols(left_op, right_op):
    return lax.dot_general(
        left_op, right_op, (((1,), (1,)), ((), ())), preferred_element_type=jnp.float32
    )


def norm_forward(residual, gain, shift):
    mean_val = jnp.mean(residual, axis=-1, keepdims=True)
    centered = residual - mean_val
    variance = jnp.mean(centered * centered, axis=-1, keepdims=True)
    inverse = lax.rsqrt(variance + NORM_EPSILON)
    normed = centered * inverse
    return (normed * gain + shift, normed, inverse)


def norm_backward(incoming, normed, inverse, gain):
    scaled = incoming * gain
    first_mean = jnp.mean(scaled, axis=-1, keepdims=True)
    second_mean = jnp.mean(scaled * normed, axis=-1, keepdims=True)
    grad_input = inverse * (scaled - first_mean - normed * second_mean)
    return (grad_input, jnp.sum(incoming * normed, axis=0), jnp.sum(incoming, axis=0))


def gelu_value(hidden):
    return 0.5 * hidden * (1.0 + lax.erf(hidden * ROOT_HALF))


def gelu_slope(hidden):
    return (
        0.5 * (1.0 + lax.erf(hidden * ROOT_HALF))
        + hidden * jnp.exp(-0.5 * hidden * hidden) * INVERSE_ROOT_TAU
    )


def core_bit_of(mesh):
    flat = list(mesh.devices.reshape(-1))
    cores = [d.core_on_chip for d in flat]
    stride = 1
    while stride < len(flat) and cores[stride] == cores[0]:
        stride *= 2
    return stride.bit_length() - 1


def bit_groups(mesh):
    flat = list(mesh.devices.reshape(-1))
    n_bits = len(flat).bit_length() - 1
    first = flat[0]
    core_bit = None
    groups = {}
    for bit in range(n_bits):
        other = flat[1 << bit]
        if other.core_on_chip != first.core_on_chip:
            core_bit = bit
            continue
        axis = [a for a in range(len(first.coords)) if first.coords[a] != other.coords[a]]
        groups.setdefault(axis[0] if axis else -1, []).append(bit)
    return core_bit, [sorted(bits) for _, bits in sorted(groups.items())]


def chain_orders(core_bit, groups):
    head = [] if core_bit is None else [core_bit]
    if len(groups) < 3:
        flat = head + [b for g in reversed(groups) for b in g]
        return {"y": flat, "x": flat, "yz": flat}
    x_bits, y_bits, z_bits = groups[0], groups[1], [b for g in groups[2:] for b in g]
    return {
        "y": head + y_bits + x_bits + z_bits,
        "x": head + x_bits + y_bits + z_bits,
        "yz": head + y_bits + z_bits + x_bits,
    }


def halving_order(n_bits, core_bit):
    rest = [b for b in reversed(range(n_bits)) if b != core_bit]
    if len(rest) >= 2:
        rest[-2:] = rest[-2:][::-1]
    return [core_bit] + rest


def rs_chain(grad, n_bits, order):
    n_dev = 2 ** n_bits
    me = lax.axis_index(AX)
    rows = grad.shape[0] // n_dev
    current = grad.reshape((2,) * n_bits + (rows,) + grad.shape[1:])
    for bit in order:
        axis = n_bits - 1 - bit
        mine = (me >> bit) & 1
        keep = lax.dynamic_slice_in_dim(current, mine, 1, axis=axis)
        send = lax.dynamic_slice_in_dim(current, 1 - mine, 1, axis=axis)
        moved = lax.ppermute(
            send.astype(jnp.bfloat16), AX, [(i, i ^ (1 << bit)) for i in range(n_dev)]
        )
        current = keep + moved.astype(jnp.float32)
    return current.reshape((rows,) + grad.shape[1:])


def ag_chain(block, n_bits, order):
    me = lax.axis_index(AX)
    n_dev = 2 ** n_bits
    current = block.reshape((1,) * n_bits + block.shape)
    for bit in reversed(order):
        axis = n_bits - 1 - bit
        mine = ((me >> bit) & 1) == 1
        moved = lax.ppermute(current, AX, [(i, i ^ (1 << bit)) for i in range(n_dev)])
        low = jnp.where(mine, moved, current)
        high = jnp.where(mine, current, moved)
        current = jnp.concatenate([low, high], axis=axis)
    return current.reshape((n_dev * block.shape[0],) + block.shape[1:])


def pack_rows(arrays, n_dev, dtype):
    flat = [a.reshape(n_dev, -1).astype(dtype) for a in arrays]
    widths = [f.shape[1] for f in flat]
    padded = -sum(widths) % 1024
    flat.append(jnp.zeros((n_dev, padded), dtype))
    packed = jnp.concatenate(flat, axis=1)
    return packed.reshape(n_dev, 8, -1), widths


def unpack_rows(packed, arrays, widths, n_dev, leading):
    flat = packed.reshape(packed.shape[0], -1)
    out = []
    offset = 0
    for a, width in zip(arrays, widths):
        piece = flat[:, offset : offset + width]
        out.append(piece.reshape((leading * a.shape[0] // n_dev,) + a.shape[1:]))
        offset += width
    return out


def attend(queries, key_rows, value_rows):
    score_scale = HD ** (-0.5)
    scores = (
        jnp.einsum("cqhd,ckhd->chqk", queries, key_rows, preferred_element_type=jnp.float32)
        * score_scale
    )
    row_peak = jnp.max(scores, axis=-1, keepdims=True)
    exponents = jnp.exp(scores - row_peak)
    row_total = jnp.sum(exponents, axis=-1, keepdims=True)
    soft_full = exponents / row_total
    soft_low = soft_full.astype(jnp.bfloat16)
    mixture = jnp.einsum(
        "chqk,ckhd->cqhd", soft_low, value_rows, preferred_element_type=jnp.float32
    )
    return mixture.astype(jnp.bfloat16), soft_full, soft_low


def attend_back(queries, key_rows, value_rows, soft_full, soft_low, grad_mixture):
    score_scale = HD ** (-0.5)
    grad_values = jnp.einsum(
        "chqk,cqhd->ckhd", soft_low, grad_mixture, preferred_element_type=jnp.float32
    )
    grad_soft = jnp.einsum(
        "cqhd,ckhd->chqk", grad_mixture, value_rows, preferred_element_type=jnp.float32
    )
    row_delta = jnp.sum(grad_soft * soft_full, axis=-1, keepdims=True)
    grad_scores = (soft_full * (grad_soft - row_delta)).astype(jnp.bfloat16)
    grad_queries = (
        jnp.einsum("chqk,ckhd->cqhd", grad_scores, key_rows, preferred_element_type=jnp.float32)
        * score_scale
    )
    grad_keys = (
        jnp.einsum("chqk,cqhd->ckhd", grad_scores, queries, preferred_element_type=jnp.float32)
        * score_scale
    )
    return grad_queries, grad_keys, grad_values


def make_local(n_bits, order, orders):
    n_dev = 2 ** n_bits

    def local(
        tokens,
        band_waves,
        visible_slot,
        wave_table,
        norm1_gain,
        norm1_bias,
        qkv_weight,
        out_weight,
        norm2_gain,
        norm2_bias,
        mlp_in,
        mlp_in_bias,
        mlp_out,
        mlp_out_bias,
        dec_weight,
        dec_bias,
        mask_token,
        cot_decoded,
    ):
        shards = (
            wave_table,
            norm1_gain,
            norm1_bias,
            qkv_weight,
            out_weight,
            norm2_gain,
            norm2_bias,
            mlp_in,
            mlp_in_bias,
            mlp_out,
            mlp_out_bias,
            dec_weight,
            dec_bias,
            mask_token,
        )
        small = (wave_table, norm1_gain, norm1_bias, norm2_gain, norm2_bias, mlp_in_bias,
                 mlp_out_bias, dec_bias, mask_token)
        packed_small, small_widths = pack_rows(
            [a.reshape(1, -1) for a in small], 1, jnp.bfloat16
        )
        gathered_small = ag_chain(packed_small, n_bits, orders["x"])
        (wave_full, gain_one, shift_one, gain_two, shift_two, inner_bias, outer_bias,
         dec_shift, mask_full) = unpack_rows(gathered_small, small, small_widths, 1, n_dev)
        qkv_full = ag_chain(qkv_weight, n_bits, orders["yz"])
        out_full = ag_chain(out_weight, n_bits, orders["x"])
        inner_full = ag_chain(mlp_in, n_bits, orders["y"])
        dec_full = ag_chain(dec_weight, n_bits, orders["y"])
        outer_full = ag_chain(mlp_out, n_bits, orders["x"])

        chip_count, vis_len, feature_width = tokens.shape
        row_count = chip_count * vis_len
        heads = feature_width // HD
        counts = jnp.sum(
            (band_waves[:, :, None] == jnp.arange(WAVES, dtype=jnp.int32)[None, None, :]).astype(
                jnp.float32
            ),
            axis=1,
        )
        spectral = jnp.dot(
            counts.astype(jnp.bfloat16), wave_full, preferred_element_type=jnp.float32
        )
        residual = (tokens.astype(jnp.float32) + spectral[:, None, :]).reshape(row_count, D)
        norm_out_one, normed_one, inverse_one = norm_forward(
            residual, gain_one.astype(jnp.float32), shift_one.astype(jnp.float32)
        )
        act_one = norm_out_one.astype(jnp.bfloat16)
        qkv_vals = product(act_one, qkv_full).astype(jnp.bfloat16)
        head_shape = (chip_count, vis_len, heads, HD)
        queries = qkv_vals[:, :D].reshape(head_shape)
        key_rows = qkv_vals[:, D : 2 * D].reshape(head_shape)
        value_rows = qkv_vals[:, 2 * D :].reshape(head_shape)
        mixture4, soft_full, soft_low = attend(queries, key_rows, value_rows)
        mixture = mixture4.reshape(row_count, D)
        res_one = residual + product(mixture, out_full)
        norm_out_two, normed_two, inverse_two = norm_forward(
            res_one, gain_two.astype(jnp.float32), shift_two.astype(jnp.float32)
        )
        act_two = norm_out_two.astype(jnp.bfloat16)
        hidden = product(act_two, inner_full) + inner_bias.astype(jnp.float32)
        active = gelu_value(hidden).astype(jnp.bfloat16)
        res_two = res_one + (product(active, outer_full) + outer_bias.astype(jnp.float32))
        enc_low = res_two.astype(jnp.bfloat16)
        projected = (product(enc_low, dec_full) + dec_shift.astype(jnp.float32)).astype(
            jnp.bfloat16
        )
        slot_ids = jnp.arange(L, dtype=jnp.int32)
        one_hot = (visible_slot[:, None, :] == slot_ids[None, :, None]).astype(jnp.bfloat16)
        filled_vis = jnp.einsum(
            "csi,cie->cse",
            one_hot,
            projected.reshape(chip_count, vis_len, DEC),
            preferred_element_type=jnp.float32,
        )
        has_row = jnp.sum(one_hot.astype(jnp.float32), axis=2, keepdims=True) > 0.5
        filled = jnp.where(has_row, filled_vis, mask_full.astype(jnp.float32)[None, None, :])
        filled = filled.astype(jnp.bfloat16)
        decoded = lax.all_to_all(filled, AX, split_axis=1, concat_axis=0, tiled=True)
        grad_full = lax.all_to_all(cot_decoded, AX, split_axis=0, concat_axis=1, tiled=True)

        grad_vis_low = (
            jnp.einsum("csi,cse->cie", one_hot, grad_full, preferred_element_type=jnp.float32)
            .astype(jnp.bfloat16)
            .reshape(row_count, DEC)
        )
        grad_vis = grad_vis_low.astype(jnp.float32)
        grad_mask_token = jnp.sum(
            jnp.where(has_row, 0.0, grad_full.astype(jnp.float32)), axis=(0, 1)
        )
        grad_dec_bias = jnp.sum(grad_vis, axis=0)
        grad_dec_weight = inner_rows(enc_low, grad_vis_low)
        grad_res_two = outer_cols(grad_vis_low, dec_full)
        grad_ffo = grad_res_two.astype(jnp.bfloat16)
        grad_mlp_out_bias = jnp.sum(grad_ffo.astype(jnp.float32), axis=0)
        grad_mlp_out = inner_rows(active, grad_ffo)
        grad_hidden = (outer_cols(grad_ffo, outer_full) * gelu_slope(hidden)).astype(jnp.bfloat16)
        grad_mlp_in_bias = jnp.sum(grad_hidden.astype(jnp.float32), axis=0)
        grad_mlp_in = inner_rows(act_two, grad_hidden)
        grad_act_two = outer_cols(grad_hidden, inner_full)
        grad_norm_two, grad_norm2_gain, grad_norm2_bias = norm_backward(
            grad_act_two, normed_two, inverse_two, gain_two.astype(jnp.float32)
        )
        grad_res_one = grad_res_two + grad_norm_two
        grad_att = grad_res_one.astype(jnp.bfloat16)
        grad_out_weight = inner_rows(mixture, grad_att)
        grad_mixed = outer_cols(grad_att, out_full).astype(jnp.bfloat16).reshape(head_shape)
        grad_queries, grad_keys, grad_values = attend_back(
            queries, key_rows, value_rows, soft_full, soft_low, grad_mixed
        )
        grad_qkv = jnp.concatenate(
            [
                grad_queries.reshape(row_count, D),
                grad_keys.reshape(row_count, D),
                grad_values.reshape(row_count, D),
            ],
            axis=1,
        ).astype(jnp.bfloat16)
        grad_qkv_weight = inner_rows(act_one, grad_qkv)
        grad_act_one = outer_cols(grad_qkv, qkv_full)
        grad_norm_one, grad_norm1_gain, grad_norm1_bias = norm_backward(
            grad_act_one, normed_one, inverse_one, gain_one.astype(jnp.float32)
        )
        grad_tokens = (grad_res_one + grad_norm_one).reshape(chip_count, vis_len, D)
        chip_sums = jnp.sum(grad_tokens, axis=1)
        grad_wave_table = lax.dot_general(
            counts, chip_sums, (((0,), (0,)), ((), ())), precision=HIGH_PRECISION
        )
        small_grads = (grad_wave_table, grad_norm1_gain, grad_norm1_bias, grad_norm2_gain,
                       grad_norm2_bias, grad_mlp_in_bias, grad_mlp_out_bias, grad_dec_bias,
                       grad_mask_token)
        packed_sg, sg_widths = pack_rows(small_grads, n_dev, jnp.float32)
        reduced_sg = rs_chain(packed_sg, n_bits, orders["yz"])
        (sum_wave, sum_g1, sum_b1, sum_g2, sum_b2, sum_ib, sum_ob, sum_db,
         sum_mask) = unpack_rows(reduced_sg, small_grads, sg_widths, n_dev, 1)
        sum_dec = rs_chain(grad_dec_weight, n_bits, orders["y"])
        sum_mlp_out = rs_chain(grad_mlp_out, n_bits, orders["x"])
        sum_mlp_in = rs_chain(grad_mlp_in, n_bits, orders["y"])
        sum_out = rs_chain(grad_out_weight, n_bits, orders["x"])
        sum_qkv = rs_chain(grad_qkv_weight, n_bits, orders["yz"])
        summed = (sum_wave, sum_g1, sum_b1, sum_qkv, sum_out, sum_g2, sum_b2, sum_mlp_in,
                  sum_ib, sum_mlp_out, sum_ob, sum_dec, sum_db, sum_mask)
        return (decoded, grad_tokens, *summed)

    return local


def solution(mesh):
    n_dev = mesh.devices.size
    n_bits = n_dev.bit_length() - 1
    order = halving_order(n_bits, core_bit_of(mesh))
    orders = chain_orders(*bit_groups(mesh))
    placed = (
        P(AX, None, None),
        P(AX, None),
        P(AX, None),
        P(AX, None),
        P(AX),
        P(AX),
        P(AX, None),
        P(AX, None),
        P(AX),
        P(AX),
        P(AX, None),
        P(AX),
        P(AX, None),
        P(AX),
        P(AX, None),
        P(AX),
        P(AX),
        P(None, AX, None),
    )
    return jax.shard_map(
        make_local(n_bits, order, orders),
        mesh=mesh,
        in_specs=placed,
        out_specs=(
            P(None, AX, None),
            P(AX, None, None),
            P(AX, None),
            P(AX),
            P(AX),
            P(AX, None),
            P(AX, None),
            P(AX),
            P(AX),
            P(AX, None),
            P(AX),
            P(AX, None),
            P(AX),
            P(AX, None),
            P(AX),
            P(AX),
        ),
        check_vma=False,
    )
```

```python
import numpy as np
import jax
import jax.numpy as jnp
from jax import lax
from jax.sharding import PartitionSpec as P

D = 768
HD = 64
DEC = 512
WAVES = 128
L = 1024

NORM_EPSILON = 1e-05
ROOT_HALF = 0.7071067811865476
INVERSE_ROOT_TAU = 0.3989422804014327
HIGH_PRECISION = lax.Precision.HIGHEST
AX = ("dp", "fsdp")


def product(left_op, right_op):
    return jnp.dot(left_op, right_op, preferred_element_type=jnp.float32)


def inner_rows(left_op, right_op):
    return lax.dot_general(
        left_op, right_op, (((0,), (0,)), ((), ())), preferred_element_type=jnp.float32
    )


def outer_cols(left_op, right_op):
    return lax.dot_general(
        left_op, right_op, (((1,), (1,)), ((), ())), preferred_element_type=jnp.float32
    )


def norm_forward(residual, gain, shift):
    mean_val = jnp.mean(residual, axis=-1, keepdims=True)
    centered = residual - mean_val
    variance = jnp.mean(centered * centered, axis=-1, keepdims=True)
    inverse = lax.rsqrt(variance + NORM_EPSILON)
    normed = centered * inverse
    return (normed * gain + shift, normed, inverse)


def norm_backward(incoming, normed, inverse, gain):
    scaled = incoming * gain
    first_mean = jnp.mean(scaled, axis=-1, keepdims=True)
    second_mean = jnp.mean(scaled * normed, axis=-1, keepdims=True)
    grad_input = inverse * (scaled - first_mean - normed * second_mean)
    return (grad_input, jnp.sum(incoming * normed, axis=0), jnp.sum(incoming, axis=0))


def gelu_value(hidden):
    return 0.5 * hidden * (1.0 + lax.erf(hidden * ROOT_HALF))


def gelu_slope(hidden):
    return (
        0.5 * (1.0 + lax.erf(hidden * ROOT_HALF))
        + hidden * jnp.exp(-0.5 * hidden * hidden) * INVERSE_ROOT_TAU
    )


def core_bit_of(mesh):
    flat = list(mesh.devices.reshape(-1))
    cores = [d.core_on_chip for d in flat]
    stride = 1
    while stride < len(flat) and cores[stride] == cores[0]:
        stride *= 2
    return stride.bit_length() - 1


def bit_groups(mesh):
    flat = list(mesh.devices.reshape(-1))
    n_bits = len(flat).bit_length() - 1
    first = flat[0]
    core_bit = None
    groups = {}
    for bit in range(n_bits):
        other = flat[1 << bit]
        if other.core_on_chip != first.core_on_chip:
            core_bit = bit
            continue
        axis = [a for a in range(len(first.coords)) if first.coords[a] != other.coords[a]]
        groups.setdefault(axis[0] if axis else -1, []).append(bit)
    return core_bit, [sorted(bits) for _, bits in sorted(groups.items())]


def chain_orders(core_bit, groups):
    head = [] if core_bit is None else [core_bit]
    if len(groups) < 3:
        flat = head + [b for g in reversed(groups) for b in g]
        return {"y": flat, "x": flat, "yz": flat}
    x_bits, y_bits, z_bits = groups[0], groups[1], [b for g in groups[2:] for b in g]
    return {
        "y": head + y_bits + x_bits + z_bits,
        "x": head + x_bits + y_bits + z_bits,
        "yz": head + y_bits + z_bits + x_bits,
    }


def halving_order(n_bits, core_bit):
    rest = [b for b in reversed(range(n_bits)) if b != core_bit]
    if len(rest) >= 2:
        rest[-2:] = rest[-2:][::-1]
    return [core_bit] + rest


def rs_chain(grad, n_bits, order):
    n_dev = 2 ** n_bits
    me = lax.axis_index(AX)
    rows = grad.shape[0] // n_dev
    current = grad.reshape((2,) * n_bits + (rows,) + grad.shape[1:])
    for bit in order:
        axis = n_bits - 1 - bit
        mine = (me >> bit) & 1
        keep = lax.dynamic_slice_in_dim(current, mine, 1, axis=axis)
        send = lax.dynamic_slice_in_dim(current, 1 - mine, 1, axis=axis)
        moved = lax.ppermute(
            send.astype(jnp.bfloat16), AX, [(i, i ^ (1 << bit)) for i in range(n_dev)]
        )
        current = keep + moved.astype(jnp.float32)
    return current.reshape((rows,) + grad.shape[1:])


def ag_chain(block, n_bits, order):
    me = lax.axis_index(AX)
    n_dev = 2 ** n_bits
    current = block.reshape((1,) * n_bits + block.shape)
    for bit in reversed(order):
        axis = n_bits - 1 - bit
        mine = ((me >> bit) & 1) == 1
        moved = lax.ppermute(current, AX, [(i, i ^ (1 << bit)) for i in range(n_dev)])
        low = jnp.where(mine, moved, current)
        high = jnp.where(mine, current, moved)
        current = jnp.concatenate([low, high], axis=axis)
    return current.reshape((n_dev * block.shape[0],) + block.shape[1:])


def pack_rows(arrays, n_dev, dtype):
    flat = [a.reshape(n_dev, -1).astype(dtype) for a in arrays]
    widths = [f.shape[1] for f in flat]
    padded = -sum(widths) % 1024
    flat.append(jnp.zeros((n_dev, padded), dtype))
    packed = jnp.concatenate(flat, axis=1)
    return packed.reshape(n_dev, 8, -1), widths


def unpack_rows(packed, arrays, widths, n_dev, leading):
    flat = packed.reshape(packed.shape[0], -1)
    out = []
    offset = 0
    for a, width in zip(arrays, widths):
        piece = flat[:, offset : offset + width]
        out.append(piece.reshape((leading * a.shape[0] // n_dev,) + a.shape[1:]))
        offset += width
    return out


def attend(queries, key_rows, value_rows):
    score_scale = HD ** (-0.5)
    scores = (
        jnp.einsum("cqhd,ckhd->chqk", queries, key_rows, preferred_element_type=jnp.float32)
        * score_scale
    )
    row_peak = jnp.max(scores, axis=-1, keepdims=True)
    exponents = jnp.exp(scores - row_peak)
    row_total = jnp.sum(exponents, axis=-1, keepdims=True)
    soft_full = exponents / row_total
    soft_low = soft_full.astype(jnp.bfloat16)
    mixture = jnp.einsum(
        "chqk,ckhd->cqhd", soft_low, value_rows, preferred_element_type=jnp.float32
    )
    return mixture.astype(jnp.bfloat16), soft_full, soft_low


def attend_back(queries, key_rows, value_rows, soft_full, soft_low, grad_mixture):
    score_scale = HD ** (-0.5)
    grad_values = jnp.einsum(
        "chqk,cqhd->ckhd", soft_low, grad_mixture, preferred_element_type=jnp.float32
    )
    grad_soft = jnp.einsum(
        "cqhd,ckhd->chqk", grad_mixture, value_rows, preferred_element_type=jnp.float32
    )
    row_delta = jnp.sum(grad_soft * soft_full, axis=-1, keepdims=True)
    grad_scores = (soft_full * (grad_soft - row_delta)).astype(jnp.bfloat16)
    grad_queries = (
        jnp.einsum("chqk,ckhd->cqhd", grad_scores, key_rows, preferred_element_type=jnp.float32)
        * score_scale
    )
    grad_keys = (
        jnp.einsum("chqk,cqhd->ckhd", grad_scores, queries, preferred_element_type=jnp.float32)
        * score_scale
    )
    return grad_queries, grad_keys, grad_values


def make_local(n_bits, order, orders):
    n_dev = 2 ** n_bits

    def local(
        tokens,
        band_waves,
        visible_slot,
        wave_table,
        norm1_gain,
        norm1_bias,
        qkv_weight,
        out_weight,
        norm2_gain,
        norm2_bias,
        mlp_in,
        mlp_in_bias,
        mlp_out,
        mlp_out_bias,
        dec_weight,
        dec_bias,
        mask_token,
        cot_decoded,
    ):
        shards = (
            wave_table,
            norm1_gain,
            norm1_bias,
            qkv_weight,
            out_weight,
            norm2_gain,
            norm2_bias,
            mlp_in,
            mlp_in_bias,
            mlp_out,
            mlp_out_bias,
            dec_weight,
            dec_bias,
            mask_token,
        )
        small = (wave_table, norm1_gain, norm1_bias, norm2_gain, norm2_bias, mlp_in_bias,
                 mlp_out_bias, dec_bias, mask_token, dec_weight)
        packed_small, small_widths = pack_rows(
            [a.reshape(1, -1) for a in small], 1, jnp.bfloat16
        )
        gathered_small = ag_chain(packed_small, n_bits, orders["x"])
        (wave_full, gain_one, shift_one, gain_two, shift_two, inner_bias, outer_bias,
         dec_shift, mask_full, dec_full) = unpack_rows(gathered_small, small, small_widths, 1, n_dev)
        wide = (qkv_weight, out_weight, mlp_in)
        wide_cols = [a.shape[1] for a in wide]
        gathered_wide = lax.all_gather(jnp.concatenate(wide, axis=1), AX, axis=0, tiled=True)
        wide_full = []
        offset = 0
        for cols in wide_cols:
            wide_full.append(gathered_wide[:, offset : offset + cols])
            offset += cols
        qkv_full, out_full, inner_full = wide_full
        outer_full = lax.all_gather(mlp_out, AX, axis=0, tiled=True)

        chip_count, vis_len, feature_width = tokens.shape
        row_count = chip_count * vis_len
        heads = feature_width // HD
        counts = jnp.sum(
            (band_waves[:, :, None] == jnp.arange(WAVES, dtype=jnp.int32)[None, None, :]).astype(
                jnp.float32
            ),
            axis=1,
        )
        spectral = jnp.dot(
            counts.astype(jnp.bfloat16), wave_full, preferred_element_type=jnp.float32
        )
        residual = (tokens.astype(jnp.float32) + spectral[:, None, :]).reshape(row_count, D)
        norm_out_one, normed_one, inverse_one = norm_forward(
            residual, gain_one.astype(jnp.float32), shift_one.astype(jnp.float32)
        )
        act_one = norm_out_one.astype(jnp.bfloat16)
        qkv_vals = product(act_one, qkv_full).astype(jnp.bfloat16)
        head_shape = (chip_count, vis_len, heads, HD)
        queries = qkv_vals[:, :D].reshape(head_shape)
        key_rows = qkv_vals[:, D : 2 * D].reshape(head_shape)
        value_rows = qkv_vals[:, 2 * D :].reshape(head_shape)
        mixture4, soft_full, soft_low = attend(queries, key_rows, value_rows)
        mixture = mixture4.reshape(row_count, D)
        res_one = residual + product(mixture, out_full)
        norm_out_two, normed_two, inverse_two = norm_forward(
            res_one, gain_two.astype(jnp.float32), shift_two.astype(jnp.float32)
        )
        act_two = norm_out_two.astype(jnp.bfloat16)
        hidden = product(act_two, inner_full) + inner_bias.astype(jnp.float32)
        active = gelu_value(hidden).astype(jnp.bfloat16)
        res_two = res_one + (product(active, outer_full) + outer_bias.astype(jnp.float32))
        enc_low = res_two.astype(jnp.bfloat16)
        projected = (product(enc_low, dec_full) + dec_shift.astype(jnp.float32)).astype(
            jnp.bfloat16
        )
        slot_ids = jnp.arange(L, dtype=jnp.int32)
        one_hot = (visible_slot[:, None, :] == slot_ids[None, :, None]).astype(jnp.bfloat16)
        filled_vis = jnp.einsum(
            "csi,cie->cse",
            one_hot,
            projected.reshape(chip_count, vis_len, DEC),
            preferred_element_type=jnp.float32,
        )
        has_row = jnp.sum(one_hot.astype(jnp.float32), axis=2, keepdims=True) > 0.5
        filled = jnp.where(has_row, filled_vis, mask_full.astype(jnp.float32)[None, None, :])
        filled = filled.astype(jnp.bfloat16)
        decoded = lax.all_to_all(filled, AX, split_axis=1, concat_axis=0, tiled=True)
        grad_full = lax.all_to_all(cot_decoded, AX, split_axis=0, concat_axis=1, tiled=True)

        grad_vis_low = (
            jnp.einsum("csi,cse->cie", one_hot, grad_full, preferred_element_type=jnp.float32)
            .astype(jnp.bfloat16)
            .reshape(row_count, DEC)
        )
        grad_vis = grad_vis_low.astype(jnp.float32)
        grad_mask_token = jnp.sum(
            jnp.where(has_row, 0.0, grad_full.astype(jnp.float32)), axis=(0, 1)
        )
        grad_dec_bias = jnp.sum(grad_vis, axis=0)
        grad_dec_weight = inner_rows(enc_low, grad_vis_low)
        grad_res_two = outer_cols(grad_vis_low, dec_full)
        grad_ffo = grad_res_two.astype(jnp.bfloat16)
        grad_mlp_out_bias = jnp.sum(grad_ffo.astype(jnp.float32), axis=0)
        grad_mlp_out = inner_rows(active, grad_ffo)
        grad_hidden = (outer_cols(grad_ffo, outer_full) * gelu_slope(hidden)).astype(jnp.bfloat16)
        grad_mlp_in_bias = jnp.sum(grad_hidden.astype(jnp.float32), axis=0)
        grad_mlp_in = inner_rows(act_two, grad_hidden)
        grad_act_two = outer_cols(grad_hidden, inner_full)
        grad_norm_two, grad_norm2_gain, grad_norm2_bias = norm_backward(
            grad_act_two, normed_two, inverse_two, gain_two.astype(jnp.float32)
        )
        grad_res_one = grad_res_two + grad_norm_two
        grad_att = grad_res_one.astype(jnp.bfloat16)
        grad_out_weight = inner_rows(mixture, grad_att)
        grad_mixed = outer_cols(grad_att, out_full).astype(jnp.bfloat16).reshape(head_shape)
        grad_queries, grad_keys, grad_values = attend_back(
            queries, key_rows, value_rows, soft_full, soft_low, grad_mixed
        )
        grad_qkv = jnp.concatenate(
            [
                grad_queries.reshape(row_count, D),
                grad_keys.reshape(row_count, D),
                grad_values.reshape(row_count, D),
            ],
            axis=1,
        ).astype(jnp.bfloat16)
        grad_qkv_weight = inner_rows(act_one, grad_qkv)
        grad_act_one = outer_cols(grad_qkv, qkv_full)
        grad_norm_one, grad_norm1_gain, grad_norm1_bias = norm_backward(
            grad_act_one, normed_one, inverse_one, gain_one.astype(jnp.float32)
        )
        grad_tokens = (grad_res_one + grad_norm_one).reshape(chip_count, vis_len, D)
        chip_sums = jnp.sum(grad_tokens, axis=1)
        grad_wave_table = lax.dot_general(
            counts, chip_sums, (((0,), (0,)), ((), ())), precision=HIGH_PRECISION
        )
        small_grads = (grad_wave_table, grad_norm1_gain, grad_norm1_bias, grad_norm2_gain,
                       grad_norm2_bias, grad_mlp_in_bias, grad_mlp_out_bias, grad_dec_bias,
                       grad_mask_token)
        packed_sg, sg_widths = pack_rows(small_grads, n_dev, jnp.float32)
        reduced_sg = rs_chain(packed_sg, n_bits, orders["yz"])
        (sum_wave, sum_g1, sum_b1, sum_g2, sum_b2, sum_ib, sum_ob, sum_db,
         sum_mask) = unpack_rows(reduced_sg, small_grads, sg_widths, n_dev, 1)
        sum_dec = rs_chain(grad_dec_weight, n_bits, orders["y"])
        sum_mlp_out = rs_chain(grad_mlp_out, n_bits, orders["x"])
        sum_mlp_in = rs_chain(grad_mlp_in, n_bits, orders["y"])
        sum_out = rs_chain(grad_out_weight, n_bits, orders["x"])
        sum_qkv = rs_chain(grad_qkv_weight, n_bits, orders["yz"])
        summed = (sum_wave, sum_g1, sum_b1, sum_qkv, sum_out, sum_g2, sum_b2, sum_mlp_in,
                  sum_ib, sum_mlp_out, sum_ob, sum_dec, sum_db, sum_mask)
        return (decoded, grad_tokens, *summed)

    return local


def solution(mesh):
    n_dev = mesh.devices.size
    n_bits = n_dev.bit_length() - 1
    order = halving_order(n_bits, core_bit_of(mesh))
    orders = chain_orders(*bit_groups(mesh))
    placed = (
        P(AX, None, None),
        P(AX, None),
        P(AX, None),
        P(AX, None),
        P(AX),
        P(AX),
        P(AX, None),
        P(AX, None),
        P(AX),
        P(AX),
        P(AX, None),
        P(AX),
        P(AX, None),
        P(AX),
        P(AX, None),
        P(AX),
        P(AX),
        P(None, AX, None),
    )
    return jax.shard_map(
        make_local(n_bits, order, orders),
        mesh=mesh,
        in_specs=placed,
        out_specs=(
            P(None, AX, None),
            P(AX, None, None),
            P(AX, None),
            P(AX),
            P(AX),
            P(AX, None),
            P(AX, None),
            P(AX),
            P(AX),
            P(AX, None),
            P(AX),
            P(AX, None),
            P(AX),
            P(AX, None),
            P(AX),
            P(AX),
        ),
        check_vma=False,
    )
```

```python
import numpy as np
import jax
import jax.numpy as jnp
from jax import lax
from jax.sharding import PartitionSpec as P

D = 768
HD = 64
DEC = 512
WAVES = 128
L = 1024

NORM_EPSILON = 1e-05
ROOT_HALF = 0.7071067811865476
INVERSE_ROOT_TAU = 0.3989422804014327
HIGH_PRECISION = lax.Precision.HIGHEST
AX = ("dp", "fsdp")


def product(left_op, right_op):
    return jnp.dot(left_op, right_op, preferred_element_type=jnp.float32)


def inner_rows(left_op, right_op):
    return lax.dot_general(
        left_op, right_op, (((0,), (0,)), ((), ())), preferred_element_type=jnp.float32
    )


def outer_cols(left_op, right_op):
    return lax.dot_general(
        left_op, right_op, (((1,), (1,)), ((), ())), preferred_element_type=jnp.float32
    )


def norm_forward(residual, gain, shift):
    mean_val = jnp.mean(residual, axis=-1, keepdims=True)
    centered = residual - mean_val
    variance = jnp.mean(centered * centered, axis=-1, keepdims=True)
    inverse = lax.rsqrt(variance + NORM_EPSILON)
    normed = centered * inverse
    return (normed * gain + shift, normed, inverse)


def norm_backward(incoming, normed, inverse, gain):
    scaled = incoming * gain
    first_mean = jnp.mean(scaled, axis=-1, keepdims=True)
    second_mean = jnp.mean(scaled * normed, axis=-1, keepdims=True)
    grad_input = inverse * (scaled - first_mean - normed * second_mean)
    return (grad_input, jnp.sum(incoming * normed, axis=0), jnp.sum(incoming, axis=0))


def gelu_value(hidden):
    return 0.5 * hidden * (1.0 + lax.erf(hidden * ROOT_HALF))


def gelu_slope(hidden):
    return (
        0.5 * (1.0 + lax.erf(hidden * ROOT_HALF))
        + hidden * jnp.exp(-0.5 * hidden * hidden) * INVERSE_ROOT_TAU
    )


def core_bit_of(mesh):
    flat = list(mesh.devices.reshape(-1))
    cores = [d.core_on_chip for d in flat]
    stride = 1
    while stride < len(flat) and cores[stride] == cores[0]:
        stride *= 2
    return stride.bit_length() - 1


def bit_groups(mesh):
    flat = list(mesh.devices.reshape(-1))
    n_bits = len(flat).bit_length() - 1
    first = flat[0]
    core_bit = None
    groups = {}
    for bit in range(n_bits):
        other = flat[1 << bit]
        if other.core_on_chip != first.core_on_chip:
            core_bit = bit
            continue
        axis = [a for a in range(len(first.coords)) if first.coords[a] != other.coords[a]]
        groups.setdefault(axis[0] if axis else -1, []).append(bit)
    return core_bit, [sorted(bits) for _, bits in sorted(groups.items())]


def chain_orders(core_bit, groups):
    head = [] if core_bit is None else [core_bit]
    if len(groups) < 3:
        flat = head + [b for g in reversed(groups) for b in g]
        return {"y": flat, "x": flat, "yz": flat}
    x_bits, y_bits, z_bits = groups[0], groups[1], [b for g in groups[2:] for b in g]
    return {
        "y": head + y_bits + x_bits + z_bits,
        "x": head + x_bits + y_bits + z_bits,
        "yz": head + y_bits + z_bits + x_bits,
    }


def halving_order(n_bits, core_bit):
    rest = [b for b in reversed(range(n_bits)) if b != core_bit]
    if len(rest) >= 2:
        rest[-2:] = rest[-2:][::-1]
    return [core_bit] + rest


def rs_chain(grad, n_bits, order):
    n_dev = 2 ** n_bits
    me = lax.axis_index(AX)
    rows = grad.shape[0] // n_dev
    current = grad.reshape((2,) * n_bits + (rows,) + grad.shape[1:])
    for bit in order:
        axis = n_bits - 1 - bit
        mine = (me >> bit) & 1
        keep = lax.dynamic_slice_in_dim(current, mine, 1, axis=axis)
        send = lax.dynamic_slice_in_dim(current, 1 - mine, 1, axis=axis)
        moved = lax.ppermute(
            send.astype(jnp.bfloat16), AX, [(i, i ^ (1 << bit)) for i in range(n_dev)]
        )
        current = keep + moved.astype(jnp.float32)
    return current.reshape((rows,) + grad.shape[1:])


def ag_chain(block, n_bits, order):
    me = lax.axis_index(AX)
    n_dev = 2 ** n_bits
    current = block.reshape((1,) * n_bits + block.shape)
    for bit in reversed(order):
        axis = n_bits - 1 - bit
        mine = ((me >> bit) & 1) == 1
        moved = lax.ppermute(current, AX, [(i, i ^ (1 << bit)) for i in range(n_dev)])
        low = jnp.where(mine, moved, current)
        high = jnp.where(mine, current, moved)
        current = jnp.concatenate([low, high], axis=axis)
    return current.reshape((n_dev * block.shape[0],) + block.shape[1:])


def pack_rows(arrays, n_dev, dtype):
    flat = [a.reshape(n_dev, -1).astype(dtype) for a in arrays]
    widths = [f.shape[1] for f in flat]
    padded = -sum(widths) % 1024
    flat.append(jnp.zeros((n_dev, padded), dtype))
    packed = jnp.concatenate(flat, axis=1)
    return packed.reshape(n_dev, 8, -1), widths


def unpack_rows(packed, arrays, widths, n_dev, leading):
    flat = packed.reshape(packed.shape[0], -1)
    out = []
    offset = 0
    for a, width in zip(arrays, widths):
        piece = flat[:, offset : offset + width]
        out.append(piece.reshape((leading * a.shape[0] // n_dev,) + a.shape[1:]))
        offset += width
    return out


def attend(queries, key_rows, value_rows):
    score_scale = HD ** (-0.5)
    scores = (
        jnp.einsum("cqhd,ckhd->chqk", queries, key_rows, preferred_element_type=jnp.float32)
        * score_scale
    )
    row_peak = jnp.max(scores, axis=-1, keepdims=True)
    exponents = jnp.exp(scores - row_peak)
    row_total = jnp.sum(exponents, axis=-1, keepdims=True)
    soft_full = exponents / row_total
    soft_low = soft_full.astype(jnp.bfloat16)
    mixture = jnp.einsum(
        "chqk,ckhd->cqhd", soft_low, value_rows, preferred_element_type=jnp.float32
    )
    return mixture.astype(jnp.bfloat16), soft_full, soft_low


def attend_back(queries, key_rows, value_rows, soft_full, soft_low, grad_mixture):
    score_scale = HD ** (-0.5)
    grad_values = jnp.einsum(
        "chqk,cqhd->ckhd", soft_low, grad_mixture, preferred_element_type=jnp.float32
    )
    grad_soft = jnp.einsum(
        "cqhd,ckhd->chqk", grad_mixture, value_rows, preferred_element_type=jnp.float32
    )
    row_delta = jnp.sum(grad_soft * soft_full, axis=-1, keepdims=True)
    grad_scores = (soft_full * (grad_soft - row_delta)).astype(jnp.bfloat16)
    grad_queries = (
        jnp.einsum("chqk,ckhd->cqhd", grad_scores, key_rows, preferred_element_type=jnp.float32)
        * score_scale
    )
    grad_keys = (
        jnp.einsum("chqk,cqhd->ckhd", grad_scores, queries, preferred_element_type=jnp.float32)
        * score_scale
    )
    return grad_queries, grad_keys, grad_values


def make_local(n_bits, order, orders):
    n_dev = 2 ** n_bits

    def local(
        tokens,
        band_waves,
        visible_slot,
        wave_table,
        norm1_gain,
        norm1_bias,
        qkv_weight,
        out_weight,
        norm2_gain,
        norm2_bias,
        mlp_in,
        mlp_in_bias,
        mlp_out,
        mlp_out_bias,
        dec_weight,
        dec_bias,
        mask_token,
        cot_decoded,
    ):
        shards = (
            wave_table,
            norm1_gain,
            norm1_bias,
            qkv_weight,
            out_weight,
            norm2_gain,
            norm2_bias,
            mlp_in,
            mlp_in_bias,
            mlp_out,
            mlp_out_bias,
            dec_weight,
            dec_bias,
            mask_token,
        )
        small = (wave_table, norm1_gain, norm1_bias, norm2_gain, norm2_bias, mlp_in_bias,
                 mlp_out_bias, dec_bias, mask_token)
        packed_small, small_widths = pack_rows(
            [a.reshape(1, -1) for a in small], 1, jnp.bfloat16
        )
        gathered_small = ag_chain(packed_small, n_bits, orders["x"])
        (wave_full, gain_one, shift_one, gain_two, shift_two, inner_bias, outer_bias,
         dec_shift, mask_full) = unpack_rows(gathered_small, small, small_widths, 1, n_dev)
        wide = (qkv_weight, out_weight, mlp_in, dec_weight)
        wide_cols = [a.shape[1] for a in wide]
        gathered_wide = lax.all_gather(jnp.concatenate(wide, axis=1), AX, axis=0, tiled=True)
        wide_full = []
        offset = 0
        for cols in wide_cols:
            wide_full.append(gathered_wide[:, offset : offset + cols])
            offset += cols
        qkv_full, out_full, inner_full, dec_full = wide_full
        outer_full = lax.all_gather(mlp_out, AX, axis=0, tiled=True)

        chip_count, vis_len, feature_width = tokens.shape
        row_count = chip_count * vis_len
        heads = feature_width // HD
        counts = jnp.sum(
            (band_waves[:, :, None] == jnp.arange(WAVES, dtype=jnp.int32)[None, None, :]).astype(
                jnp.float32
            ),
            axis=1,
        )
        spectral = jnp.dot(
            counts.astype(jnp.bfloat16), wave_full, preferred_element_type=jnp.float32
        )
        residual = (tokens.astype(jnp.float32) + spectral[:, None, :]).reshape(row_count, D)
        norm_out_one, normed_one, inverse_one = norm_forward(
            residual, gain_one.astype(jnp.float32), shift_one.astype(jnp.float32)
        )
        act_one = norm_out_one.astype(jnp.bfloat16)
        qkv_vals = product(act_one, qkv_full).astype(jnp.bfloat16)
        head_shape = (chip_count, vis_len, heads, HD)
        queries = qkv_vals[:, :D].reshape(head_shape)
        key_rows = qkv_vals[:, D : 2 * D].reshape(head_shape)
        value_rows = qkv_vals[:, 2 * D :].reshape(head_shape)
        mixture4, soft_full, soft_low = attend(queries, key_rows, value_rows)
        mixture = mixture4.reshape(row_count, D)
        res_one = residual + product(mixture, out_full)
        norm_out_two, normed_two, inverse_two = norm_forward(
            res_one, gain_two.astype(jnp.float32), shift_two.astype(jnp.float32)
        )
        act_two = norm_out_two.astype(jnp.bfloat16)
        hidden = product(act_two, inner_full) + inner_bias.astype(jnp.float32)
        active = gelu_value(hidden).astype(jnp.bfloat16)
        res_two = res_one + (product(active, outer_full) + outer_bias.astype(jnp.float32))
        enc_low = res_two.astype(jnp.bfloat16)
        projected = (product(enc_low, dec_full) + dec_shift.astype(jnp.float32)).astype(
            jnp.bfloat16
        )
        slot_ids = jnp.arange(L, dtype=jnp.int32)
        one_hot = (visible_slot[:, None, :] == slot_ids[None, :, None]).astype(jnp.bfloat16)
        filled_vis = jnp.einsum(
            "csi,cie->cse",
            one_hot,
            projected.reshape(chip_count, vis_len, DEC),
            preferred_element_type=jnp.float32,
        )
        has_row = jnp.sum(one_hot.astype(jnp.float32), axis=2, keepdims=True) > 0.5
        filled = jnp.where(has_row, filled_vis, mask_full.astype(jnp.float32)[None, None, :])
        filled = filled.astype(jnp.bfloat16)
        decoded = lax.all_to_all(filled, AX, split_axis=1, concat_axis=0, tiled=True)
        grad_full = lax.all_to_all(cot_decoded, AX, split_axis=0, concat_axis=1, tiled=True)

        grad_vis_low = (
            jnp.einsum("csi,cse->cie", one_hot, grad_full, preferred_element_type=jnp.float32)
            .astype(jnp.bfloat16)
            .reshape(row_count, DEC)
        )
        grad_vis = grad_vis_low.astype(jnp.float32)
        grad_mask_token = jnp.sum(
            jnp.where(has_row, 0.0, grad_full.astype(jnp.float32)), axis=(0, 1)
        )
        grad_dec_bias = jnp.sum(grad_vis, axis=0)
        grad_dec_weight = inner_rows(enc_low, grad_vis_low)
        grad_res_two = outer_cols(grad_vis_low, dec_full)
        grad_ffo = grad_res_two.astype(jnp.bfloat16)
        grad_mlp_out_bias = jnp.sum(grad_ffo.astype(jnp.float32), axis=0)
        grad_mlp_out = inner_rows(active, grad_ffo)
        grad_hidden = (outer_cols(grad_ffo, outer_full) * gelu_slope(hidden)).astype(jnp.bfloat16)
        grad_mlp_in_bias = jnp.sum(grad_hidden.astype(jnp.float32), axis=0)
        grad_mlp_in = inner_rows(act_two, grad_hidden)
        grad_act_two = outer_cols(grad_hidden, inner_full)
        grad_norm_two, grad_norm2_gain, grad_norm2_bias = norm_backward(
            grad_act_two, normed_two, inverse_two, gain_two.astype(jnp.float32)
        )
        grad_res_one = grad_res_two + grad_norm_two
        grad_att = grad_res_one.astype(jnp.bfloat16)
        grad_out_weight = inner_rows(mixture, grad_att)
        grad_mixed = outer_cols(grad_att, out_full).astype(jnp.bfloat16).reshape(head_shape)
        grad_queries, grad_keys, grad_values = attend_back(
            queries, key_rows, value_rows, soft_full, soft_low, grad_mixed
        )
        grad_qkv = jnp.concatenate(
            [
                grad_queries.reshape(row_count, D),
                grad_keys.reshape(row_count, D),
                grad_values.reshape(row_count, D),
            ],
            axis=1,
        ).astype(jnp.bfloat16)
        grad_qkv_weight = inner_rows(act_one, grad_qkv)
        grad_act_one = outer_cols(grad_qkv, qkv_full)
        grad_norm_one, grad_norm1_gain, grad_norm1_bias = norm_backward(
            grad_act_one, normed_one, inverse_one, gain_one.astype(jnp.float32)
        )
        grad_tokens = (grad_res_one + grad_norm_one).reshape(chip_count, vis_len, D)
        chip_sums = jnp.sum(grad_tokens, axis=1)
        grad_wave_table = lax.dot_general(
            counts, chip_sums, (((0,), (0,)), ((), ())), precision=HIGH_PRECISION
        )
        small_grads = (grad_wave_table, grad_norm1_gain, grad_norm1_bias, grad_norm2_gain,
                       grad_norm2_bias, grad_mlp_in_bias, grad_mlp_out_bias, grad_dec_bias,
                       grad_mask_token)
        rows_block = grad_out_weight.shape[0] // n_dev
        sg_flat = [g.reshape(n_dev, -1) for g in small_grads]
        sg_widths = [f.shape[1] for f in sg_flat]
        sg_cols = -(-sum(sg_widths) // (rows_block * 128)) * 128
        sg_pad = rows_block * sg_cols - sum(sg_widths)
        sg_block = jnp.concatenate(
            sg_flat + [jnp.zeros((n_dev, sg_pad), jnp.float32)], axis=1
        ).reshape(n_dev * rows_block, sg_cols)
        joined = jnp.concatenate([grad_out_weight, grad_dec_weight, sg_block], axis=1)
        reduced_joined = rs_chain(joined, n_bits, orders["yz"])
        out_cols = grad_out_weight.shape[1]
        dec_cols = grad_dec_weight.shape[1]
        sum_out = reduced_joined[:, :out_cols]
        sum_dec = reduced_joined[:, out_cols : out_cols + dec_cols]
        sg_sum = reduced_joined[:, out_cols + dec_cols :].reshape(-1)
        sg_parts = []
        offset = 0
        for g, width in zip(small_grads, sg_widths):
            sg_parts.append(sg_sum[offset : offset + width].reshape((g.shape[0] // n_dev,) + g.shape[1:]))
            offset += width
        (sum_wave, sum_g1, sum_b1, sum_g2, sum_b2, sum_ib, sum_ob, sum_db, sum_mask) = sg_parts
        sum_mlp_out = rs_chain(grad_mlp_out, n_bits, orders["x"])
        sum_mlp_in = rs_chain(grad_mlp_in, n_bits, orders["y"])
        sum_qkv = rs_chain(grad_qkv_weight, n_bits, orders["yz"])
        summed = (sum_wave, sum_g1, sum_b1, sum_qkv, sum_out, sum_g2, sum_b2, sum_mlp_in,
                  sum_ib, sum_mlp_out, sum_ob, sum_dec, sum_db, sum_mask)
        return (decoded, grad_tokens, *summed)

    return local


def solution(mesh):
    n_dev = mesh.devices.size
    n_bits = n_dev.bit_length() - 1
    order = halving_order(n_bits, core_bit_of(mesh))
    orders = chain_orders(*bit_groups(mesh))
    placed = (
        P(AX, None, None),
        P(AX, None),
        P(AX, None),
        P(AX, None),
        P(AX),
        P(AX),
        P(AX, None),
        P(AX, None),
        P(AX),
        P(AX),
        P(AX, None),
        P(AX),
        P(AX, None),
        P(AX),
        P(AX, None),
        P(AX),
        P(AX),
        P(None, AX, None),
    )
    return jax.shard_map(
        make_local(n_bits, order, orders),
        mesh=mesh,
        in_specs=placed,
        out_specs=(
            P(None, AX, None),
            P(AX, None, None),
            P(AX, None),
            P(AX),
            P(AX),
            P(AX, None),
            P(AX, None),
            P(AX),
            P(AX),
            P(AX, None),
            P(AX),
            P(AX, None),
            P(AX),
            P(AX, None),
            P(AX),
            P(AX),
        ),
        check_vma=False,
    )
```

```python
import numpy as np
import jax
import jax.numpy as jnp
from jax import lax
from jax.sharding import PartitionSpec as P

D = 768
HD = 64
DEC = 512
WAVES = 128
L = 1024

NORM_EPSILON = 1e-05
ROOT_HALF = 0.7071067811865476
INVERSE_ROOT_TAU = 0.3989422804014327
HIGH_PRECISION = lax.Precision.HIGHEST
AX = ("dp", "fsdp")


def product(left_op, right_op):
    return jnp.dot(left_op, right_op, preferred_element_type=jnp.float32)


def inner_rows(left_op, right_op):
    return lax.dot_general(
        left_op, right_op, (((0,), (0,)), ((), ())), preferred_element_type=jnp.float32
    )


def outer_cols(left_op, right_op):
    return lax.dot_general(
        left_op, right_op, (((1,), (1,)), ((), ())), preferred_element_type=jnp.float32
    )


def norm_forward(residual, gain, shift):
    mean_val = jnp.mean(residual, axis=-1, keepdims=True)
    centered = residual - mean_val
    variance = jnp.mean(centered * centered, axis=-1, keepdims=True)
    inverse = lax.rsqrt(variance + NORM_EPSILON)
    normed = centered * inverse
    return (normed * gain + shift, normed, inverse)


def norm_backward(incoming, normed, inverse, gain):
    scaled = incoming * gain
    first_mean = jnp.mean(scaled, axis=-1, keepdims=True)
    second_mean = jnp.mean(scaled * normed, axis=-1, keepdims=True)
    grad_input = inverse * (scaled - first_mean - normed * second_mean)
    return (grad_input, jnp.sum(incoming * normed, axis=0), jnp.sum(incoming, axis=0))


def gelu_value(hidden):
    return 0.5 * hidden * (1.0 + lax.erf(hidden * ROOT_HALF))


def gelu_slope(hidden):
    return (
        0.5 * (1.0 + lax.erf(hidden * ROOT_HALF))
        + hidden * jnp.exp(-0.5 * hidden * hidden) * INVERSE_ROOT_TAU
    )


def core_bit_of(mesh):
    flat = list(mesh.devices.reshape(-1))
    cores = [d.core_on_chip for d in flat]
    stride = 1
    while stride < len(flat) and cores[stride] == cores[0]:
        stride *= 2
    return stride.bit_length() - 1


def bit_groups(mesh):
    flat = list(mesh.devices.reshape(-1))
    n_bits = len(flat).bit_length() - 1
    first = flat[0]
    core_bit = None
    groups = {}
    for bit in range(n_bits):
        other = flat[1 << bit]
        if other.core_on_chip != first.core_on_chip:
            core_bit = bit
            continue
        axis = [a for a in range(len(first.coords)) if first.coords[a] != other.coords[a]]
        groups.setdefault(axis[0] if axis else -1, []).append(bit)
    return core_bit, [sorted(bits) for _, bits in sorted(groups.items())]


def chain_orders(core_bit, groups):
    head = [] if core_bit is None else [core_bit]
    if len(groups) < 3:
        flat = head + [b for g in reversed(groups) for b in g]
        return {"y": flat, "x": flat, "yz": flat}
    x_bits, y_bits, z_bits = groups[0], groups[1], [b for g in groups[2:] for b in g]
    return {
        "y": head + y_bits + x_bits + z_bits,
        "x": head + x_bits + y_bits + z_bits,
        "yz": head + y_bits + z_bits + x_bits,
    }


def halving_order(n_bits, core_bit):
    rest = [b for b in reversed(range(n_bits)) if b != core_bit]
    if len(rest) >= 2:
        rest[-2:] = rest[-2:][::-1]
    return [core_bit] + rest


def rs_chain(grad, n_bits, order):
    n_dev = 2 ** n_bits
    me = lax.axis_index(AX)
    rows = grad.shape[0] // n_dev
    current = grad.reshape((2,) * n_bits + (rows,) + grad.shape[1:])
    for bit in order:
        axis = n_bits - 1 - bit
        mine = (me >> bit) & 1
        keep = lax.dynamic_slice_in_dim(current, mine, 1, axis=axis)
        send = lax.dynamic_slice_in_dim(current, 1 - mine, 1, axis=axis)
        moved = lax.ppermute(
            send.astype(jnp.bfloat16), AX, [(i, i ^ (1 << bit)) for i in range(n_dev)]
        )
        current = keep + moved.astype(jnp.float32)
    return current.reshape((rows,) + grad.shape[1:])


def ag_chain(block, n_bits, order):
    me = lax.axis_index(AX)
    n_dev = 2 ** n_bits
    current = block.reshape((1,) * n_bits + block.shape)
    for bit in reversed(order):
        axis = n_bits - 1 - bit
        mine = ((me >> bit) & 1) == 1
        moved = lax.ppermute(current, AX, [(i, i ^ (1 << bit)) for i in range(n_dev)])
        low = jnp.where(mine, moved, current)
        high = jnp.where(mine, current, moved)
        current = jnp.concatenate([low, high], axis=axis)
    return current.reshape((n_dev * block.shape[0],) + block.shape[1:])


def pack_rows(arrays, n_dev, dtype):
    flat = [a.reshape(n_dev, -1).astype(dtype) for a in arrays]
    widths = [f.shape[1] for f in flat]
    padded = -sum(widths) % 1024
    flat.append(jnp.zeros((n_dev, padded), dtype))
    packed = jnp.concatenate(flat, axis=1)
    return packed.reshape(n_dev, 8, -1), widths


def unpack_rows(packed, arrays, widths, n_dev, leading):
    flat = packed.reshape(packed.shape[0], -1)
    out = []
    offset = 0
    for a, width in zip(arrays, widths):
        piece = flat[:, offset : offset + width]
        out.append(piece.reshape((leading * a.shape[0] // n_dev,) + a.shape[1:]))
        offset += width
    return out


def attend(queries, key_rows, value_rows):
    score_scale = HD ** (-0.5)
    scores = (
        jnp.einsum("cqhd,ckhd->chqk", queries, key_rows, preferred_element_type=jnp.float32)
        * score_scale
    )
    row_peak = jnp.max(scores, axis=-1, keepdims=True)
    exponents = jnp.exp(scores - row_peak)
    row_total = jnp.sum(exponents, axis=-1, keepdims=True)
    soft_full = exponents / row_total
    soft_low = soft_full.astype(jnp.bfloat16)
    mixture = jnp.einsum(
        "chqk,ckhd->cqhd", soft_low, value_rows, preferred_element_type=jnp.float32
    )
    return mixture.astype(jnp.bfloat16), soft_full, soft_low


def attend_back(queries, key_rows, value_rows, soft_full, soft_low, grad_mixture):
    score_scale = HD ** (-0.5)
    grad_values = jnp.einsum(
        "chqk,cqhd->ckhd", soft_low, grad_mixture, preferred_element_type=jnp.float32
    )
    grad_soft = jnp.einsum(
        "cqhd,ckhd->chqk", grad_mixture, value_rows, preferred_element_type=jnp.float32
    )
    row_delta = jnp.sum(grad_soft * soft_full, axis=-1, keepdims=True)
    grad_scores = (soft_full * (grad_soft - row_delta)).astype(jnp.bfloat16)
    grad_queries = (
        jnp.einsum("chqk,ckhd->cqhd", grad_scores, key_rows, preferred_element_type=jnp.float32)
        * score_scale
    )
    grad_keys = (
        jnp.einsum("chqk,cqhd->ckhd", grad_scores, queries, preferred_element_type=jnp.float32)
        * score_scale
    )
    return grad_queries, grad_keys, grad_values


def make_local(n_bits, order, orders):
    n_dev = 2 ** n_bits

    def local(
        tokens,
        band_waves,
        visible_slot,
        wave_table,
        norm1_gain,
        norm1_bias,
        qkv_weight,
        out_weight,
        norm2_gain,
        norm2_bias,
        mlp_in,
        mlp_in_bias,
        mlp_out,
        mlp_out_bias,
        dec_weight,
        dec_bias,
        mask_token,
        cot_decoded,
    ):
        shards = (
            wave_table,
            norm1_gain,
            norm1_bias,
            qkv_weight,
            out_weight,
            norm2_gain,
            norm2_bias,
            mlp_in,
            mlp_in_bias,
            mlp_out,
            mlp_out_bias,
            dec_weight,
            dec_bias,
            mask_token,
        )
        small = (wave_table, norm1_gain, norm1_bias, norm2_gain, norm2_bias, mlp_in_bias,
                 mlp_out_bias, dec_bias, mask_token)
        packed_small, small_widths = pack_rows(
            [a.reshape(1, -1) for a in small], 1, jnp.bfloat16
        )
        gathered_small = ag_chain(packed_small, n_bits, orders["x"])
        (wave_full, gain_one, shift_one, gain_two, shift_two, inner_bias, outer_bias,
         dec_shift, mask_full) = unpack_rows(gathered_small, small, small_widths, 1, n_dev)
        wide = (qkv_weight, out_weight, mlp_in, dec_weight)
        wide_cols = [a.shape[1] for a in wide]
        gathered_wide = lax.all_gather(jnp.concatenate(wide, axis=1), AX, axis=0, tiled=True)
        wide_full = []
        offset = 0
        for cols in wide_cols:
            wide_full.append(gathered_wide[:, offset : offset + cols])
            offset += cols
        qkv_full, out_full, inner_full, dec_full = wide_full
        outer_full = lax.all_gather(mlp_out, AX, axis=0, tiled=True)

        chip_count, vis_len, feature_width = tokens.shape
        row_count = chip_count * vis_len
        heads = feature_width // HD
        counts = jnp.sum(
            (band_waves[:, :, None] == jnp.arange(WAVES, dtype=jnp.int32)[None, None, :]).astype(
                jnp.float32
            ),
            axis=1,
        )
        spectral = jnp.dot(
            counts.astype(jnp.bfloat16), wave_full, preferred_element_type=jnp.float32
        )
        residual = (tokens.astype(jnp.float32) + spectral[:, None, :]).reshape(row_count, D)
        norm_out_one, normed_one, inverse_one = norm_forward(
            residual, gain_one.astype(jnp.float32), shift_one.astype(jnp.float32)
        )
        act_one = norm_out_one.astype(jnp.bfloat16)
        qkv_vals = product(act_one, qkv_full).astype(jnp.bfloat16)
        head_shape = (chip_count, vis_len, heads, HD)
        queries = qkv_vals[:, :D].reshape(head_shape)
        key_rows = qkv_vals[:, D : 2 * D].reshape(head_shape)
        value_rows = qkv_vals[:, 2 * D :].reshape(head_shape)
        mixture4, soft_full, soft_low = attend(queries, key_rows, value_rows)
        mixture = mixture4.reshape(row_count, D)
        res_one = residual + product(mixture, out_full)
        norm_out_two, normed_two, inverse_two = norm_forward(
            res_one, gain_two.astype(jnp.float32), shift_two.astype(jnp.float32)
        )
        act_two = norm_out_two.astype(jnp.bfloat16)
        hidden = product(act_two, inner_full) + inner_bias.astype(jnp.float32)
        active = gelu_value(hidden).astype(jnp.bfloat16)
        res_two = res_one + (product(active, outer_full) + outer_bias.astype(jnp.float32))
        enc_low = res_two.astype(jnp.bfloat16)
        projected = (product(enc_low, dec_full) + dec_shift.astype(jnp.float32)).astype(
            jnp.bfloat16
        )
        slot_ids = jnp.arange(L, dtype=jnp.int32)
        one_hot = (visible_slot[:, None, :] == slot_ids[None, :, None]).astype(jnp.bfloat16)
        filled_vis = jnp.einsum(
            "csi,cie->cse",
            one_hot,
            projected.reshape(chip_count, vis_len, DEC),
            preferred_element_type=jnp.float32,
        )
        has_row = jnp.sum(one_hot.astype(jnp.float32), axis=2, keepdims=True) > 0.5
        filled = jnp.where(has_row, filled_vis, mask_full.astype(jnp.float32)[None, None, :])
        filled = filled.astype(jnp.bfloat16)
        decoded = lax.all_to_all(filled, AX, split_axis=1, concat_axis=0, tiled=True)
        grad_full = lax.all_to_all(cot_decoded, AX, split_axis=0, concat_axis=1, tiled=True)

        grad_vis_low = (
            jnp.einsum("csi,cse->cie", one_hot, grad_full, preferred_element_type=jnp.float32)
            .astype(jnp.bfloat16)
            .reshape(row_count, DEC)
        )
        grad_vis = grad_vis_low.astype(jnp.float32)
        grad_mask_token = jnp.sum(
            jnp.where(has_row, 0.0, grad_full.astype(jnp.float32)), axis=(0, 1)
        )
        grad_dec_bias = jnp.sum(grad_vis, axis=0)
        grad_dec_weight = inner_rows(enc_low, grad_vis_low)
        grad_res_two = outer_cols(grad_vis_low, dec_full)
        grad_ffo = grad_res_two.astype(jnp.bfloat16)
        grad_mlp_out_bias = jnp.sum(grad_ffo.astype(jnp.float32), axis=0)
        grad_mlp_out = inner_rows(active, grad_ffo)
        grad_hidden = (outer_cols(grad_ffo, outer_full) * gelu_slope(hidden)).astype(jnp.bfloat16)
        grad_mlp_in_bias = jnp.sum(grad_hidden.astype(jnp.float32), axis=0)
        grad_mlp_in = inner_rows(act_two, grad_hidden)
        grad_act_two = outer_cols(grad_hidden, inner_full)
        grad_norm_two, grad_norm2_gain, grad_norm2_bias = norm_backward(
            grad_act_two, normed_two, inverse_two, gain_two.astype(jnp.float32)
        )
        grad_res_one = grad_res_two + grad_norm_two
        grad_att = grad_res_one.astype(jnp.bfloat16)
        grad_out_weight = inner_rows(mixture, grad_att)
        grad_mixed = outer_cols(grad_att, out_full).astype(jnp.bfloat16).reshape(head_shape)
        grad_queries, grad_keys, grad_values = attend_back(
            queries, key_rows, value_rows, soft_full, soft_low, grad_mixed
        )
        grad_qkv = jnp.concatenate(
            [
                grad_queries.reshape(row_count, D),
                grad_keys.reshape(row_count, D),
                grad_values.reshape(row_count, D),
            ],
            axis=1,
        ).astype(jnp.bfloat16)
        grad_qkv_weight = inner_rows(act_one, grad_qkv)
        grad_act_one = outer_cols(grad_qkv, qkv_full)
        grad_norm_one, grad_norm1_gain, grad_norm1_bias = norm_backward(
            grad_act_one, normed_one, inverse_one, gain_one.astype(jnp.float32)
        )
        grad_tokens = (grad_res_one + grad_norm_one).reshape(chip_count, vis_len, D)
        chip_sums = jnp.sum(grad_tokens, axis=1)
        grad_wave_table = lax.dot_general(
            counts, chip_sums, (((0,), (0,)), ((), ())), precision=HIGH_PRECISION
        )
        small_grads = (grad_wave_table, grad_norm1_gain, grad_norm1_bias, grad_norm2_gain,
                       grad_norm2_bias, grad_mlp_in_bias, grad_mlp_out_bias, grad_dec_bias,
                       grad_mask_token)
        rows_block = grad_out_weight.shape[0] // n_dev
        sg_flat = [g.reshape(n_dev, -1) for g in small_grads]
        sg_widths = [f.shape[1] for f in sg_flat]
        sg_cols = -(-sum(sg_widths) // (rows_block * 128)) * 128
        sg_pad = rows_block * sg_cols - sum(sg_widths)
        sg_block = jnp.concatenate(
            sg_flat + [jnp.zeros((n_dev, sg_pad), jnp.float32)], axis=1
        ).reshape(n_dev * rows_block, sg_cols)
        joined = jnp.concatenate(
            [grad_qkv_weight, grad_out_weight, grad_dec_weight, sg_block], axis=1
        )
        reduced_joined = rs_chain(joined, n_bits, orders["yz"])
        qkv_cols = grad_qkv_weight.shape[1]
        out_cols = grad_out_weight.shape[1]
        dec_cols = grad_dec_weight.shape[1]
        sum_qkv = reduced_joined[:, :qkv_cols]
        sum_out = reduced_joined[:, qkv_cols : qkv_cols + out_cols]
        sum_dec = reduced_joined[:, qkv_cols + out_cols : qkv_cols + out_cols + dec_cols]
        sg_sum = reduced_joined[:, qkv_cols + out_cols + dec_cols :].reshape(-1)
        sg_parts = []
        offset = 0
        for g, width in zip(small_grads, sg_widths):
            sg_parts.append(sg_sum[offset : offset + width].reshape((g.shape[0] // n_dev,) + g.shape[1:]))
            offset += width
        (sum_wave, sum_g1, sum_b1, sum_g2, sum_b2, sum_ib, sum_ob, sum_db, sum_mask) = sg_parts
        sum_mlp_out = rs_chain(grad_mlp_out, n_bits, orders["x"])
        sum_mlp_in = rs_chain(grad_mlp_in, n_bits, orders["y"])
        summed = (sum_wave, sum_g1, sum_b1, sum_qkv, sum_out, sum_g2, sum_b2, sum_mlp_in,
                  sum_ib, sum_mlp_out, sum_ob, sum_dec, sum_db, sum_mask)
        return (decoded, grad_tokens, *summed)

    return local


def solution(mesh):
    n_dev = mesh.devices.size
    n_bits = n_dev.bit_length() - 1
    order = halving_order(n_bits, core_bit_of(mesh))
    orders = chain_orders(*bit_groups(mesh))
    placed = (
        P(AX, None, None),
        P(AX, None),
        P(AX, None),
        P(AX, None),
        P(AX),
        P(AX),
        P(AX, None),
        P(AX, None),
        P(AX),
        P(AX),
        P(AX, None),
        P(AX),
        P(AX, None),
        P(AX),
        P(AX, None),
        P(AX),
        P(AX),
        P(None, AX, None),
    )
    return jax.shard_map(
        make_local(n_bits, order, orders),
        mesh=mesh,
        in_specs=placed,
        out_specs=(
            P(None, AX, None),
            P(AX, None, None),
            P(AX, None),
            P(AX),
            P(AX),
            P(AX, None),
            P(AX, None),
            P(AX),
            P(AX),
            P(AX, None),
            P(AX),
            P(AX, None),
            P(AX),
            P(AX, None),
            P(AX),
            P(AX),
        ),
        check_vma=False,
    )
```

```python
import numpy as np
import jax
import jax.numpy as jnp
from jax import lax
from jax.sharding import PartitionSpec as P

D = 768
HD = 64
DEC = 512
WAVES = 128
L = 1024

NORM_EPSILON = 1e-05
ROOT_HALF = 0.7071067811865476
INVERSE_ROOT_TAU = 0.3989422804014327
HIGH_PRECISION = lax.Precision.HIGHEST
AX = ("dp", "fsdp")


def product(left_op, right_op):
    return jnp.dot(left_op, right_op, preferred_element_type=jnp.float32)


def inner_rows(left_op, right_op):
    return lax.dot_general(
        left_op, right_op, (((0,), (0,)), ((), ())), preferred_element_type=jnp.float32
    )


def outer_cols(left_op, right_op):
    return lax.dot_general(
        left_op, right_op, (((1,), (1,)), ((), ())), preferred_element_type=jnp.float32
    )


def norm_forward(residual, gain, shift):
    mean_val = jnp.mean(residual, axis=-1, keepdims=True)
    centered = residual - mean_val
    variance = jnp.mean(centered * centered, axis=-1, keepdims=True)
    inverse = lax.rsqrt(variance + NORM_EPSILON)
    normed = centered * inverse
    return (normed * gain + shift, normed, inverse)


def norm_backward(incoming, normed, inverse, gain):
    scaled = incoming * gain
    first_mean = jnp.mean(scaled, axis=-1, keepdims=True)
    second_mean = jnp.mean(scaled * normed, axis=-1, keepdims=True)
    grad_input = inverse * (scaled - first_mean - normed * second_mean)
    return (grad_input, jnp.sum(incoming * normed, axis=0), jnp.sum(incoming, axis=0))


def gelu_value(hidden):
    return 0.5 * hidden * (1.0 + lax.erf(hidden * ROOT_HALF))


def gelu_slope(hidden):
    return (
        0.5 * (1.0 + lax.erf(hidden * ROOT_HALF))
        + hidden * jnp.exp(-0.5 * hidden * hidden) * INVERSE_ROOT_TAU
    )


def core_bit_of(mesh):
    flat = list(mesh.devices.reshape(-1))
    cores = [d.core_on_chip for d in flat]
    stride = 1
    while stride < len(flat) and cores[stride] == cores[0]:
        stride *= 2
    return stride.bit_length() - 1


def bit_groups(mesh):
    flat = list(mesh.devices.reshape(-1))
    n_bits = len(flat).bit_length() - 1
    first = flat[0]
    core_bit = None
    groups = {}
    for bit in range(n_bits):
        other = flat[1 << bit]
        if other.core_on_chip != first.core_on_chip:
            core_bit = bit
            continue
        axis = [a for a in range(len(first.coords)) if first.coords[a] != other.coords[a]]
        groups.setdefault(axis[0] if axis else -1, []).append(bit)
    return core_bit, [sorted(bits) for _, bits in sorted(groups.items())]


def chain_orders(core_bit, groups):
    head = [] if core_bit is None else [core_bit]
    if len(groups) < 3:
        flat = head + [b for g in reversed(groups) for b in g]
        return {"y": flat, "x": flat, "yz": flat}
    x_bits, y_bits, z_bits = groups[0], groups[1], [b for g in groups[2:] for b in g]
    return {
        "y": head + y_bits + x_bits + z_bits,
        "x": head + x_bits + y_bits + z_bits,
        "yz": head + y_bits + z_bits + x_bits,
    }


def halving_order(n_bits, core_bit):
    rest = [b for b in reversed(range(n_bits)) if b != core_bit]
    if len(rest) >= 2:
        rest[-2:] = rest[-2:][::-1]
    return [core_bit] + rest


def rs_chain(grad, n_bits, order):
    n_dev = 2 ** n_bits
    me = lax.axis_index(AX)
    rows = grad.shape[0] // n_dev
    current = grad.reshape((2,) * n_bits + (rows,) + grad.shape[1:])
    for bit in order:
        axis = n_bits - 1 - bit
        mine = (me >> bit) & 1
        keep = lax.dynamic_slice_in_dim(current, mine, 1, axis=axis)
        send = lax.dynamic_slice_in_dim(current, 1 - mine, 1, axis=axis)
        moved = lax.ppermute(
            send.astype(jnp.bfloat16), AX, [(i, i ^ (1 << bit)) for i in range(n_dev)]
        )
        current = keep + moved.astype(jnp.float32)
    return current.reshape((rows,) + grad.shape[1:])


def ag_chain(block, n_bits, order):
    me = lax.axis_index(AX)
    n_dev = 2 ** n_bits
    current = block.reshape((1,) * n_bits + block.shape)
    for bit in reversed(order):
        axis = n_bits - 1 - bit
        mine = ((me >> bit) & 1) == 1
        moved = lax.ppermute(current, AX, [(i, i ^ (1 << bit)) for i in range(n_dev)])
        low = jnp.where(mine, moved, current)
        high = jnp.where(mine, current, moved)
        current = jnp.concatenate([low, high], axis=axis)
    return current.reshape((n_dev * block.shape[0],) + block.shape[1:])


def pack_rows(arrays, n_dev, dtype):
    flat = [a.reshape(n_dev, -1).astype(dtype) for a in arrays]
    widths = [f.shape[1] for f in flat]
    padded = -sum(widths) % 1024
    flat.append(jnp.zeros((n_dev, padded), dtype))
    packed = jnp.concatenate(flat, axis=1)
    return packed.reshape(n_dev, 8, -1), widths


def unpack_rows(packed, arrays, widths, n_dev, leading):
    flat = packed.reshape(packed.shape[0], -1)
    out = []
    offset = 0
    for a, width in zip(arrays, widths):
        piece = flat[:, offset : offset + width]
        out.append(piece.reshape((leading * a.shape[0] // n_dev,) + a.shape[1:]))
        offset += width
    return out


def attend(queries, key_rows, value_rows):
    score_scale = HD ** (-0.5)
    scores = (
        jnp.einsum("cqhd,ckhd->chqk", queries, key_rows, preferred_element_type=jnp.float32)
        * score_scale
    )
    row_peak = jnp.max(scores, axis=-1, keepdims=True)
    exponents = jnp.exp(scores - row_peak)
    row_total = jnp.sum(exponents, axis=-1, keepdims=True)
    soft_full = exponents / row_total
    soft_low = soft_full.astype(jnp.bfloat16)
    mixture = jnp.einsum(
        "chqk,ckhd->cqhd", soft_low, value_rows, preferred_element_type=jnp.float32
    )
    return mixture.astype(jnp.bfloat16), soft_full, soft_low


def attend_back(queries, key_rows, value_rows, soft_full, soft_low, grad_mixture):
    score_scale = HD ** (-0.5)
    grad_values = jnp.einsum(
        "chqk,cqhd->ckhd", soft_low, grad_mixture, preferred_element_type=jnp.float32
    )
    grad_soft = jnp.einsum(
        "cqhd,ckhd->chqk", grad_mixture, value_rows, preferred_element_type=jnp.float32
    )
    row_delta = jnp.sum(grad_soft * soft_full, axis=-1, keepdims=True)
    grad_scores = (soft_full * (grad_soft - row_delta)).astype(jnp.bfloat16)
    grad_queries = (
        jnp.einsum("chqk,ckhd->cqhd", grad_scores, key_rows, preferred_element_type=jnp.float32)
        * score_scale
    )
    grad_keys = (
        jnp.einsum("chqk,cqhd->ckhd", grad_scores, queries, preferred_element_type=jnp.float32)
        * score_scale
    )
    return grad_queries, grad_keys, grad_values


def make_local(n_bits, order, orders):
    n_dev = 2 ** n_bits

    def local(
        tokens,
        band_waves,
        visible_slot,
        wave_table,
        norm1_gain,
        norm1_bias,
        qkv_weight,
        out_weight,
        norm2_gain,
        norm2_bias,
        mlp_in,
        mlp_in_bias,
        mlp_out,
        mlp_out_bias,
        dec_weight,
        dec_bias,
        mask_token,
        cot_decoded,
    ):
        shards = (
            wave_table,
            norm1_gain,
            norm1_bias,
            qkv_weight,
            out_weight,
            norm2_gain,
            norm2_bias,
            mlp_in,
            mlp_in_bias,
            mlp_out,
            mlp_out_bias,
            dec_weight,
            dec_bias,
            mask_token,
        )
        out_split = mlp_out.shape[1] // 2
        small = (wave_table, norm1_gain, norm1_bias, norm2_gain, norm2_bias, mlp_in_bias,
                 mlp_out_bias, dec_bias, mask_token, mlp_out[:, out_split:])
        packed_small, small_widths = pack_rows(
            [a.reshape(1, -1) for a in small], 1, jnp.bfloat16
        )
        gathered_small = ag_chain(packed_small, n_bits, orders["x"])
        (wave_full, gain_one, shift_one, gain_two, shift_two, inner_bias, outer_bias,
         dec_shift, mask_full, outer_right) = unpack_rows(
            gathered_small, small, small_widths, 1, n_dev)
        wide = (qkv_weight, out_weight, mlp_in, dec_weight)
        wide_cols = [a.shape[1] for a in wide]
        gathered_wide = lax.all_gather(jnp.concatenate(wide, axis=1), AX, axis=0, tiled=True)
        wide_full = []
        offset = 0
        for cols in wide_cols:
            wide_full.append(gathered_wide[:, offset : offset + cols])
            offset += cols
        qkv_full, out_full, inner_full, dec_full = wide_full
        outer_left = lax.all_gather(mlp_out[:, :out_split], AX, axis=0, tiled=True)
        outer_full = jnp.concatenate([outer_left, outer_right], axis=1)

        chip_count, vis_len, feature_width = tokens.shape
        row_count = chip_count * vis_len
        heads = feature_width // HD
        counts = jnp.sum(
            (band_waves[:, :, None] == jnp.arange(WAVES, dtype=jnp.int32)[None, None, :]).astype(
                jnp.float32
            ),
            axis=1,
        )
        spectral = jnp.dot(
            counts.astype(jnp.bfloat16), wave_full, preferred_element_type=jnp.float32
        )
        residual = (tokens.astype(jnp.float32) + spectral[:, None, :]).reshape(row_count, D)
        norm_out_one, normed_one, inverse_one = norm_forward(
            residual, gain_one.astype(jnp.float32), shift_one.astype(jnp.float32)
        )
        act_one = norm_out_one.astype(jnp.bfloat16)
        qkv_vals = product(act_one, qkv_full).astype(jnp.bfloat16)
        head_shape = (chip_count, vis_len, heads, HD)
        queries = qkv_vals[:, :D].reshape(head_shape)
        key_rows = qkv_vals[:, D : 2 * D].reshape(head_shape)
        value_rows = qkv_vals[:, 2 * D :].reshape(head_shape)
        mixture4, soft_full, soft_low = attend(queries, key_rows, value_rows)
        mixture = mixture4.reshape(row_count, D)
        res_one = residual + product(mixture, out_full)
        norm_out_two, normed_two, inverse_two = norm_forward(
            res_one, gain_two.astype(jnp.float32), shift_two.astype(jnp.float32)
        )
        act_two = norm_out_two.astype(jnp.bfloat16)
        hidden = product(act_two, inner_full) + inner_bias.astype(jnp.float32)
        active = gelu_value(hidden).astype(jnp.bfloat16)
        res_two = res_one + (product(active, outer_full) + outer_bias.astype(jnp.float32))
        enc_low = res_two.astype(jnp.bfloat16)
        projected = (product(enc_low, dec_full) + dec_shift.astype(jnp.float32)).astype(
            jnp.bfloat16
        )
        slot_ids = jnp.arange(L, dtype=jnp.int32)
        one_hot = (visible_slot[:, None, :] == slot_ids[None, :, None]).astype(jnp.bfloat16)
        filled_vis = jnp.einsum(
            "csi,cie->cse",
            one_hot,
            projected.reshape(chip_count, vis_len, DEC),
            preferred_element_type=jnp.float32,
        )
        has_row = jnp.sum(one_hot.astype(jnp.float32), axis=2, keepdims=True) > 0.5
        filled = jnp.where(has_row, filled_vis, mask_full.astype(jnp.float32)[None, None, :])
        filled = filled.astype(jnp.bfloat16)
        decoded = lax.all_to_all(filled, AX, split_axis=1, concat_axis=0, tiled=True)
        grad_full = lax.all_to_all(cot_decoded, AX, split_axis=0, concat_axis=1, tiled=True)

        grad_vis_low = (
            jnp.einsum("csi,cse->cie", one_hot, grad_full, preferred_element_type=jnp.float32)
            .astype(jnp.bfloat16)
            .reshape(row_count, DEC)
        )
        grad_vis = grad_vis_low.astype(jnp.float32)
        grad_mask_token = jnp.sum(
            jnp.where(has_row, 0.0, grad_full.astype(jnp.float32)), axis=(0, 1)
        )
        grad_dec_bias = jnp.sum(grad_vis, axis=0)
        grad_dec_weight = inner_rows(enc_low, grad_vis_low)
        grad_res_two = outer_cols(grad_vis_low, dec_full)
        grad_ffo = grad_res_two.astype(jnp.bfloat16)
        grad_mlp_out_bias = jnp.sum(grad_ffo.astype(jnp.float32), axis=0)
        grad_mlp_out = inner_rows(active, grad_ffo)
        grad_hidden = (outer_cols(grad_ffo, outer_full) * gelu_slope(hidden)).astype(jnp.bfloat16)
        grad_mlp_in_bias = jnp.sum(grad_hidden.astype(jnp.float32), axis=0)
        grad_mlp_in = inner_rows(act_two, grad_hidden)
        grad_act_two = outer_cols(grad_hidden, inner_full)
        grad_norm_two, grad_norm2_gain, grad_norm2_bias = norm_backward(
            grad_act_two, normed_two, inverse_two, gain_two.astype(jnp.float32)
        )
        grad_res_one = grad_res_two + grad_norm_two
        grad_att = grad_res_one.astype(jnp.bfloat16)
        grad_out_weight = inner_rows(mixture, grad_att)
        grad_mixed = outer_cols(grad_att, out_full).astype(jnp.bfloat16).reshape(head_shape)
        grad_queries, grad_keys, grad_values = attend_back(
            queries, key_rows, value_rows, soft_full, soft_low, grad_mixed
        )
        grad_qkv = jnp.concatenate(
            [
                grad_queries.reshape(row_count, D),
                grad_keys.reshape(row_count, D),
                grad_values.reshape(row_count, D),
            ],
            axis=1,
        ).astype(jnp.bfloat16)
        grad_qkv_weight = inner_rows(act_one, grad_qkv)
        grad_act_one = outer_cols(grad_qkv, qkv_full)
        grad_norm_one, grad_norm1_gain, grad_norm1_bias = norm_backward(
            grad_act_one, normed_one, inverse_one, gain_one.astype(jnp.float32)
        )
        grad_tokens = (grad_res_one + grad_norm_one).reshape(chip_count, vis_len, D)
        chip_sums = jnp.sum(grad_tokens, axis=1)
        grad_wave_table = lax.dot_general(
            counts, chip_sums, (((0,), (0,)), ((), ())), precision=HIGH_PRECISION
        )
        small_grads = (grad_wave_table, grad_norm1_gain, grad_norm1_bias, grad_norm2_gain,
                       grad_norm2_bias, grad_mlp_in_bias, grad_mlp_out_bias, grad_dec_bias,
                       grad_mask_token)
        rows_block = grad_out_weight.shape[0] // n_dev
        sg_flat = [g.reshape(n_dev, -1) for g in small_grads]
        sg_widths = [f.shape[1] for f in sg_flat]
        sg_cols = -(-sum(sg_widths) // (rows_block * 128)) * 128
        sg_pad = rows_block * sg_cols - sum(sg_widths)
        sg_block = jnp.concatenate(
            sg_flat + [jnp.zeros((n_dev, sg_pad), jnp.float32)], axis=1
        ).reshape(n_dev * rows_block, sg_cols)
        joined = jnp.concatenate([grad_out_weight, grad_dec_weight, sg_block], axis=1)
        reduced_joined = rs_chain(joined, n_bits, orders["yz"])
        out_cols = grad_out_weight.shape[1]
        dec_cols = grad_dec_weight.shape[1]
        sum_out = reduced_joined[:, :out_cols]
        sum_dec = reduced_joined[:, out_cols : out_cols + dec_cols]
        sg_sum = reduced_joined[:, out_cols + dec_cols :].reshape(-1)
        sg_parts = []
        offset = 0
        for g, width in zip(small_grads, sg_widths):
            sg_parts.append(sg_sum[offset : offset + width].reshape((g.shape[0] // n_dev,) + g.shape[1:]))
            offset += width
        (sum_wave, sum_g1, sum_b1, sum_g2, sum_b2, sum_ib, sum_ob, sum_db, sum_mask) = sg_parts
        sum_mlp_out = rs_chain(grad_mlp_out, n_bits, orders["x"])
        sum_mlp_in = rs_chain(grad_mlp_in, n_bits, orders["y"])
        sum_qkv = rs_chain(grad_qkv_weight, n_bits, orders["yz"])
        summed = (sum_wave, sum_g1, sum_b1, sum_qkv, sum_out, sum_g2, sum_b2, sum_mlp_in,
                  sum_ib, sum_mlp_out, sum_ob, sum_dec, sum_db, sum_mask)
        return (decoded, grad_tokens, *summed)

    return local


def solution(mesh):
    n_dev = mesh.devices.size
    n_bits = n_dev.bit_length() - 1
    order = halving_order(n_bits, core_bit_of(mesh))
    orders = chain_orders(*bit_groups(mesh))
    placed = (
        P(AX, None, None),
        P(AX, None),
        P(AX, None),
        P(AX, None),
        P(AX),
        P(AX),
        P(AX, None),
        P(AX, None),
        P(AX),
        P(AX),
        P(AX, None),
        P(AX),
        P(AX, None),
        P(AX),
        P(AX, None),
        P(AX),
        P(AX),
        P(None, AX, None),
    )
    return jax.shard_map(
        make_local(n_bits, order, orders),
        mesh=mesh,
        in_specs=placed,
        out_specs=(
            P(None, AX, None),
            P(AX, None, None),
            P(AX, None),
            P(AX),
            P(AX),
            P(AX, None),
            P(AX, None),
            P(AX),
            P(AX),
            P(AX, None),
            P(AX),
            P(AX, None),
            P(AX),
            P(AX, None),
            P(AX),
            P(AX),
        ),
        check_vma=False,
    )
```

```python
import numpy as np
import jax
import jax.numpy as jnp
from jax import lax
from jax.sharding import PartitionSpec as P

D = 768
HD = 64
DEC = 512
WAVES = 128
L = 1024

NORM_EPSILON = 1e-05
ROOT_HALF = 0.7071067811865476
INVERSE_ROOT_TAU = 0.3989422804014327
HIGH_PRECISION = lax.Precision.HIGHEST
AX = ("dp", "fsdp")


def product(left_op, right_op):
    return jnp.dot(left_op, right_op, preferred_element_type=jnp.float32)


def inner_rows(left_op, right_op):
    return lax.dot_general(
        left_op, right_op, (((0,), (0,)), ((), ())), preferred_element_type=jnp.float32
    )


def outer_cols(left_op, right_op):
    return lax.dot_general(
        left_op, right_op, (((1,), (1,)), ((), ())), preferred_element_type=jnp.float32
    )


def norm_forward(residual, gain, shift):
    mean_val = jnp.mean(residual, axis=-1, keepdims=True)
    centered = residual - mean_val
    variance = jnp.mean(centered * centered, axis=-1, keepdims=True)
    inverse = lax.rsqrt(variance + NORM_EPSILON)
    normed = centered * inverse
    return (normed * gain + shift, normed, inverse)


def norm_backward(incoming, normed, inverse, gain):
    scaled = incoming * gain
    first_mean = jnp.mean(scaled, axis=-1, keepdims=True)
    second_mean = jnp.mean(scaled * normed, axis=-1, keepdims=True)
    grad_input = inverse * (scaled - first_mean - normed * second_mean)
    return (grad_input, jnp.sum(incoming * normed, axis=0), jnp.sum(incoming, axis=0))


def gelu_value(hidden):
    return 0.5 * hidden * (1.0 + lax.erf(hidden * ROOT_HALF))


def gelu_slope(hidden):
    return (
        0.5 * (1.0 + lax.erf(hidden * ROOT_HALF))
        + hidden * jnp.exp(-0.5 * hidden * hidden) * INVERSE_ROOT_TAU
    )


def core_bit_of(mesh):
    flat = list(mesh.devices.reshape(-1))
    cores = [d.core_on_chip for d in flat]
    stride = 1
    while stride < len(flat) and cores[stride] == cores[0]:
        stride *= 2
    return stride.bit_length() - 1


def bit_groups(mesh):
    flat = list(mesh.devices.reshape(-1))
    n_bits = len(flat).bit_length() - 1
    first = flat[0]
    core_bit = None
    groups = {}
    for bit in range(n_bits):
        other = flat[1 << bit]
        if other.core_on_chip != first.core_on_chip:
            core_bit = bit
            continue
        axis = [a for a in range(len(first.coords)) if first.coords[a] != other.coords[a]]
        groups.setdefault(axis[0] if axis else -1, []).append(bit)
    return core_bit, [sorted(bits) for _, bits in sorted(groups.items())]


def chain_orders(core_bit, groups):
    head = [] if core_bit is None else [core_bit]
    if len(groups) < 3:
        flat = head + [b for g in reversed(groups) for b in g]
        return {"y": flat, "x": flat, "yz": flat}
    x_bits, y_bits, z_bits = groups[0], groups[1], [b for g in groups[2:] for b in g]
    return {
        "y": head + y_bits + x_bits + z_bits,
        "x": head + x_bits + y_bits + z_bits,
        "yz": head + y_bits + z_bits + x_bits,
    }


def halving_order(n_bits, core_bit):
    rest = [b for b in reversed(range(n_bits)) if b != core_bit]
    if len(rest) >= 2:
        rest[-2:] = rest[-2:][::-1]
    return [core_bit] + rest


def rs_chain(grad, n_bits, order):
    n_dev = 2 ** n_bits
    me = lax.axis_index(AX)
    rows = grad.shape[0] // n_dev
    current = grad.reshape((2,) * n_bits + (rows,) + grad.shape[1:])
    for bit in order:
        axis = n_bits - 1 - bit
        mine = (me >> bit) & 1
        keep = lax.dynamic_slice_in_dim(current, mine, 1, axis=axis)
        send = lax.dynamic_slice_in_dim(current, 1 - mine, 1, axis=axis)
        moved = lax.ppermute(
            send.astype(jnp.bfloat16), AX, [(i, i ^ (1 << bit)) for i in range(n_dev)]
        )
        current = keep + moved.astype(jnp.float32)
    return current.reshape((rows,) + grad.shape[1:])


def ag_chain(block, n_bits, order):
    me = lax.axis_index(AX)
    n_dev = 2 ** n_bits
    current = block.reshape((1,) * n_bits + block.shape)
    for bit in reversed(order):
        axis = n_bits - 1 - bit
        mine = ((me >> bit) & 1) == 1
        moved = lax.ppermute(current, AX, [(i, i ^ (1 << bit)) for i in range(n_dev)])
        low = jnp.where(mine, moved, current)
        high = jnp.where(mine, current, moved)
        current = jnp.concatenate([low, high], axis=axis)
    return current.reshape((n_dev * block.shape[0],) + block.shape[1:])


def pack_rows(arrays, n_dev, dtype):
    flat = [a.reshape(n_dev, -1).astype(dtype) for a in arrays]
    widths = [f.shape[1] for f in flat]
    padded = -sum(widths) % 1024
    flat.append(jnp.zeros((n_dev, padded), dtype))
    packed = jnp.concatenate(flat, axis=1)
    return packed.reshape(n_dev, 8, -1), widths


def unpack_rows(packed, arrays, widths, n_dev, leading):
    flat = packed.reshape(packed.shape[0], -1)
    out = []
    offset = 0
    for a, width in zip(arrays, widths):
        piece = flat[:, offset : offset + width]
        out.append(piece.reshape((leading * a.shape[0] // n_dev,) + a.shape[1:]))
        offset += width
    return out


def attend(queries, key_rows, value_rows):
    score_scale = HD ** (-0.5)
    scores = (
        jnp.einsum("cqhd,ckhd->chqk", queries, key_rows, preferred_element_type=jnp.float32)
        * score_scale
    )
    row_peak = jnp.max(scores, axis=-1, keepdims=True)
    exponents = jnp.exp(scores - row_peak)
    row_total = jnp.sum(exponents, axis=-1, keepdims=True)
    soft_full = exponents / row_total
    soft_low = soft_full.astype(jnp.bfloat16)
    mixture = jnp.einsum(
        "chqk,ckhd->cqhd", soft_low, value_rows, preferred_element_type=jnp.float32
    )
    return mixture.astype(jnp.bfloat16), soft_full, soft_low


def attend_back(queries, key_rows, value_rows, soft_full, soft_low, grad_mixture):
    score_scale = HD ** (-0.5)
    grad_values = jnp.einsum(
        "chqk,cqhd->ckhd", soft_low, grad_mixture, preferred_element_type=jnp.float32
    )
    grad_soft = jnp.einsum(
        "cqhd,ckhd->chqk", grad_mixture, value_rows, preferred_element_type=jnp.float32
    )
    row_delta = jnp.sum(grad_soft * soft_full, axis=-1, keepdims=True)
    grad_scores = (soft_full * (grad_soft - row_delta)).astype(jnp.bfloat16)
    grad_queries = (
        jnp.einsum("chqk,ckhd->cqhd", grad_scores, key_rows, preferred_element_type=jnp.float32)
        * score_scale
    )
    grad_keys = (
        jnp.einsum("chqk,cqhd->ckhd", grad_scores, queries, preferred_element_type=jnp.float32)
        * score_scale
    )
    return grad_queries, grad_keys, grad_values


def make_local(n_bits, order, orders):
    n_dev = 2 ** n_bits

    def local(
        tokens,
        band_waves,
        visible_slot,
        wave_table,
        norm1_gain,
        norm1_bias,
        qkv_weight,
        out_weight,
        norm2_gain,
        norm2_bias,
        mlp_in,
        mlp_in_bias,
        mlp_out,
        mlp_out_bias,
        dec_weight,
        dec_bias,
        mask_token,
        cot_decoded,
    ):
        shards = (
            wave_table,
            norm1_gain,
            norm1_bias,
            qkv_weight,
            out_weight,
            norm2_gain,
            norm2_bias,
            mlp_in,
            mlp_in_bias,
            mlp_out,
            mlp_out_bias,
            dec_weight,
            dec_bias,
            mask_token,
        )
        small = (wave_table, norm1_gain, norm1_bias, norm2_gain, norm2_bias, mlp_in_bias,
                 mlp_out_bias, dec_bias, mask_token)
        packed_small, small_widths = pack_rows(
            [a.reshape(1, -1) for a in small], 1, jnp.bfloat16
        )
        gathered_small = ag_chain(packed_small, n_bits, orders["x"])
        (wave_full, gain_one, shift_one, gain_two, shift_two, inner_bias, outer_bias,
         dec_shift, mask_full) = unpack_rows(gathered_small, small, small_widths, 1, n_dev)
        wide = (qkv_weight, out_weight, mlp_in, dec_weight)
        wide_cols = [a.shape[1] for a in wide]
        gathered_wide = lax.all_gather(jnp.concatenate(wide, axis=1), AX, axis=0, tiled=True)
        wide_full = []
        offset = 0
        for cols in wide_cols:
            wide_full.append(gathered_wide[:, offset : offset + cols])
            offset += cols
        qkv_full, out_full, inner_full, dec_full = wide_full
        outer_full = lax.all_gather(mlp_out, AX, axis=0, tiled=True)

        chip_count, vis_len, feature_width = tokens.shape
        row_count = chip_count * vis_len
        heads = feature_width // HD
        counts = jnp.sum(
            (band_waves[:, :, None] == jnp.arange(WAVES, dtype=jnp.int32)[None, None, :]).astype(
                jnp.float32
            ),
            axis=1,
        )
        spectral = jnp.dot(
            counts.astype(jnp.bfloat16), wave_full, preferred_element_type=jnp.float32
        )
        residual = (tokens.astype(jnp.float32) + spectral[:, None, :]).reshape(row_count, D)
        norm_out_one, normed_one, inverse_one = norm_forward(
            residual, gain_one.astype(jnp.float32), shift_one.astype(jnp.float32)
        )
        act_one = norm_out_one.astype(jnp.bfloat16)
        head_shape = (chip_count, vis_len, heads, HD)
        queries = product(act_one, qkv_full[:, :D]).astype(jnp.bfloat16).reshape(head_shape)
        key_rows = product(act_one, qkv_full[:, D : 2 * D]).astype(jnp.bfloat16).reshape(head_shape)
        value_rows = product(act_one, qkv_full[:, 2 * D :]).astype(jnp.bfloat16).reshape(head_shape)
        mixture4, soft_full, soft_low = attend(queries, key_rows, value_rows)
        mixture = mixture4.reshape(row_count, D)
        res_one = residual + product(mixture, out_full)
        norm_out_two, normed_two, inverse_two = norm_forward(
            res_one, gain_two.astype(jnp.float32), shift_two.astype(jnp.float32)
        )
        act_two = norm_out_two.astype(jnp.bfloat16)
        hidden = product(act_two, inner_full) + inner_bias.astype(jnp.float32)
        active = gelu_value(hidden).astype(jnp.bfloat16)
        res_two = res_one + (product(active, outer_full) + outer_bias.astype(jnp.float32))
        enc_low = res_two.astype(jnp.bfloat16)
        projected = (product(enc_low, dec_full) + dec_shift.astype(jnp.float32)).astype(
            jnp.bfloat16
        )
        slot_ids = jnp.arange(L, dtype=jnp.int32)
        one_hot = (visible_slot[:, None, :] == slot_ids[None, :, None]).astype(jnp.bfloat16)
        filled_vis = jnp.einsum(
            "csi,cie->cse",
            one_hot,
            projected.reshape(chip_count, vis_len, DEC),
            preferred_element_type=jnp.float32,
        )
        has_row = jnp.sum(one_hot.astype(jnp.float32), axis=2, keepdims=True) > 0.5
        filled = jnp.where(has_row, filled_vis, mask_full.astype(jnp.float32)[None, None, :])
        filled = filled.astype(jnp.bfloat16)
        decoded = lax.all_to_all(filled, AX, split_axis=1, concat_axis=0, tiled=True)
        grad_full = lax.all_to_all(cot_decoded, AX, split_axis=0, concat_axis=1, tiled=True)

        grad_vis_low = (
            jnp.einsum("csi,cse->cie", one_hot, grad_full, preferred_element_type=jnp.float32)
            .astype(jnp.bfloat16)
            .reshape(row_count, DEC)
        )
        grad_vis = grad_vis_low.astype(jnp.float32)
        grad_mask_token = jnp.sum(
            jnp.where(has_row, 0.0, grad_full.astype(jnp.float32)), axis=(0, 1)
        )
        grad_dec_bias = jnp.sum(grad_vis, axis=0)
        grad_dec_weight = inner_rows(enc_low, grad_vis_low)
        grad_res_two = outer_cols(grad_vis_low, dec_full)
        grad_ffo = grad_res_two.astype(jnp.bfloat16)
        grad_mlp_out_bias = jnp.sum(grad_ffo.astype(jnp.float32), axis=0)
        grad_mlp_out = inner_rows(active, grad_ffo)
        grad_hidden = (outer_cols(grad_ffo, outer_full) * gelu_slope(hidden)).astype(jnp.bfloat16)
        grad_mlp_in_bias = jnp.sum(grad_hidden.astype(jnp.float32), axis=0)
        grad_mlp_in = inner_rows(act_two, grad_hidden)
        grad_act_two = outer_cols(grad_hidden, inner_full)
        grad_norm_two, grad_norm2_gain, grad_norm2_bias = norm_backward(
            grad_act_two, normed_two, inverse_two, gain_two.astype(jnp.float32)
        )
        grad_res_one = grad_res_two + grad_norm_two
        grad_att = grad_res_one.astype(jnp.bfloat16)
        grad_out_weight = inner_rows(mixture, grad_att)
        grad_mixed = outer_cols(grad_att, out_full).astype(jnp.bfloat16).reshape(head_shape)
        grad_queries, grad_keys, grad_values = attend_back(
            queries, key_rows, value_rows, soft_full, soft_low, grad_mixed
        )
        grad_qkv = jnp.concatenate(
            [
                grad_queries.reshape(row_count, D),
                grad_keys.reshape(row_count, D),
                grad_values.reshape(row_count, D),
            ],
            axis=1,
        ).astype(jnp.bfloat16)
        grad_qkv_weight = inner_rows(act_one, grad_qkv)
        grad_act_one = outer_cols(grad_qkv, qkv_full)
        grad_norm_one, grad_norm1_gain, grad_norm1_bias = norm_backward(
            grad_act_one, normed_one, inverse_one, gain_one.astype(jnp.float32)
        )
        grad_tokens = (grad_res_one + grad_norm_one).reshape(chip_count, vis_len, D)
        chip_sums = jnp.sum(grad_tokens, axis=1)
        grad_wave_table = lax.dot_general(
            counts, chip_sums, (((0,), (0,)), ((), ())), precision=HIGH_PRECISION
        )
        small_grads = (grad_wave_table, grad_norm1_gain, grad_norm1_bias, grad_norm2_gain,
                       grad_norm2_bias, grad_mlp_in_bias, grad_mlp_out_bias, grad_dec_bias,
                       grad_mask_token)
        rows_block = grad_out_weight.shape[0] // n_dev
        sg_flat = [g.reshape(n_dev, -1) for g in small_grads]
        sg_widths = [f.shape[1] for f in sg_flat]
        sg_cols = -(-sum(sg_widths) // (rows_block * 128)) * 128
        sg_pad = rows_block * sg_cols - sum(sg_widths)
        sg_block = jnp.concatenate(
            sg_flat + [jnp.zeros((n_dev, sg_pad), jnp.float32)], axis=1
        ).reshape(n_dev * rows_block, sg_cols)
        joined = jnp.concatenate([grad_out_weight, grad_dec_weight, sg_block], axis=1)
        reduced_joined = rs_chain(joined, n_bits, orders["yz"])
        out_cols = grad_out_weight.shape[1]
        dec_cols = grad_dec_weight.shape[1]
        sum_out = reduced_joined[:, :out_cols]
        sum_dec = reduced_joined[:, out_cols : out_cols + dec_cols]
        sg_sum = reduced_joined[:, out_cols + dec_cols :].reshape(-1)
        sg_parts = []
        offset = 0
        for g, width in zip(small_grads, sg_widths):
            sg_parts.append(sg_sum[offset : offset + width].reshape((g.shape[0] // n_dev,) + g.shape[1:]))
            offset += width
        (sum_wave, sum_g1, sum_b1, sum_g2, sum_b2, sum_ib, sum_ob, sum_db, sum_mask) = sg_parts
        sum_mlp_out = rs_chain(grad_mlp_out, n_bits, orders["x"])
        sum_mlp_in = rs_chain(grad_mlp_in, n_bits, orders["y"])
        sum_qkv = rs_chain(grad_qkv_weight, n_bits, orders["yz"])
        summed = (sum_wave, sum_g1, sum_b1, sum_qkv, sum_out, sum_g2, sum_b2, sum_mlp_in,
                  sum_ib, sum_mlp_out, sum_ob, sum_dec, sum_db, sum_mask)
        return (decoded, grad_tokens, *summed)

    return local


def solution(mesh):
    n_dev = mesh.devices.size
    n_bits = n_dev.bit_length() - 1
    order = halving_order(n_bits, core_bit_of(mesh))
    orders = chain_orders(*bit_groups(mesh))
    placed = (
        P(AX, None, None),
        P(AX, None),
        P(AX, None),
        P(AX, None),
        P(AX),
        P(AX),
        P(AX, None),
        P(AX, None),
        P(AX),
        P(AX),
        P(AX, None),
        P(AX),
        P(AX, None),
        P(AX),
        P(AX, None),
        P(AX),
        P(AX),
        P(None, AX, None),
    )
    return jax.shard_map(
        make_local(n_bits, order, orders),
        mesh=mesh,
        in_specs=placed,
        out_specs=(
            P(None, AX, None),
            P(AX, None, None),
            P(AX, None),
            P(AX),
            P(AX),
            P(AX, None),
            P(AX, None),
            P(AX),
            P(AX),
            P(AX, None),
            P(AX),
            P(AX, None),
            P(AX),
            P(AX, None),
            P(AX),
            P(AX),
        ),
        check_vma=False,
    )
```

```python
import numpy as np
import jax
import jax.numpy as jnp
from jax import lax
from jax.sharding import PartitionSpec as P

D = 768
HD = 64
DEC = 512
WAVES = 128
L = 1024

NORM_EPSILON = 1e-05
ROOT_HALF = 0.7071067811865476
INVERSE_ROOT_TAU = 0.3989422804014327
HIGH_PRECISION = lax.Precision.HIGHEST
AX = ("dp", "fsdp")


def product(left_op, right_op):
    return jnp.dot(left_op, right_op, preferred_element_type=jnp.float32)


def inner_rows(left_op, right_op):
    return lax.dot_general(
        left_op, right_op, (((0,), (0,)), ((), ())), preferred_element_type=jnp.float32
    )


def outer_cols(left_op, right_op):
    return lax.dot_general(
        left_op, right_op, (((1,), (1,)), ((), ())), preferred_element_type=jnp.float32
    )


def norm_forward(residual, gain, shift):
    mean_val = jnp.mean(residual, axis=-1, keepdims=True)
    centered = residual - mean_val
    variance = jnp.mean(centered * centered, axis=-1, keepdims=True)
    inverse = lax.rsqrt(variance + NORM_EPSILON)
    normed = centered * inverse
    return (normed * gain + shift, normed, inverse)


def norm_backward(incoming, normed, inverse, gain):
    scaled = incoming * gain
    first_mean = jnp.mean(scaled, axis=-1, keepdims=True)
    second_mean = jnp.mean(scaled * normed, axis=-1, keepdims=True)
    grad_input = inverse * (scaled - first_mean - normed * second_mean)
    return (grad_input, jnp.sum(incoming * normed, axis=0), jnp.sum(incoming, axis=0))


def gelu_value(hidden):
    return 0.5 * hidden * (1.0 + lax.erf(hidden * ROOT_HALF))


def gelu_slope(hidden):
    return (
        0.5 * (1.0 + lax.erf(hidden * ROOT_HALF))
        + hidden * jnp.exp(-0.5 * hidden * hidden) * INVERSE_ROOT_TAU
    )


def core_bit_of(mesh):
    flat = list(mesh.devices.reshape(-1))
    cores = [d.core_on_chip for d in flat]
    stride = 1
    while stride < len(flat) and cores[stride] == cores[0]:
        stride *= 2
    return stride.bit_length() - 1


def bit_groups(mesh):
    flat = list(mesh.devices.reshape(-1))
    n_bits = len(flat).bit_length() - 1
    first = flat[0]
    core_bit = None
    groups = {}
    for bit in range(n_bits):
        other = flat[1 << bit]
        if other.core_on_chip != first.core_on_chip:
            core_bit = bit
            continue
        axis = [a for a in range(len(first.coords)) if first.coords[a] != other.coords[a]]
        groups.setdefault(axis[0] if axis else -1, []).append(bit)
    return core_bit, [sorted(bits) for _, bits in sorted(groups.items())]


def chain_orders(core_bit, groups):
    head = [] if core_bit is None else [core_bit]
    if len(groups) < 3:
        flat = head + [b for g in reversed(groups) for b in g]
        return {"y": flat, "x": flat, "yz": flat}
    x_bits, y_bits, z_bits = groups[0], groups[1], [b for g in groups[2:] for b in g]
    return {
        "y": head + y_bits + x_bits + z_bits,
        "x": head + x_bits + y_bits + z_bits,
        "yz": head + y_bits + z_bits + x_bits,
    }


def halving_order(n_bits, core_bit):
    rest = [b for b in reversed(range(n_bits)) if b != core_bit]
    if len(rest) >= 2:
        rest[-2:] = rest[-2:][::-1]
    return [core_bit] + rest


def rs_chain(grad, n_bits, order):
    n_dev = 2 ** n_bits
    me = lax.axis_index(AX)
    rows = grad.shape[0] // n_dev
    current = grad.reshape((2,) * n_bits + (rows,) + grad.shape[1:])
    for bit in order:
        axis = n_bits - 1 - bit
        mine = (me >> bit) & 1
        keep = lax.dynamic_slice_in_dim(current, mine, 1, axis=axis)
        send = lax.dynamic_slice_in_dim(current, 1 - mine, 1, axis=axis)
        moved = lax.ppermute(
            send.astype(jnp.bfloat16), AX, [(i, i ^ (1 << bit)) for i in range(n_dev)]
        )
        current = keep + moved.astype(jnp.float32)
    return current.reshape((rows,) + grad.shape[1:])


def ag_chain(block, n_bits, order):
    me = lax.axis_index(AX)
    n_dev = 2 ** n_bits
    current = block.reshape((1,) * n_bits + block.shape)
    for bit in reversed(order):
        axis = n_bits - 1 - bit
        mine = ((me >> bit) & 1) == 1
        moved = lax.ppermute(current, AX, [(i, i ^ (1 << bit)) for i in range(n_dev)])
        low = jnp.where(mine, moved, current)
        high = jnp.where(mine, current, moved)
        current = jnp.concatenate([low, high], axis=axis)
    return current.reshape((n_dev * block.shape[0],) + block.shape[1:])


def pack_rows(arrays, n_dev, dtype):
    flat = [a.reshape(n_dev, -1).astype(dtype) for a in arrays]
    widths = [f.shape[1] for f in flat]
    padded = -sum(widths) % 1024
    flat.append(jnp.zeros((n_dev, padded), dtype))
    packed = jnp.concatenate(flat, axis=1)
    return packed.reshape(n_dev, 8, -1), widths


def unpack_rows(packed, arrays, widths, n_dev, leading):
    flat = packed.reshape(packed.shape[0], -1)
    out = []
    offset = 0
    for a, width in zip(arrays, widths):
        piece = flat[:, offset : offset + width]
        out.append(piece.reshape((leading * a.shape[0] // n_dev,) + a.shape[1:]))
        offset += width
    return out


def attend(queries, key_rows, value_rows):
    score_scale = HD ** (-0.5)
    scores = (
        jnp.einsum("cqhd,ckhd->chqk", queries, key_rows, preferred_element_type=jnp.float32)
        * score_scale
    )
    row_peak = jnp.max(scores, axis=-1, keepdims=True)
    exponents = jnp.exp(scores - row_peak)
    row_total = jnp.sum(exponents, axis=-1, keepdims=True)
    soft_full = exponents / row_total
    soft_low = soft_full.astype(jnp.bfloat16)
    mixture = jnp.einsum(
        "chqk,ckhd->cqhd", soft_low, value_rows, preferred_element_type=jnp.float32
    )
    return mixture.astype(jnp.bfloat16), soft_full, soft_low


def attend_back(queries, key_rows, value_rows, soft_full, soft_low, grad_mixture):
    score_scale = HD ** (-0.5)
    grad_values = jnp.einsum(
        "chqk,cqhd->ckhd", soft_low, grad_mixture, preferred_element_type=jnp.float32
    )
    grad_soft = jnp.einsum(
        "cqhd,ckhd->chqk", grad_mixture, value_rows, preferred_element_type=jnp.float32
    )
    row_delta = jnp.sum(grad_soft * soft_full, axis=-1, keepdims=True)
    grad_scores = (soft_full * (grad_soft - row_delta)).astype(jnp.bfloat16)
    grad_queries = (
        jnp.einsum("chqk,ckhd->cqhd", grad_scores, key_rows, preferred_element_type=jnp.float32)
        * score_scale
    )
    grad_keys = (
        jnp.einsum("chqk,cqhd->ckhd", grad_scores, queries, preferred_element_type=jnp.float32)
        * score_scale
    )
    return grad_queries, grad_keys, grad_values


def make_local(n_bits, order, orders):
    n_dev = 2 ** n_bits

    def local(
        tokens,
        band_waves,
        visible_slot,
        wave_table,
        norm1_gain,
        norm1_bias,
        qkv_weight,
        out_weight,
        norm2_gain,
        norm2_bias,
        mlp_in,
        mlp_in_bias,
        mlp_out,
        mlp_out_bias,
        dec_weight,
        dec_bias,
        mask_token,
        cot_decoded,
    ):
        shards = (
            wave_table,
            norm1_gain,
            norm1_bias,
            qkv_weight,
            out_weight,
            norm2_gain,
            norm2_bias,
            mlp_in,
            mlp_in_bias,
            mlp_out,
            mlp_out_bias,
            dec_weight,
            dec_bias,
            mask_token,
        )
        small = (wave_table, norm1_gain, norm1_bias, norm2_gain, norm2_bias, mlp_in_bias,
                 mlp_out_bias, dec_bias, mask_token)
        packed_small, small_widths = pack_rows(
            [a.reshape(1, -1) for a in small], 1, jnp.bfloat16
        )
        gathered_small = ag_chain(packed_small, n_bits, orders["x"])
        (wave_full, gain_one, shift_one, gain_two, shift_two, inner_bias, outer_bias,
         dec_shift, mask_full) = unpack_rows(gathered_small, small, small_widths, 1, n_dev)
        wide = (qkv_weight, out_weight, mlp_in, dec_weight)
        wide_cols = [a.shape[1] for a in wide]
        gathered_wide = lax.all_gather(jnp.concatenate(wide, axis=1), AX, axis=0, tiled=True)
        wide_full = []
        offset = 0
        for cols in wide_cols:
            wide_full.append(gathered_wide[:, offset : offset + cols])
            offset += cols
        qkv_full, out_full, inner_full, dec_full = wide_full
        outer_full = lax.all_gather(mlp_out, AX, axis=0, tiled=True)

        chip_count, vis_len, feature_width = tokens.shape
        row_count = chip_count * vis_len
        heads = feature_width // HD
        counts = jnp.sum(
            (band_waves[:, :, None] == jnp.arange(WAVES, dtype=jnp.int32)[None, None, :]).astype(
                jnp.float32
            ),
            axis=1,
        )
        spectral = jnp.dot(
            counts.astype(jnp.bfloat16), wave_full, preferred_element_type=jnp.float32
        )
        residual = (tokens.astype(jnp.float32) + spectral[:, None, :]).reshape(row_count, D)
        norm_out_one, normed_one, inverse_one = norm_forward(
            residual, gain_one.astype(jnp.float32), shift_one.astype(jnp.float32)
        )
        act_one = norm_out_one.astype(jnp.bfloat16)
        head_shape = (chip_count, vis_len, heads, HD)
        queries = product(act_one, qkv_full[:, :D]).astype(jnp.bfloat16).reshape(head_shape)
        key_rows = product(act_one, qkv_full[:, D : 2 * D]).astype(jnp.bfloat16).reshape(head_shape)
        value_rows = product(act_one, qkv_full[:, 2 * D :]).astype(jnp.bfloat16).reshape(head_shape)
        mixture4, soft_full, soft_low = attend(queries, key_rows, value_rows)
        mixture = mixture4.reshape(row_count, D)
        res_one = residual + product(mixture, out_full)
        norm_out_two, normed_two, inverse_two = norm_forward(
            res_one, gain_two.astype(jnp.float32), shift_two.astype(jnp.float32)
        )
        act_two = norm_out_two.astype(jnp.bfloat16)
        hidden = product(act_two, inner_full) + inner_bias.astype(jnp.float32)
        active = gelu_value(hidden).astype(jnp.bfloat16)
        res_two = res_one + (product(active, outer_full) + outer_bias.astype(jnp.float32))
        enc_low = res_two.astype(jnp.bfloat16)
        projected = (product(enc_low, dec_full) + dec_shift.astype(jnp.float32)).astype(
            jnp.bfloat16
        )
        slot_ids = jnp.arange(L, dtype=jnp.int32)
        one_hot = (visible_slot[:, None, :] == slot_ids[None, :, None]).astype(jnp.bfloat16)
        filled_vis = jnp.einsum(
            "csi,cie->cse",
            one_hot,
            projected.reshape(chip_count, vis_len, DEC),
            preferred_element_type=jnp.float32,
        )
        has_row = jnp.sum(one_hot.astype(jnp.float32), axis=2, keepdims=True) > 0.5
        filled = jnp.where(has_row, filled_vis, mask_full.astype(jnp.float32)[None, None, :])
        filled = filled.astype(jnp.bfloat16)
        decoded = lax.all_to_all(filled, AX, split_axis=1, concat_axis=0, tiled=True)
        grad_full = lax.all_to_all(cot_decoded, AX, split_axis=0, concat_axis=1, tiled=True)

        grad_vis_low = (
            jnp.einsum("csi,cse->cie", one_hot, grad_full, preferred_element_type=jnp.float32)
            .astype(jnp.bfloat16)
            .reshape(row_count, DEC)
        )
        grad_vis = grad_vis_low.astype(jnp.float32)
        grad_mask_token = jnp.sum(
            jnp.where(has_row, 0.0, grad_full.astype(jnp.float32)), axis=(0, 1)
        )
        grad_dec_bias = jnp.sum(grad_vis, axis=0)
        grad_dec_weight = inner_rows(enc_low, grad_vis_low)
        grad_res_two = outer_cols(grad_vis_low, dec_full)
        grad_ffo = grad_res_two.astype(jnp.bfloat16)
        grad_mlp_out_bias = jnp.sum(grad_ffo.astype(jnp.float32), axis=0)
        grad_mlp_out = inner_rows(active, grad_ffo)
        grad_hidden = (outer_cols(grad_ffo, outer_full) * gelu_slope(hidden)).astype(jnp.bfloat16)
        grad_mlp_in_bias = jnp.sum(grad_hidden.astype(jnp.float32), axis=0)
        grad_mlp_in = inner_rows(act_two, grad_hidden)
        grad_act_two = outer_cols(grad_hidden, inner_full)
        grad_norm_two, grad_norm2_gain, grad_norm2_bias = norm_backward(
            grad_act_two, normed_two, inverse_two, gain_two.astype(jnp.float32)
        )
        grad_res_one = grad_res_two + grad_norm_two
        grad_att = grad_res_one.astype(jnp.bfloat16)
        grad_out_weight = inner_rows(mixture, grad_att)
        grad_mixed = outer_cols(grad_att, out_full).astype(jnp.bfloat16).reshape(head_shape)
        grad_queries, grad_keys, grad_values = attend_back(
            queries, key_rows, value_rows, soft_full, soft_low, grad_mixed
        )
        grad_parts = [
            g.reshape(row_count, D).astype(jnp.bfloat16)
            for g in (grad_queries, grad_keys, grad_values)
        ]
        grad_qkv_weight = jnp.concatenate([inner_rows(act_one, g) for g in grad_parts], axis=1)
        grad_act_one = (
            outer_cols(grad_parts[0], qkv_full[:, :D])
            + outer_cols(grad_parts[1], qkv_full[:, D : 2 * D])
            + outer_cols(grad_parts[2], qkv_full[:, 2 * D :])
        )
        grad_norm_one, grad_norm1_gain, grad_norm1_bias = norm_backward(
            grad_act_one, normed_one, inverse_one, gain_one.astype(jnp.float32)
        )
        grad_tokens = (grad_res_one + grad_norm_one).reshape(chip_count, vis_len, D)
        chip_sums = jnp.sum(grad_tokens, axis=1)
        grad_wave_table = lax.dot_general(
            counts, chip_sums, (((0,), (0,)), ((), ())), precision=HIGH_PRECISION
        )
        small_grads = (grad_wave_table, grad_norm1_gain, grad_norm1_bias, grad_norm2_gain,
                       grad_norm2_bias, grad_mlp_in_bias, grad_mlp_out_bias, grad_dec_bias,
                       grad_mask_token)
        rows_block = grad_out_weight.shape[0] // n_dev
        sg_flat = [g.reshape(n_dev, -1) for g in small_grads]
        sg_widths = [f.shape[1] for f in sg_flat]
        sg_cols = -(-sum(sg_widths) // (rows_block * 128)) * 128
        sg_pad = rows_block * sg_cols - sum(sg_widths)
        sg_block = jnp.concatenate(
            sg_flat + [jnp.zeros((n_dev, sg_pad), jnp.float32)], axis=1
        ).reshape(n_dev * rows_block, sg_cols)
        joined = jnp.concatenate([grad_out_weight, grad_dec_weight, sg_block], axis=1)
        reduced_joined = rs_chain(joined, n_bits, orders["yz"])
        out_cols = grad_out_weight.shape[1]
        dec_cols = grad_dec_weight.shape[1]
        sum_out = reduced_joined[:, :out_cols]
        sum_dec = reduced_joined[:, out_cols : out_cols + dec_cols]
        sg_sum = reduced_joined[:, out_cols + dec_cols :].reshape(-1)
        sg_parts = []
        offset = 0
        for g, width in zip(small_grads, sg_widths):
            sg_parts.append(sg_sum[offset : offset + width].reshape((g.shape[0] // n_dev,) + g.shape[1:]))
            offset += width
        (sum_wave, sum_g1, sum_b1, sum_g2, sum_b2, sum_ib, sum_ob, sum_db, sum_mask) = sg_parts
        sum_mlp_out = rs_chain(grad_mlp_out, n_bits, orders["x"])
        sum_mlp_in = rs_chain(grad_mlp_in, n_bits, orders["y"])
        sum_qkv = rs_chain(grad_qkv_weight, n_bits, orders["yz"])
        summed = (sum_wave, sum_g1, sum_b1, sum_qkv, sum_out, sum_g2, sum_b2, sum_mlp_in,
                  sum_ib, sum_mlp_out, sum_ob, sum_dec, sum_db, sum_mask)
        return (decoded, grad_tokens, *summed)

    return local


def solution(mesh):
    n_dev = mesh.devices.size
    n_bits = n_dev.bit_length() - 1
    order = halving_order(n_bits, core_bit_of(mesh))
    orders = chain_orders(*bit_groups(mesh))
    placed = (
        P(AX, None, None),
        P(AX, None),
        P(AX, None),
        P(AX, None),
        P(AX),
        P(AX),
        P(AX, None),
        P(AX, None),
        P(AX),
        P(AX),
        P(AX, None),
        P(AX),
        P(AX, None),
        P(AX),
        P(AX, None),
        P(AX),
        P(AX),
        P(None, AX, None),
    )
    return jax.shard_map(
        make_local(n_bits, order, orders),
        mesh=mesh,
        in_specs=placed,
        out_specs=(
            P(None, AX, None),
            P(AX, None, None),
            P(AX, None),
            P(AX),
            P(AX),
            P(AX, None),
            P(AX, None),
            P(AX),
            P(AX),
            P(AX, None),
            P(AX),
            P(AX, None),
            P(AX),
            P(AX, None),
            P(AX),
            P(AX),
        ),
        check_vma=False,
    )
```
